32 devices in a mesh: dp: 8 (over y, x, core), expert: 4 (over z).
Axes of the slice: x: 2, y: 2, z: 4, core: 2. Of those that a mesh axis runs over, the one named last changes fastest.
Arguments:
- hidden_in: bfloat16 [2, 8, 128, 2048], P(None, 'dp', None, 'expert'), may hold values from -6 to 6
- request_order: int32 [2, 8], replicated, may hold values from 0 to 7, each once within a row
- request_lengths: int32 [2, 8], replicated, may hold values from 1 to 128, 640 in all within a row
- attention_routes: int32 [2, 8, 128, 2], P(None, 'dp'), may hold values from 0 to 7, all different within a row
- expert_routes: int32 [2, 8, 128, 2], P(None, 'dp'), may hold values from 0 to 7, as said below
- replica_picks: int32 [2, 8, 128, 2], P(None, 'dp'), may hold values from 0 to 5
- old_slots: int32 [16], replicated, may hold values from 0 to 7, as said below
- new_slots: int32 [16], replicated, may hold values from 0 to 7, as said below
- norm_gain_att: float32 [2048], replicated, may hold values from 0.1 to 1.9
- norm_gain_ffn: float32 [2048], replicated, may hold values from 0.1 to 1.9
- att_router: bfloat16 [2048, 8], replicated, may hold values from -0.125 to 0.125
- query_weight: bfloat16 [2048, 8, 16, 128], P(None, None, 'expert'), may hold values from -0.125 to 0.125
- key_value_weight: bfloat16 [2048, 2, 16, 128], P(None, None, 'expert'), may hold values from -0.125 to 0.125
- output_weight: bfloat16 [8, 16, 128, 2048], P(None, 'expert'), may hold values from -0.125 to 0.125
- ffn_router: bfloat16 [2048, 8], replicated, may hold values from -0.125 to 0.125
- expert_weights: bfloat16 [8, 2048, 3, 3072], P(None, 'dp', None, 'expert'), may hold values from -0.125 to 0.125
Outputs:
- layer_out: bfloat16 [2, 8, 128, 2048], P(None, 'dp', None, 'expert')
The draws below stay inside these ranges and needn't reach their ends.
Inputs may be any that keep to these rules, and one draw needn't show every extreme that they name: `request_order`: each batch's row names every request once. `request_lengths`: the longest request of each batch has exactly 128 tokens. `attention_routes`: the two experts of a token differ. `expert_routes`: the two experts of a token differ. `old_slots`: every expert is held by one, two or three slots; two experts by three. `new_slots`: every expert is held by one, two or three slots; two experts by three.
All inputs are finite; a program needn't handle non-finite values.
Results may differ from the reference program's by a relative error of at most 0.017.
Values may be sent and summed in bfloat16 or wider, within the bound.
No kernel may reach another device: no remote copies, remote signals or barrier semaphores. Data moves between devices by JAX's collectives and lax.ppermute only.
A program may use at most 256 MiB of HBM per device.

```python
import math
import jax
import jax.numpy as jnp
import numpy as np
from jax import lax

D = 2048
KVH = 16
HD = 128
AEXP = 8
FEXP = 8
TOPK = 2
FFW = 3072
SLOTS = 16
BATCHES = 2
LEN = 128
REQ_DEV = 1
REQUESTS = 8
TOK_GROUP = 128
CAP = 12
HG = 4
FB = 768


def ranked_experts(key, salt):
    return jax.random.permutation(jax.random.fold_in(key, salt), FEXP)


def placement_listing(key, salt, shuffle_salt):
    ranked = ranked_experts(key, salt)
    base_count = SLOTS // FEXP
    counts = jnp.full((FEXP,), base_count, jnp.int32)
    counts = counts.at[ranked[:2]].add(base_count // 2).at[ranked[2:4]].add(-(base_count // 2))
    listing = jnp.repeat(jnp.arange(FEXP, dtype=jnp.int32), counts, total_repeat_length=SLOTS)
    return jax.random.permutation(jax.random.fold_in(key, shuffle_salt), listing).astype(jnp.int32)


def draw_old_slots(key, part):
    return placement_listing(key, 21, 13)


def draw_new_slots(key, part):
    return placement_listing(key, 11, 12)


def draw_expert_routes(key, part):
    ranked = ranked_experts(key, 11)
    weights = jnp.full((FEXP,), 2, jnp.int32).at[ranked[:2]].set(5).at[ranked[2:4]].set(1)
    weight_sum = jnp.sum(weights)
    row_total = BATCHES * REQUESTS * LEN
    bounds = jnp.cumsum(weights)
    first_draw = jax.random.randint(jax.random.fold_in(key, 14), (row_total,), 0, weight_sum)
    first_pick = jnp.sum((first_draw[:, None] >= bounds[None, :]).astype(jnp.int32), axis=1)
    remaining = weights[None, :] * (jnp.arange(FEXP, dtype=jnp.int32)[None, :] != first_pick[:, None]).astype(jnp.int32)
    second_draw = jax.random.randint(jax.random.fold_in(key, 15), (row_total,), 0, jnp.sum(remaining, axis=1))
    second_pick = jnp.sum((second_draw[:, None] >= jnp.cumsum(remaining, axis=1)).astype(jnp.int32), axis=1)
    return jnp.stack([first_pick, second_pick], axis=1).reshape(BATCHES, REQUESTS, LEN, 2).astype(jnp.int32)


def touch_ends(array, rng, smallest, largest):
    spot = [jax.random.randint(jax.random.fold_in(rng, axis), (), 0, length) for axis, length in enumerate(array.shape)]
    main_axis = array.shape.index(max(array.shape))
    beside = spot[:main_axis] + [(spot[main_axis] + 1) % array.shape[main_axis]] + spot[main_axis + 1:]
    return array.at[tuple(spot)].set(smallest).at[tuple(beside)].set(largest)


def steps_of(own_key, shape, cuts, low, top_value):
    def one(dim, parts):
        draws = jax.random.uniform(jax.random.fold_in(jax.random.fold_in(own_key, 6), dim), (parts,), jnp.float32, low / len(cuts), top_value / len(cuts))
        return jnp.repeat(jnp.exp(draws), shape[dim] // parts).reshape((-1,) + (1,) * (len(shape) - dim - 1))

    loudness = one(*cuts[0])
    for cut in cuts[1:]:
        loudness = loudness * one(*cut)
    return loudness


def distinct(stream_key, rows, amount, top, lift):
    sequence = jax.random.permutation(jax.random.fold_in(stream_key, 1), amount)
    boost = sequence
    for power in range(3):
        boost = boost * boost // amount
    boost = boost * lift // amount
    lots = jax.random.randint(jax.random.fold_in(stream_key, 2), (rows, amount), 0, 4096) + boost
    holders = jax.random.permutation(jax.random.fold_in(stream_key, 3), rows)[jnp.arange(amount) % rows]
    lots = jnp.where(jnp.arange(rows)[:, None] == holders[None, :], 1 << 14, lots)
    score = lots * amount + jnp.arange(amount)
    return lax.top_k(score.astype(jnp.int32), top)[1].astype(jnp.int32)


def length_profile(count, total, limit, lean):
    portions = [(1 << 20) // math.isqrt(rank ** lean) + 1 for rank in range(2, count + 1)]
    surplus, given = total - limit - (count - 1), [1] * (count - 1)
    while surplus > 0:
        candidates = [i for i in range(count - 1) if given[i] < limit]
        whole, left = sum([portions[i] for i in candidates]), surplus
        for i in candidates:
            more = min(limit - given[i], max(1, left * portions[i] // whole), surplus)
            given[i] = given[i] + more
            surplus = surplus - more
    return np.array([limit] + given)


def ragged_sizes(own_key, number_of, total, most, lean):
    if number_of == 2:
        one = jax.random.randint(own_key, (), max(1, total - most), min(most, total - 1) + 1)
        return jnp.stack([one, total - one])
    lengths = jnp.asarray(length_profile(number_of, total, most, lean), jnp.int32)
    pairs = (number_of - 1) // 2
    donor, receiver = lengths[1:1 + 2 * pairs:2], lengths[2:2 + 2 * pairs:2]
    margin = jnp.minimum(donor - 1, most - receiver)
    passed = jax.random.randint(jax.random.fold_in(own_key, 1), (pairs,), 0, 1 << 20) % (margin + 1)
    lengths = lengths.at[1:1 + 2 * pairs:2].set(donor - passed).at[2:2 + 2 * pairs:2].set(receiver + passed)
    return lengths[jax.random.permutation(jax.random.fold_in(own_key, 2), number_of)]


def gaussian(rng, extent, deviation, reach, pieces=(), held_as=jnp.bfloat16):
    array = deviation * jax.random.normal(rng, extent, jnp.float32)
    if pieces:
        array = array * steps_of(rng, extent, pieces, -0.22, 0.18)
    return jnp.clip(array, -reach, reach).astype(held_as)


def setup_inputs(seed: int = 0) -> dict:
    key_list = jax.random.split(jax.random.key(seed), 17)
    return {
        "hidden_in": gaussian(key_list[0], (BATCHES, REQUESTS, LEN, D), 1.0, 6.0, ((1, 8), (3, 4))),
        "request_order": jax.vmap(lambda own: jax.random.permutation(own, REQUESTS))(jax.random.split(key_list[1], BATCHES)).reshape((BATCHES, REQUESTS)).astype(jnp.int32),
        "request_lengths": jax.vmap(lambda own: ragged_sizes(own, REQUESTS, REQUESTS * LEN * 5 // 8, LEN, 2))(jax.random.split(key_list[2], BATCHES)).reshape((BATCHES, REQUESTS)).astype(jnp.int32),
        "attention_routes": distinct(key_list[3], BATCHES * REQUESTS * LEN, AEXP, TOPK, 2048).reshape((BATCHES, REQUESTS, LEN, TOPK)),
        "expert_routes": draw_expert_routes(jax.random.fold_in(key_list[16], 71), 0),
        "replica_picks": touch_ends(jax.random.randint(key_list[5], (BATCHES, REQUESTS, LEN, TOPK), 0, 6), jax.random.fold_in(key_list[5], 1), 0, 5).astype(jnp.int32),
        "old_slots": draw_old_slots(jax.random.fold_in(key_list[16], 71), 0),
        "new_slots": draw_new_slots(jax.random.fold_in(key_list[16], 71), 0),
        "norm_gain_att": jnp.clip(1.0 + 0.18 * jax.random.normal(key_list[8], (D,), jnp.float32), 0.1, 1.9),
        "norm_gain_ffn": jnp.clip(1.0 + 0.18 * jax.random.normal(key_list[9], (D,), jnp.float32), 0.1, 1.9),
        "att_router": gaussian(key_list[10], (D, AEXP), D ** -0.5, 0.125),
        "query_weight": gaussian(key_list[11], (D, AEXP, KVH, HD), D ** -0.5, 0.125, ((2, 4),)),
        "key_value_weight": gaussian(key_list[12], (D, 2, KVH, HD), D ** -0.5, 0.125, ((2, 4),)),
        "output_weight": gaussian(key_list[13], (AEXP, KVH, HD, D), (KVH * HD) ** -0.5, 0.125, ((1, 4),)),
        "ffn_router": gaussian(key_list[14], (D, FEXP), D ** -0.5, 0.125),
        "expert_weights": gaussian(key_list[15], (FEXP, D, 3, FFW), D ** -0.5, 0.125, ((1, 8), (3, 4))),
    }


EPS = 1e-06
ROPE_BASE = 10000.0

def rope_tables(seq_len, head_width):
    half_width = head_width // 2
    frequency = ROPE_BASE ** (-(jnp.arange(half_width, dtype=jnp.float32) * 2.0 / head_width))
    angles = jnp.arange(seq_len, dtype=jnp.float32)[:, None] * frequency[None, :]
    return (jnp.cos(angles), jnp.sin(angles))

def rope_apply(values, cosine, sine_table, along_axis):
    half_width = values.shape[-1] // 2
    tile_shape = [1] * values.ndim
    tile_shape[along_axis] = cosine.shape[0]
    tile_shape[-1] = half_width
    cos_part = cosine.reshape(tile_shape)
    sin_part = sine_table.reshape(tile_shape)
    front_half = values[..., :half_width]
    back_half = values[..., half_width:]
    return jnp.concatenate([front_half * cos_part - back_half * sin_part, back_half * cos_part + front_half * sin_part], axis=-1)

def rms_norm(rows, gain_vec):
    widened = rows.astype(jnp.float32)
    inv_rms = lax.rsqrt(lax.optimization_barrier(jnp.mean(widened * widened, axis=-1, keepdims=True)) + EPS)
    return (widened * inv_rms * gain_vec).astype(jnp.bfloat16)

def pair_gates(logits, routes):
    picked = jnp.take_along_axis(logits, routes, axis=-1)
    leading = jax.nn.sigmoid(picked[..., 0] - picked[..., 1])
    return jnp.stack([leading, 1.0 - leading], axis=-1)

def slot_targets(placement, expert_ids, replica_ids, live_rows):
    slot_range = jnp.arange(SLOTS, dtype=jnp.int32)
    same_expert = placement[:, None] == placement[None, :]
    earlier = slot_range[:, None] > slot_range[None, :]
    occurrence = lax.optimization_barrier(jnp.sum((same_expert & earlier).astype(jnp.int32), axis=1))
    hosting = (placement[None, :] == jnp.arange(FEXP, dtype=jnp.int32)[:, None]).astype(jnp.int32)
    copies_all = lax.optimization_barrier(jnp.sum(hosting, axis=1))
    chosen = (expert_ids[:, None] == jnp.arange(FEXP, dtype=jnp.int32)[None, :]).astype(jnp.int32)
    copies = lax.optimization_barrier(jnp.sum(chosen * copies_all[None, :], axis=1))
    replica = replica_ids % copies
    slot_hits = (placement[None, :] == expert_ids[:, None]) & (occurrence[None, :] == replica[:, None]) & live_rows[:, None]
    slot_hits = slot_hits.astype(jnp.int32)
    before = jnp.cumsum(slot_hits, axis=0) - slot_hits
    ranking = lax.optimization_barrier(jnp.sum(before * slot_hits, axis=1))
    slot_ids = lax.optimization_barrier(jnp.sum(slot_hits * slot_range[None, :], axis=1))
    within_cap = (lax.optimization_barrier(jnp.sum(slot_hits, axis=1)) > 0) & (ranking < CAP)
    return jnp.where(within_cap, slot_ids * CAP + ranking, SLOTS * CAP).astype(jnp.int32)

def fill_buffer(rows, target):
    token_total = rows.shape[0]
    source = jnp.full((SLOTS * CAP + 1,), token_total, jnp.int32)
    source = source.at[target].set(jnp.arange(target.shape[0], dtype=jnp.int32) // TOPK)
    padded = jnp.concatenate([rows, jnp.zeros((1, rows.shape[1]), rows.dtype)], axis=0)
    return jnp.take(padded, source[:-1], axis=0).reshape(SLOTS, CAP, rows.shape[1])

def collect(results, target):
    flat_rows = results.reshape(SLOTS * CAP, results.shape[-1])
    padded = jnp.concatenate([flat_rows, jnp.zeros((1, flat_rows.shape[1]), flat_rows.dtype)], axis=0)
    return jnp.take(padded, target, axis=0)

def attend_request(bundle, gain_vec, router, query_flat, key_value_flat, output_wide, cosine, sine_table):
    hidden_rows, length, routes = bundle
    normed = rms_norm(hidden_rows, gain_vec)
    logits = jnp.dot(normed, router, preferred_element_type=jnp.float32)
    gate_pair = pair_gates(logits, routes)
    every_query = jnp.dot(normed, query_flat, preferred_element_type=jnp.float32).reshape(LEN, AEXP, KVH, HD)
    queries = jnp.take_along_axis(every_query, routes[:, :, None, None], axis=1)
    queries = rope_apply(queries, cosine, sine_table, 0).astype(jnp.bfloat16)
    key_value = jnp.dot(normed, key_value_flat, preferred_element_type=jnp.float32).reshape(LEN, 2, KVH, HD)
    key_rows = rope_apply(key_value[:, 0], cosine, sine_table, 0).astype(jnp.bfloat16)
    values = key_value[:, 1].astype(jnp.bfloat16)
    scores = jnp.einsum('tkhd,uhd->khtu', queries.astype(jnp.float32), key_rows.astype(jnp.float32)) / math.sqrt(HD)
    positions = jnp.arange(LEN, dtype=jnp.int32)
    allowed = (positions[None, :] <= positions[:, None]) & (positions[None, :] < length)
    raised = jnp.where(allowed[None, None], jnp.exp(scores), 0.0)
    probability = (raised / lax.optimization_barrier(jnp.sum(raised, axis=-1, keepdims=True))).astype(jnp.bfloat16)
    head_out = jnp.einsum('khtu,uhd->tkhd', probability.astype(jnp.float32), values.astype(jnp.float32))
    expert_hits = (routes[:, :, None] == jnp.arange(AEXP, dtype=jnp.int32)[None, None, :]).astype(jnp.float32) * gate_pair[:, :, None]
    mixed_heads = lax.optimization_barrier(jnp.sum(expert_hits[:, :, :, None, None] * head_out[:, :, None, :, :], axis=1)).astype(jnp.bfloat16)
    grouped = mixed_heads.reshape(LEN, AEXP, KVH // HG, HG, HD).astype(jnp.float32)
    partial_value = jnp.einsum('tegxd,egxdn->tgn', grouped, output_wide)
    rounded = lax.optimization_barrier(partial_value.astype(jnp.bfloat16)).astype(jnp.float32)
    attn = lax.optimization_barrier(jnp.sum(rounded, axis=1))
    return (hidden_rows.astype(jnp.float32) + attn).astype(jnp.bfloat16)

def ffn_batch(residual, lens_pos, routes, picks, placement, gain_vec, router, expert_weights):
    groups = REQUESTS // REQ_DEV
    normed = rms_norm(residual, gain_vec)
    logits = jnp.dot(normed.reshape(-1, D), router, preferred_element_type=jnp.float32).reshape(REQUESTS, LEN, FEXP)
    gate_pair = pair_gates(logits, routes)
    live_rows = jnp.arange(LEN, dtype=jnp.int32)[None, :] < lens_pos[:, None]
    group_rows = normed.reshape(groups, TOK_GROUP, D)
    group_routes = routes.reshape(groups, TOK_GROUP * TOPK)
    group_picks = picks.reshape(groups, TOK_GROUP * TOPK)
    group_live = jnp.repeat(live_rows.reshape(groups, TOK_GROUP), TOPK, axis=1)

    def group_target(expert_ids, replica_ids, live_assign):
        return slot_targets(placement, expert_ids, replica_ids, live_assign)
    targets = jax.vmap(group_target)(group_routes, group_picks, group_live)
    buffers = jax.vmap(fill_buffer)(group_rows, targets)

    def per_slot(slot_index):
        slot_rows = lax.dynamic_index_in_dim(buffers, slot_index, axis=1, keepdims=False).reshape(-1, D)
        chosen = lax.dynamic_index_in_dim(expert_weights, placement[slot_index], axis=0, keepdims=False)
        gate_proj = jnp.dot(slot_rows, chosen[:, 0, :], preferred_element_type=jnp.float32)
        up_proj = jnp.dot(slot_rows, chosen[:, 1, :], preferred_element_type=jnp.float32)
        hidden = (jax.nn.silu(gate_proj) * up_proj).astype(jnp.bfloat16)
        split_hidden = hidden.reshape(-1, FFW // FB, FB).astype(jnp.float32)
        down_rows = chosen[:, 2, :].reshape(D, FFW // FB, FB).astype(jnp.float32)
        term_rows = jnp.einsum('rgf,ngf->rgn', split_hidden, down_rows)
        rounded = lax.optimization_barrier(term_rows.astype(jnp.bfloat16)).astype(jnp.float32)
        return lax.optimization_barrier(jnp.sum(rounded, axis=1)).astype(jnp.bfloat16)
    slot_outs = lax.map(per_slot, jnp.arange(SLOTS, dtype=jnp.int32))
    slot_outs = slot_outs.reshape(SLOTS, groups, CAP, D).transpose(1, 0, 2, 3)
    part_rows = jax.vmap(collect)(slot_outs, targets).astype(jnp.float32).reshape(REQUESTS, LEN, TOPK, D)
    combined = residual.astype(jnp.float32) + gate_pair[..., 0:1] * part_rows[:, :, 0] + gate_pair[..., 1:2] * part_rows[:, :, 1]
    return jnp.where(live_rows[:, :, None], combined, 0.0).astype(jnp.bfloat16)

def reference(hidden_in, request_order, request_lengths, attention_routes, expert_routes, replica_picks, old_slots, new_slots, norm_gain_att, norm_gain_ffn, att_router, query_weight, key_value_weight, output_weight, ffn_router, expert_weights):
    cosine, sine_table = rope_tables(LEN, HD)
    query_flat = query_weight.reshape(D, -1)
    key_value_flat = key_value_weight.reshape(D, -1)
    output_wide = output_weight.reshape(AEXP, KVH // HG, HG, HD, D).astype(jnp.float32)
    placements = (old_slots, new_slots)
    outputs = []
    for batch_index in range(BATCHES):
        lens_pos = jnp.take(request_lengths[batch_index], request_order[batch_index])

        def one_request(bundle):
            return attend_request(bundle, norm_gain_att, att_router, query_flat, key_value_flat, output_wide, cosine, sine_table)
        residual = lax.map(one_request, (hidden_in[batch_index], lens_pos, attention_routes[batch_index]))
        outputs.append(ffn_batch(residual, lens_pos, expert_routes[batch_index], replica_picks[batch_index], placements[batch_index], norm_gain_ffn, ffn_router, expert_weights))
    return jnp.stack(outputs, axis=0)
```

```python
import math

import jax
import jax.numpy as jnp
from jax import lax
from jax.sharding import PartitionSpec as P

FEXP = 8
TOPK = 2
SLOTS = 16
CAP = 12


EPS = 1e-06
ROPE_BASE = 10000.0


def rope_tables(seq_len, head_width):
    half_width = head_width // 2
    frequency = ROPE_BASE ** (-(jnp.arange(half_width, dtype=jnp.float32) * 2.0 / head_width))
    angles = jnp.arange(seq_len, dtype=jnp.float32)[:, None] * frequency[None, :]
    return (jnp.cos(angles), jnp.sin(angles))


def rope_apply(values, cosine, sine_table, along_axis):
    half_width = values.shape[-1] // 2
    tile_shape = [1] * values.ndim
    tile_shape[along_axis] = cosine.shape[0]
    tile_shape[-1] = half_width
    cos_part = cosine.reshape(tile_shape)
    sin_part = sine_table.reshape(tile_shape)
    front_half = values[..., :half_width]
    back_half = values[..., half_width:]
    return jnp.concatenate(
        [
            front_half * cos_part - back_half * sin_part,
            back_half * cos_part + front_half * sin_part,
        ],
        axis=-1,
    )


def rms_norm(rows, gain_vec):
    widened = rows.astype(jnp.float32)
    inv_rms = lax.rsqrt(jnp.mean(widened * widened, axis=-1, keepdims=True) + EPS)
    return (widened * inv_rms * gain_vec).astype(jnp.bfloat16)


def pair_gates(logits, routes):
    picked = jnp.take_along_axis(logits, routes, axis=-1)
    leading = jax.nn.sigmoid(picked[..., 0] - picked[..., 1])
    return jnp.stack([leading, 1.0 - leading], axis=-1)


def slot_targets(placement, expert_ids, replica_ids, live_rows):
    slot_range = jnp.arange(SLOTS, dtype=jnp.int32)
    same_expert = placement[:, None] == placement[None, :]
    earlier = slot_range[:, None] > slot_range[None, :]
    occurrence = jnp.sum((same_expert & earlier).astype(jnp.int32), axis=1)
    hosting = (placement[None, :] == jnp.arange(FEXP, dtype=jnp.int32)[:, None]).astype(jnp.int32)
    copies_all = jnp.sum(hosting, axis=1)
    chosen = (expert_ids[:, None] == jnp.arange(FEXP, dtype=jnp.int32)[None, :]).astype(jnp.int32)
    copies = jnp.sum(chosen * copies_all[None, :], axis=1)
    replica = replica_ids % copies
    slot_hits = (
        (placement[None, :] == expert_ids[:, None])
        & (occurrence[None, :] == replica[:, None])
        & live_rows[:, None]
    )
    slot_hits = slot_hits.astype(jnp.int32)
    before = jnp.cumsum(slot_hits, axis=0) - slot_hits
    ranking = jnp.sum(before * slot_hits, axis=1)
    slot_ids = jnp.sum(slot_hits * slot_range[None, :], axis=1)
    within_cap = (jnp.sum(slot_hits, axis=1) > 0) & (ranking < CAP)
    return jnp.where(within_cap, slot_ids * CAP + ranking, SLOTS * CAP)


def fill_buffer(rows, target):
    token_total = rows.shape[0]
    source = jnp.full((SLOTS * CAP + 1,), token_total, jnp.int32)
    source = source.at[target].set(jnp.arange(target.shape[0], dtype=jnp.int32) // TOPK)
    padded = jnp.concatenate([rows, jnp.zeros((1, rows.shape[1]), rows.dtype)], axis=0)
    return jnp.take(padded, source[:-1], axis=0).reshape(SLOTS, CAP, rows.shape[1])


def collect(results, target):
    flat_rows = results.reshape(SLOTS * CAP, results.shape[-1])
    padded = jnp.concatenate(
        [flat_rows, jnp.zeros((1, flat_rows.shape[1]), flat_rows.dtype)], axis=0
    )
    return jnp.take(padded, target, axis=0)


def load_weights(stored, placement):
    dp_groups = lax.axis_size("dp")
    per = SLOTS // dp_groups
    me = lax.axis_index("dp")
    pieces = []
    for shift in range(dp_groups):
        partner = me ^ shift
        ids = lax.dynamic_slice_in_dim(placement, partner * per, per)
        piece = jnp.take(stored, ids, axis=0)
        if shift:
            pairs = [(i, i ^ shift) for i in range(dp_groups)]
            piece = lax.ppermute(piece, "dp", pairs)
        pieces.append(piece)
    return jnp.stack(pieces, axis=1)


def block_order(rows, axis):
    dp_groups = lax.axis_size("dp")
    me = lax.axis_index("dp")
    shape = rows.shape
    split = shape[:axis] + (dp_groups, shape[axis] // dp_groups) + shape[axis + 1 :]
    order = me ^ jnp.arange(dp_groups, dtype=jnp.int32)
    return jnp.take(rows.reshape(split), order, axis=axis).reshape(shape)


def expert_terms(slot_items, loaded):
    per, groups, block, _, cols = loaded.shape
    weights_here = loaded.reshape(per, groups * block, 3, cols)
    slot_items = block_order(slot_items, 3)
    gate_proj = jnp.einsum(
        "gjcd,jdf->gjcf", slot_items, weights_here[:, :, 0, :], preferred_element_type=jnp.float32
    )
    up_proj = jnp.einsum(
        "gjcd,jdf->gjcf", slot_items, weights_here[:, :, 1, :], preferred_element_type=jnp.float32
    )
    hidden = (jax.nn.silu(gate_proj) * up_proj).astype(jnp.bfloat16)
    terms = jnp.einsum(
        "gjcf,jdf->gjcd", hidden, weights_here[:, :, 2, :], preferred_element_type=jnp.float32
    )
    return block_order(terms.astype(jnp.bfloat16), 3)


def attend(
    hidden_cols,
    lens_here,
    routes,
    gain_vec,
    router,
    query_flat,
    key_value_flat,
    output_flat,
    cosine,
    sine_table,
):
    full_rows = lax.all_gather(hidden_cols, "expert", axis=2, tiled=True)
    req_count, seq_len, model_width = full_rows.shape
    token_count = req_count * seq_len
    expert_count = router.shape[1]
    head_width = cosine.shape[1] * 2
    normed = rms_norm(full_rows.reshape(token_count, model_width), gain_vec)
    logits = jnp.dot(normed, router, preferred_element_type=jnp.float32)
    gate_pair = pair_gates(logits, routes)
    every_query = jnp.einsum(
        "td,dehk->tehk", normed, query_flat, preferred_element_type=jnp.float32
    )
    queries = jnp.take_along_axis(every_query, routes[:, :, None, None], axis=1)
    queries = rope_apply(
        queries.reshape(req_count, seq_len, 2, -1, head_width), cosine, sine_table, 1
    ).astype(jnp.bfloat16)
    key_value = jnp.einsum(
        "td,dchk->tchk", normed, key_value_flat, preferred_element_type=jnp.float32
    ).reshape(req_count, seq_len, 2, -1, head_width)
    key_rows = rope_apply(key_value[:, :, 0], cosine, sine_table, 1).astype(jnp.bfloat16)
    values = key_value[:, :, 1].astype(jnp.bfloat16)
    scores = jnp.einsum(
        "rtkhd,ruhd->rkhtu", queries, key_rows, preferred_element_type=jnp.float32
    ) / math.sqrt(head_width)
    positions = jnp.arange(seq_len, dtype=jnp.int32)
    allowed = (positions[None, None, :] <= positions[None, :, None]) & (
        positions[None, None, :] < lens_here[:, None, None]
    )
    raised = jnp.where(allowed[:, None, None], jnp.exp(scores), 0.0)
    probability = (raised / jnp.sum(raised, axis=-1, keepdims=True)).astype(jnp.bfloat16)
    head_out = jnp.einsum(
        "rkhtu,ruhd->rtkhd", probability, values, preferred_element_type=jnp.float32
    )
    head_out = head_out.reshape(token_count, 2, -1, head_width)
    expert_hits = (
        routes[:, :, None] == jnp.arange(expert_count, dtype=jnp.int32)[None, None, :]
    ).astype(jnp.float32) * gate_pair[:, :, None]
    mixed_heads = jnp.einsum(
        "tke,tkhd->tehd", expert_hits, head_out, precision=lax.Precision.HIGHEST
    ).astype(jnp.bfloat16)
    partial_value = jnp.dot(
        mixed_heads.reshape(token_count, -1), output_flat, preferred_element_type=jnp.float32
    )
    attn_cols = lax.psum_scatter(
        partial_value.astype(jnp.bfloat16), "expert", scatter_dimension=1, tiled=True
    ).astype(jnp.float32)
    return (hidden_cols.reshape(token_count, -1).astype(jnp.float32) + attn_cols).astype(
        jnp.bfloat16
    )


def per_device(
    hidden_in,
    request_order,
    request_lengths,
    attention_routes,
    expert_routes,
    replica_picks,
    old_slots,
    new_slots,
    norm_gain_att,
    norm_gain_ffn,
    att_router,
    query_weight,
    key_value_weight,
    output_weight,
    ffn_router,
    expert_weights,
):
    req_count = hidden_in.shape[1]
    seq_len = hidden_in.shape[2]
    col_width = hidden_in.shape[3]
    model_width = norm_gain_att.shape[0]
    token_count = req_count * seq_len
    dp_groups = lax.axis_size("dp")
    slots_here = SLOTS // dp_groups
    head_width = query_weight.shape[3]
    cosine, sine_table = rope_tables(seq_len, head_width)
    query_flat = query_weight
    key_value_flat = key_value_weight
    output_flat = output_weight.reshape(-1, model_width)
    column_start = lax.axis_index("expert") * col_width
    placements = (old_slots, new_slots)
    results = []
    loads = []
    for batch_index in range(2):
        with jax.named_scope(f"wload{batch_index}"):
            loads.append(load_weights(expert_weights, placements[batch_index]))
    for batch_index in range(2):
        placement = placements[batch_index]
        weights_here = loads[batch_index]
        lens_all = jnp.take(request_lengths[batch_index], request_order[batch_index])
        lens_here = lax.dynamic_slice_in_dim(lens_all, lax.axis_index("dp") * req_count, req_count)
        live_rows = (jnp.arange(seq_len, dtype=jnp.int32)[None, :] < lens_here[:, None]).reshape(
            token_count
        )
        att_pairs = attention_routes[batch_index].reshape(token_count, 2)
        residual = attend(
            hidden_in[batch_index],
            lens_here,
            att_pairs,
            norm_gain_att,
            att_router,
            query_flat,
            key_value_flat,
            output_flat,
            cosine,
            sine_table,
        )
        ffn_pairs = expert_routes[batch_index].reshape(token_count, 2)
        routes_flat = ffn_pairs.reshape(-1)
        picks_flat = replica_picks[batch_index].reshape(-1)
        live_assign = jnp.repeat(live_rows, 2)
        target = slot_targets(placement, routes_flat, picks_flat, live_assign)
        widened = residual.astype(jnp.float32)
        squares = lax.psum(jnp.sum(widened * widened, axis=1), "expert")
        inv_rms = lax.rsqrt(squares / model_width + EPS)
        gain_cols = lax.dynamic_slice_in_dim(norm_gain_ffn, column_start, col_width)
        normed_cols = (widened * inv_rms[:, None] * gain_cols[None, :]).astype(jnp.bfloat16)
        router_cols = lax.dynamic_slice_in_dim(ffn_router, column_start, col_width, 0)
        logits = lax.psum(
            jnp.dot(normed_cols, router_cols, preferred_element_type=jnp.float32), "expert"
        )
        gate_pair = pair_gates(logits, ffn_pairs)
        buffer = fill_buffer(normed_cols, target).reshape(dp_groups, slots_here, CAP, col_width)
        whole_rows = lax.all_gather(
            lax.all_to_all(buffer, "dp", split_axis=0, concat_axis=0, tiled=True),
            "expert",
            axis=3,
            tiled=True,
        )
        term_rows = expert_terms(whole_rows, weights_here)
        reduced = lax.psum_scatter(term_rows, "expert", scatter_dimension=3, tiled=True)
        returned = lax.all_to_all(reduced, "dp", split_axis=0, concat_axis=0, tiled=True)
        expert_out = collect(returned.reshape(SLOTS, CAP, col_width), target).astype(jnp.float32)
        paired = expert_out.reshape(token_count, 2, col_width)
        combined = (
            residual.astype(jnp.float32)
            + gate_pair[:, 0:1] * paired[:, 0]
            + gate_pair[:, 1:2] * paired[:, 1]
        )
        combined = jnp.where(live_rows[:, None], combined, 0.0).astype(jnp.bfloat16)
        results.append(combined.reshape(req_count, seq_len, col_width))
    return jnp.stack(results, axis=0)


def solution(mesh):
    in_specs = (
        P(None, "dp", None, "expert"),
        P(),
        P(),
        P(None, "dp", None, None),
        P(None, "dp", None, None),
        P(None, "dp", None, None),
        P(),
        P(),
        P(),
        P(),
        P(),
        P(None, None, "expert", None),
        P(None, None, "expert", None),
        P(None, "expert", None, None),
        P(),
        P(None, "dp", None, "expert"),
    )
    out_specs = P(None, "dp", None, "expert")
    return jax.shard_map(
        per_device, mesh=mesh, in_specs=in_specs, out_specs=out_specs, check_vma=False
    )
```

```python
import math

import jax
import jax.numpy as jnp
from jax import lax
from jax.sharding import PartitionSpec as P

FEXP = 8
TOPK = 2
SLOTS = 16
CAP = 12


EPS = 1e-06
ROPE_BASE = 10000.0


def rope_tables(seq_len, head_width):
    half_width = head_width // 2
    frequency = ROPE_BASE ** (-(jnp.arange(half_width, dtype=jnp.float32) * 2.0 / head_width))
    angles = jnp.arange(seq_len, dtype=jnp.float32)[:, None] * frequency[None, :]
    return (jnp.cos(angles), jnp.sin(angles))


def rope_apply(values, cosine, sine_table, along_axis):
    half_width = values.shape[-1] // 2
    tile_shape = [1] * values.ndim
    tile_shape[along_axis] = cosine.shape[0]
    tile_shape[-1] = half_width
    cos_part = cosine.reshape(tile_shape)
    sin_part = sine_table.reshape(tile_shape)
    front_half = values[..., :half_width]
    back_half = values[..., half_width:]
    return jnp.concatenate(
        [
            front_half * cos_part - back_half * sin_part,
            back_half * cos_part + front_half * sin_part,
        ],
        axis=-1,
    )


def rms_norm(rows, gain_vec):
    widened = rows.astype(jnp.float32)
    inv_rms = lax.rsqrt(jnp.mean(widened * widened, axis=-1, keepdims=True) + EPS)
    return (widened * inv_rms * gain_vec).astype(jnp.bfloat16)


def pair_gates(logits, routes):
    picked = jnp.take_along_axis(logits, routes, axis=-1)
    leading = jax.nn.sigmoid(picked[..., 0] - picked[..., 1])
    return jnp.stack([leading, 1.0 - leading], axis=-1)


def slot_targets(placement, expert_ids, replica_ids, live_rows):
    slot_range = jnp.arange(SLOTS, dtype=jnp.int32)
    same_expert = placement[:, None] == placement[None, :]
    earlier = slot_range[:, None] > slot_range[None, :]
    occurrence = jnp.sum((same_expert & earlier).astype(jnp.int32), axis=1)
    hosting = (placement[None, :] == jnp.arange(FEXP, dtype=jnp.int32)[:, None]).astype(jnp.int32)
    copies_all = jnp.sum(hosting, axis=1)
    chosen = (expert_ids[:, None] == jnp.arange(FEXP, dtype=jnp.int32)[None, :]).astype(jnp.int32)
    copies = jnp.sum(chosen * copies_all[None, :], axis=1)
    replica = replica_ids % copies
    slot_hits = (
        (placement[None, :] == expert_ids[:, None])
        & (occurrence[None, :] == replica[:, None])
        & live_rows[:, None]
    )
    slot_hits = slot_hits.astype(jnp.int32)
    before = jnp.cumsum(slot_hits, axis=0) - slot_hits
    ranking = jnp.sum(before * slot_hits, axis=1)
    slot_ids = jnp.sum(slot_hits * slot_range[None, :], axis=1)
    within_cap = (jnp.sum(slot_hits, axis=1) > 0) & (ranking < CAP)
    return jnp.where(within_cap, slot_ids * CAP + ranking, SLOTS * CAP)


def fill_buffer(rows, target):
    token_total = rows.shape[0]
    source = jnp.full((SLOTS * CAP + 1,), token_total, jnp.int32)
    source = source.at[target].set(jnp.arange(target.shape[0], dtype=jnp.int32) // TOPK)
    padded = jnp.concatenate([rows, jnp.zeros((1, rows.shape[1]), rows.dtype)], axis=0)
    return jnp.take(padded, source[:-1], axis=0).reshape(SLOTS, CAP, rows.shape[1])


def collect(results, target):
    flat_rows = results.reshape(SLOTS * CAP, results.shape[-1])
    padded = jnp.concatenate(
        [flat_rows, jnp.zeros((1, flat_rows.shape[1]), flat_rows.dtype)], axis=0
    )
    return jnp.take(padded, target, axis=0)


def load_weights(stored, placement):
    dp_groups = lax.axis_size("dp")
    per = SLOTS // dp_groups
    me = lax.axis_index("dp")
    pieces = []
    for shift in range(dp_groups):
        partner = me ^ shift
        ids = lax.dynamic_slice_in_dim(placement, partner * per, per)
        piece = jnp.take(stored, ids, axis=0)
        if shift:
            pairs = [(i, i ^ shift) for i in range(dp_groups)]
            piece = lax.ppermute(piece, "dp", pairs)
        pieces.append(piece)
    return jnp.stack(pieces, axis=1)


def block_order(rows, axis):
    dp_groups = lax.axis_size("dp")
    me = lax.axis_index("dp")
    shape = rows.shape
    split = shape[:axis] + (dp_groups, shape[axis] // dp_groups) + shape[axis + 1 :]
    order = me ^ jnp.arange(dp_groups, dtype=jnp.int32)
    return jnp.take(rows.reshape(split), order, axis=axis).reshape(shape)


def expert_terms(slot_items, loaded):
    per, groups, block, _, cols = loaded.shape
    weights_here = loaded.reshape(per, groups * block, 3, cols)
    slot_items = block_order(slot_items, 3)
    gate_proj = jnp.einsum(
        "gjcd,jdf->gjcf", slot_items, weights_here[:, :, 0, :], preferred_element_type=jnp.float32
    )
    up_proj = jnp.einsum(
        "gjcd,jdf->gjcf", slot_items, weights_here[:, :, 1, :], preferred_element_type=jnp.float32
    )
    hidden = (jax.nn.silu(gate_proj) * up_proj).astype(jnp.bfloat16)
    terms = jnp.einsum(
        "gjcf,jdf->gjcd", hidden, weights_here[:, :, 2, :], preferred_element_type=jnp.float32
    )
    return block_order(terms.astype(jnp.bfloat16), 3)


def ffn_stationary(normed_cols, target, placement, stored):
    dp_groups = lax.axis_size("dp")
    ex_groups = lax.axis_size("expert")
    me_dp = lax.axis_index("dp")
    col_width = normed_cols.shape[1]
    model_width = col_width * ex_groups
    block = model_width // dp_groups
    ratio = dp_groups // ex_groups
    buffer = fill_buffer(normed_cols, target)
    full = lax.all_gather(buffer, "expert", axis=2, tiled=True)
    blocks = full.reshape(SLOTS, CAP, dp_groups, block).transpose(2, 0, 1, 3)
    rows_here = lax.all_to_all(blocks, "dp", split_axis=0, concat_axis=0, tiled=True)
    chosen = jnp.take(stored, placement, axis=0)
    partial = jnp.einsum(
        "gscd,sdkf->gsckf", rows_here, chosen[:, :, 0:2, :], preferred_element_type=jnp.float32
    ).astype(jnp.bfloat16)
    summed = lax.psum_scatter(partial, "dp", scatter_dimension=1, tiled=True).astype(jnp.float32)
    hidden = (jax.nn.silu(summed[..., 0, :]) * summed[..., 1, :]).astype(jnp.bfloat16)
    hidden_all = lax.all_gather(hidden, "dp", axis=1, tiled=True)
    terms = jnp.einsum(
        "gscf,sdf->gscd", hidden_all, chosen[:, :, 2, :], preferred_element_type=jnp.float32
    ).astype(jnp.bfloat16)
    reduced = lax.psum_scatter(terms, "expert", scatter_dimension=0, tiled=True)
    pieces = []
    for part in range(ratio):
        got = None
        for lead in range(ratio):
            pairs = []
            for src_dp in range(dp_groups):
                if src_dp % ratio != part:
                    continue
                for src_ex in range(ex_groups):
                    dst = (ratio * src_ex + lead) * ex_groups + src_dp // ratio
                    pairs.append((src_dp * ex_groups + src_ex, dst))
            moved = lax.ppermute(reduced[lead], ("dp", "expert"), pairs)
            moved = jnp.where(me_dp % ratio == lead, moved, jnp.zeros_like(moved))
            got = moved if got is None else got + moved
        pieces.append(got)
    cols = jnp.concatenate(pieces, axis=-1)
    return collect(cols.reshape(SLOTS * CAP, col_width), target)


def attend(
    hidden_cols,
    lens_here,
    routes,
    gain_vec,
    router,
    query_flat,
    key_value_flat,
    output_flat,
    cosine,
    sine_table,
):
    full_rows = lax.all_gather(hidden_cols, "expert", axis=2, tiled=True)
    req_count, seq_len, model_width = full_rows.shape
    token_count = req_count * seq_len
    expert_count = router.shape[1]
    head_width = cosine.shape[1] * 2
    normed = rms_norm(full_rows.reshape(token_count, model_width), gain_vec)
    logits = jnp.dot(normed, router, preferred_element_type=jnp.float32)
    gate_pair = pair_gates(logits, routes)
    every_query = jnp.einsum(
        "td,dehk->tehk", normed, query_flat, preferred_element_type=jnp.float32
    )
    queries = jnp.take_along_axis(every_query, routes[:, :, None, None], axis=1)
    queries = rope_apply(
        queries.reshape(req_count, seq_len, 2, -1, head_width), cosine, sine_table, 1
    ).astype(jnp.bfloat16)
    key_value = jnp.einsum(
        "td,dchk->tchk", normed, key_value_flat, preferred_element_type=jnp.float32
    ).reshape(req_count, seq_len, 2, -1, head_width)
    key_rows = rope_apply(key_value[:, :, 0], cosine, sine_table, 1).astype(jnp.bfloat16)
    values = key_value[:, :, 1].astype(jnp.bfloat16)
    scores = jnp.einsum(
        "rtkhd,ruhd->rkhtu", queries, key_rows, preferred_element_type=jnp.float32
    ) / math.sqrt(head_width)
    positions = jnp.arange(seq_len, dtype=jnp.int32)
    allowed = (positions[None, None, :] <= positions[None, :, None]) & (
        positions[None, None, :] < lens_here[:, None, None]
    )
    raised = jnp.where(allowed[:, None, None], jnp.exp(scores), 0.0)
    probability = (raised / jnp.sum(raised, axis=-1, keepdims=True)).astype(jnp.bfloat16)
    head_out = jnp.einsum(
        "rkhtu,ruhd->rtkhd", probability, values, preferred_element_type=jnp.float32
    )
    head_out = head_out.reshape(token_count, 2, -1, head_width)
    expert_hits = (
        routes[:, :, None] == jnp.arange(expert_count, dtype=jnp.int32)[None, None, :]
    ).astype(jnp.float32) * gate_pair[:, :, None]
    mixed_heads = jnp.einsum(
        "tke,tkhd->tehd", expert_hits, head_out, precision=lax.Precision.HIGHEST
    ).astype(jnp.bfloat16)
    partial_value = jnp.dot(
        mixed_heads.reshape(token_count, -1), output_flat, preferred_element_type=jnp.float32
    )
    attn_cols = lax.psum_scatter(
        partial_value.astype(jnp.bfloat16), "expert", scatter_dimension=1, tiled=True
    ).astype(jnp.float32)
    return (hidden_cols.reshape(token_count, -1).astype(jnp.float32) + attn_cols).astype(
        jnp.bfloat16
    )


def per_device(
    hidden_in,
    request_order,
    request_lengths,
    attention_routes,
    expert_routes,
    replica_picks,
    old_slots,
    new_slots,
    norm_gain_att,
    norm_gain_ffn,
    att_router,
    query_weight,
    key_value_weight,
    output_weight,
    ffn_router,
    expert_weights,
):
    req_count = hidden_in.shape[1]
    seq_len = hidden_in.shape[2]
    col_width = hidden_in.shape[3]
    model_width = norm_gain_att.shape[0]
    token_count = req_count * seq_len
    dp_groups = lax.axis_size("dp")
    slots_here = SLOTS // dp_groups
    head_width = query_weight.shape[3]
    cosine, sine_table = rope_tables(seq_len, head_width)
    query_flat = query_weight
    key_value_flat = key_value_weight
    output_flat = output_weight.reshape(-1, model_width)
    column_start = lax.axis_index("expert") * col_width
    placements = (old_slots, new_slots)
    results = []
    for batch_index in range(2):
        placement = placements[batch_index]
        lens_all = jnp.take(request_lengths[batch_index], request_order[batch_index])
        lens_here = lax.dynamic_slice_in_dim(lens_all, lax.axis_index("dp") * req_count, req_count)
        live_rows = (jnp.arange(seq_len, dtype=jnp.int32)[None, :] < lens_here[:, None]).reshape(
            token_count
        )
        att_pairs = attention_routes[batch_index].reshape(token_count, 2)
        residual = attend(
            hidden_in[batch_index],
            lens_here,
            att_pairs,
            norm_gain_att,
            att_router,
            query_flat,
            key_value_flat,
            output_flat,
            cosine,
            sine_table,
        )
        ffn_pairs = expert_routes[batch_index].reshape(token_count, 2)
        routes_flat = ffn_pairs.reshape(-1)
        picks_flat = replica_picks[batch_index].reshape(-1)
        live_assign = jnp.repeat(live_rows, 2)
        target = slot_targets(placement, routes_flat, picks_flat, live_assign)
        widened = residual.astype(jnp.float32)
        squares = lax.psum(jnp.sum(widened * widened, axis=1), "expert")
        inv_rms = lax.rsqrt(squares / model_width + EPS)
        gain_cols = lax.dynamic_slice_in_dim(norm_gain_ffn, column_start, col_width)
        normed_cols = (widened * inv_rms[:, None] * gain_cols[None, :]).astype(jnp.bfloat16)
        router_cols = lax.dynamic_slice_in_dim(ffn_router, column_start, col_width, 0)
        logits = lax.psum(
            jnp.dot(normed_cols, router_cols, preferred_element_type=jnp.float32), "expert"
        )
        gate_pair = pair_gates(logits, ffn_pairs)
        expert_out = ffn_stationary(normed_cols, target, placement, expert_weights).astype(
            jnp.float32
        )
        paired = expert_out.reshape(token_count, 2, col_width)
        combined = (
            residual.astype(jnp.float32)
            + gate_pair[:, 0:1] * paired[:, 0]
            + gate_pair[:, 1:2] * paired[:, 1]
        )
        combined = jnp.where(live_rows[:, None], combined, 0.0).astype(jnp.bfloat16)
        results.append(combined.reshape(req_count, seq_len, col_width))
    return jnp.stack(results, axis=0)


def solution(mesh):
    in_specs = (
        P(None, "dp", None, "expert"),
        P(),
        P(),
        P(None, "dp", None, None),
        P(None, "dp", None, None),
        P(None, "dp", None, None),
        P(),
        P(),
        P(),
        P(),
        P(),
        P(None, None, "expert", None),
        P(None, None, "expert", None),
        P(None, "expert", None, None),
        P(),
        P(None, "dp", None, "expert"),
    )
    out_specs = P(None, "dp", None, "expert")
    return jax.shard_map(
        per_device, mesh=mesh, in_specs=in_specs, out_specs=out_specs, check_vma=False
    )
```

```python
import math

import jax
import jax.numpy as jnp
from jax import lax
from jax.sharding import PartitionSpec as P

FEXP = 8
TOPK = 2
SLOTS = 16
CAP = 12


EPS = 1e-06
ROPE_BASE = 10000.0


def rope_tables(seq_len, head_width):
    half_width = head_width // 2
    frequency = ROPE_BASE ** (-(jnp.arange(half_width, dtype=jnp.float32) * 2.0 / head_width))
    angles = jnp.arange(seq_len, dtype=jnp.float32)[:, None] * frequency[None, :]
    return (jnp.cos(angles), jnp.sin(angles))


def rope_apply(values, cosine, sine_table, along_axis):
    half_width = values.shape[-1] // 2
    tile_shape = [1] * values.ndim
    tile_shape[along_axis] = cosine.shape[0]
    tile_shape[-1] = half_width
    cos_part = cosine.reshape(tile_shape)
    sin_part = sine_table.reshape(tile_shape)
    front_half = values[..., :half_width]
    back_half = values[..., half_width:]
    return jnp.concatenate(
        [
            front_half * cos_part - back_half * sin_part,
            back_half * cos_part + front_half * sin_part,
        ],
        axis=-1,
    )


def rms_norm(rows, gain_vec):
    widened = rows.astype(jnp.float32)
    inv_rms = lax.rsqrt(jnp.mean(widened * widened, axis=-1, keepdims=True) + EPS)
    return (widened * inv_rms * gain_vec).astype(jnp.bfloat16)


def pair_gates(logits, routes):
    picked = jnp.take_along_axis(logits, routes, axis=-1)
    leading = jax.nn.sigmoid(picked[..., 0] - picked[..., 1])
    return jnp.stack([leading, 1.0 - leading], axis=-1)


def slot_targets(placement, expert_ids, replica_ids, live_rows):
    slot_range = jnp.arange(SLOTS, dtype=jnp.int32)
    same_expert = placement[:, None] == placement[None, :]
    earlier = slot_range[:, None] > slot_range[None, :]
    occurrence = jnp.sum((same_expert & earlier).astype(jnp.int32), axis=1)
    hosting = (placement[None, :] == jnp.arange(FEXP, dtype=jnp.int32)[:, None]).astype(jnp.int32)
    copies_all = jnp.sum(hosting, axis=1)
    chosen = (expert_ids[:, None] == jnp.arange(FEXP, dtype=jnp.int32)[None, :]).astype(jnp.int32)
    copies = jnp.sum(chosen * copies_all[None, :], axis=1)
    replica = replica_ids % copies
    slot_hits = (
        (placement[None, :] == expert_ids[:, None])
        & (occurrence[None, :] == replica[:, None])
        & live_rows[:, None]
    )
    slot_hits = slot_hits.astype(jnp.int32)
    before = jnp.cumsum(slot_hits, axis=0) - slot_hits
    ranking = jnp.sum(before * slot_hits, axis=1)
    slot_ids = jnp.sum(slot_hits * slot_range[None, :], axis=1)
    within_cap = (jnp.sum(slot_hits, axis=1) > 0) & (ranking < CAP)
    return jnp.where(within_cap, slot_ids * CAP + ranking, SLOTS * CAP)


def fill_buffer(rows, target):
    token_total = rows.shape[0]
    source = jnp.full((SLOTS * CAP + 1,), token_total, jnp.int32)
    source = source.at[target].set(jnp.arange(target.shape[0], dtype=jnp.int32) // TOPK)
    padded = jnp.concatenate([rows, jnp.zeros((1, rows.shape[1]), rows.dtype)], axis=0)
    return jnp.take(padded, source[:-1], axis=0).reshape(SLOTS, CAP, rows.shape[1])


def collect(results, target):
    flat_rows = results.reshape(SLOTS * CAP, results.shape[-1])
    padded = jnp.concatenate(
        [flat_rows, jnp.zeros((1, flat_rows.shape[1]), flat_rows.dtype)], axis=0
    )
    return jnp.take(padded, target, axis=0)


def load_weights(stored, placement):
    dp_groups = lax.axis_size("dp")
    per = SLOTS // dp_groups
    me = lax.axis_index("dp")
    pieces = []
    for shift in range(dp_groups):
        partner = me ^ shift
        ids = lax.dynamic_slice_in_dim(placement, partner * per, per)
        piece = jnp.take(stored, ids, axis=0)
        if shift:
            pairs = [(i, i ^ shift) for i in range(dp_groups)]
            piece = lax.ppermute(piece, "dp", pairs)
        pieces.append(piece)
    return jnp.stack(pieces, axis=1)


def block_order(rows, axis):
    dp_groups = lax.axis_size("dp")
    me = lax.axis_index("dp")
    shape = rows.shape
    split = shape[:axis] + (dp_groups, shape[axis] // dp_groups) + shape[axis + 1 :]
    order = me ^ jnp.arange(dp_groups, dtype=jnp.int32)
    return jnp.take(rows.reshape(split), order, axis=axis).reshape(shape)


def expert_terms(slot_items, loaded):
    per, groups, block, _, cols = loaded.shape
    weights_here = loaded.reshape(per, groups * block, 3, cols)
    slot_items = block_order(slot_items, 3)
    gate_proj = jnp.einsum(
        "gjcd,jdf->gjcf", slot_items, weights_here[:, :, 0, :], preferred_element_type=jnp.float32
    )
    up_proj = jnp.einsum(
        "gjcd,jdf->gjcf", slot_items, weights_here[:, :, 1, :], preferred_element_type=jnp.float32
    )
    hidden = (jax.nn.silu(gate_proj) * up_proj).astype(jnp.bfloat16)
    terms = jnp.einsum(
        "gjcf,jdf->gjcd", hidden, weights_here[:, :, 2, :], preferred_element_type=jnp.float32
    )
    return block_order(terms.astype(jnp.bfloat16), 3)


def ffn_stationary(normed_cols, target, placement, stored):
    dp_groups = lax.axis_size("dp")
    ex_groups = lax.axis_size("expert")
    me_dp = lax.axis_index("dp")
    col_width = normed_cols.shape[1]
    model_width = col_width * ex_groups
    block = model_width // dp_groups
    ratio = dp_groups // ex_groups
    buffer = fill_buffer(normed_cols, target)
    full = lax.all_gather(buffer, "expert", axis=2, tiled=True)
    blocks = full.reshape(SLOTS, CAP, dp_groups, block).transpose(2, 0, 1, 3)
    rows_here = lax.all_to_all(blocks, "dp", split_axis=0, concat_axis=0, tiled=True)
    chosen = stored.at[placement].get(mode="promise_in_bounds")
    partial = jnp.einsum(
        "gscd,sdkf->gsckf", rows_here, chosen[:, :, 0:2, :], preferred_element_type=jnp.float32
    ).astype(jnp.bfloat16)
    summed = lax.psum_scatter(partial, "dp", scatter_dimension=1, tiled=True).astype(jnp.float32)
    hidden = (jax.nn.silu(summed[..., 0, :]) * summed[..., 1, :]).astype(jnp.bfloat16)
    hidden_all = lax.all_gather(hidden, "dp", axis=1, tiled=True)
    terms = jnp.einsum(
        "gscf,sdf->gscd", hidden_all, chosen[:, :, 2, :], preferred_element_type=jnp.float32
    ).astype(jnp.bfloat16)
    reduced = lax.psum_scatter(terms, "expert", scatter_dimension=0, tiled=True)
    pieces = []
    for part in range(ratio):
        got = None
        for lead in range(ratio):
            pairs = []
            for src_dp in range(dp_groups):
                if src_dp % ratio != part:
                    continue
                for src_ex in range(ex_groups):
                    dst = (ratio * src_ex + lead) * ex_groups + src_dp // ratio
                    pairs.append((src_dp * ex_groups + src_ex, dst))
            moved = lax.ppermute(reduced[lead], ("dp", "expert"), pairs)
            moved = jnp.where(me_dp % ratio == lead, moved, jnp.zeros_like(moved))
            got = moved if got is None else got + moved
        pieces.append(got)
    cols = jnp.concatenate(pieces, axis=-1)
    return collect(cols.reshape(SLOTS * CAP, col_width), target)


def attend(
    hidden_cols,
    lens_here,
    routes,
    gain_vec,
    router,
    query_flat,
    key_value_flat,
    output_flat,
    cosine,
    sine_table,
):
    full_rows = lax.all_gather(hidden_cols, "expert", axis=2, tiled=True)
    req_count, seq_len, model_width = full_rows.shape
    token_count = req_count * seq_len
    expert_count = router.shape[1]
    head_width = cosine.shape[1] * 2
    normed = rms_norm(full_rows.reshape(token_count, model_width), gain_vec)
    logits = jnp.dot(normed, router, preferred_element_type=jnp.float32)
    gate_pair = pair_gates(logits, routes)
    every_query = jnp.einsum(
        "td,dehk->tehk", normed, query_flat, preferred_element_type=jnp.float32
    )
    queries = jnp.take_along_axis(every_query, routes[:, :, None, None], axis=1)
    queries = rope_apply(
        queries.reshape(req_count, seq_len, 2, -1, head_width), cosine, sine_table, 1
    ).astype(jnp.bfloat16)
    key_value = jnp.einsum(
        "td,dchk->tchk", normed, key_value_flat, preferred_element_type=jnp.float32
    ).reshape(req_count, seq_len, 2, -1, head_width)
    key_rows = rope_apply(key_value[:, :, 0], cosine, sine_table, 1).astype(jnp.bfloat16)
    values = key_value[:, :, 1].astype(jnp.bfloat16)
    scores = jnp.einsum(
        "rtkhd,ruhd->rkhtu", queries, key_rows, preferred_element_type=jnp.float32
    ) / math.sqrt(head_width)
    positions = jnp.arange(seq_len, dtype=jnp.int32)
    allowed = (positions[None, None, :] <= positions[None, :, None]) & (
        positions[None, None, :] < lens_here[:, None, None]
    )
    raised = jnp.where(allowed[:, None, None], jnp.exp(scores), 0.0)
    probability = (raised / jnp.sum(raised, axis=-1, keepdims=True)).astype(jnp.bfloat16)
    head_out = jnp.einsum(
        "rkhtu,ruhd->rtkhd", probability, values, preferred_element_type=jnp.float32
    )
    head_out = head_out.reshape(token_count, 2, -1, head_width)
    expert_hits = (
        routes[:, :, None] == jnp.arange(expert_count, dtype=jnp.int32)[None, None, :]
    ).astype(jnp.float32) * gate_pair[:, :, None]
    mixed_heads = jnp.einsum(
        "tke,tkhd->tehd", expert_hits, head_out, precision=lax.Precision.HIGHEST
    ).astype(jnp.bfloat16)
    partial_value = jnp.dot(
        mixed_heads.reshape(token_count, -1), output_flat, preferred_element_type=jnp.float32
    )
    attn_cols = lax.psum_scatter(
        partial_value.astype(jnp.bfloat16), "expert", scatter_dimension=1, tiled=True
    ).astype(jnp.float32)
    return (hidden_cols.reshape(token_count, -1).astype(jnp.float32) + attn_cols).astype(
        jnp.bfloat16
    )


def per_device(
    hidden_in,
    request_order,
    request_lengths,
    attention_routes,
    expert_routes,
    replica_picks,
    old_slots,
    new_slots,
    norm_gain_att,
    norm_gain_ffn,
    att_router,
    query_weight,
    key_value_weight,
    output_weight,
    ffn_router,
    expert_weights,
):
    req_count = hidden_in.shape[1]
    seq_len = hidden_in.shape[2]
    col_width = hidden_in.shape[3]
    model_width = norm_gain_att.shape[0]
    token_count = req_count * seq_len
    dp_groups = lax.axis_size("dp")
    slots_here = SLOTS // dp_groups
    head_width = query_weight.shape[3]
    cosine, sine_table = rope_tables(seq_len, head_width)
    query_flat = query_weight
    key_value_flat = key_value_weight
    output_flat = output_weight.reshape(-1, model_width)
    column_start = lax.axis_index("expert") * col_width
    placements = jnp.stack([old_slots, new_slots])
    lens_all = jnp.take_along_axis(request_lengths, request_order, axis=1)
    lens_here = lax.dynamic_slice_in_dim(lens_all, lax.axis_index("dp") * req_count, req_count, 1)

    def one_batch(hidden_b, lens_b, att_b, ffn_b, picks_b, placement):
        live_rows = (jnp.arange(seq_len, dtype=jnp.int32)[None, :] < lens_b[:, None]).reshape(
            token_count
        )
        att_pairs = att_b.reshape(token_count, 2)
        residual = attend(
            hidden_b,
            lens_b,
            att_pairs,
            norm_gain_att,
            att_router,
            query_flat,
            key_value_flat,
            output_flat,
            cosine,
            sine_table,
        )
        ffn_pairs = ffn_b.reshape(token_count, 2)
        routes_flat = ffn_pairs.reshape(-1)
        picks_flat = picks_b.reshape(-1)
        live_assign = jnp.repeat(live_rows, 2)
        target = slot_targets(placement, routes_flat, picks_flat, live_assign)
        widened = residual.astype(jnp.float32)
        squares = lax.psum(jnp.sum(widened * widened, axis=1), "expert")
        inv_rms = lax.rsqrt(squares / model_width + EPS)
        gain_cols = lax.dynamic_slice_in_dim(norm_gain_ffn, column_start, col_width)
        normed_cols = (widened * inv_rms[:, None] * gain_cols[None, :]).astype(jnp.bfloat16)
        router_cols = lax.dynamic_slice_in_dim(ffn_router, column_start, col_width, 0)
        logits = lax.psum(
            jnp.dot(normed_cols, router_cols, preferred_element_type=jnp.float32), "expert"
        )
        gate_pair = pair_gates(logits, ffn_pairs)
        expert_out = ffn_stationary(normed_cols, target, placement, expert_weights).astype(
            jnp.float32
        )
        paired = expert_out.reshape(token_count, 2, col_width)
        combined = (
            residual.astype(jnp.float32)
            + gate_pair[:, 0:1] * paired[:, 0]
            + gate_pair[:, 1:2] * paired[:, 1]
        )
        combined = jnp.where(live_rows[:, None], combined, 0.0).astype(jnp.bfloat16)
        return combined.reshape(req_count, seq_len, col_width)

    return jax.vmap(one_batch)(
        hidden_in, lens_here, attention_routes, expert_routes, replica_picks, placements
    )


def solution(mesh):
    in_specs = (
        P(None, "dp", None, "expert"),
        P(),
        P(),
        P(None, "dp", None, None),
        P(None, "dp", None, None),
        P(None, "dp", None, None),
        P(),
        P(),
        P(),
        P(),
        P(),
        P(None, None, "expert", None),
        P(None, None, "expert", None),
        P(None, "expert", None, None),
        P(),
        P(None, "dp", None, "expert"),
    )
    out_specs = P(None, "dp", None, "expert")
    return jax.shard_map(
        per_device, mesh=mesh, in_specs=in_specs, out_specs=out_specs, check_vma=False
    )
```

```python
import math

import jax
import jax.numpy as jnp
from jax import lax
from jax.sharding import PartitionSpec as P

FEXP = 8
TOPK = 2
SLOTS = 16
CAP = 12


EPS = 1e-06
ROPE_BASE = 10000.0


def rope_tables(seq_len, head_width):
    half_width = head_width // 2
    frequency = ROPE_BASE ** (-(jnp.arange(half_width, dtype=jnp.float32) * 2.0 / head_width))
    angles = jnp.arange(seq_len, dtype=jnp.float32)[:, None] * frequency[None, :]
    return (jnp.cos(angles), jnp.sin(angles))


def rope_apply(values, cosine, sine_table, along_axis):
    half_width = values.shape[-1] // 2
    tile_shape = [1] * values.ndim
    tile_shape[along_axis] = cosine.shape[0]
    tile_shape[-1] = half_width
    cos_part = cosine.reshape(tile_shape)
    sin_part = sine_table.reshape(tile_shape)
    front_half = values[..., :half_width]
    back_half = values[..., half_width:]
    return jnp.concatenate(
        [
            front_half * cos_part - back_half * sin_part,
            back_half * cos_part + front_half * sin_part,
        ],
        axis=-1,
    )


def rms_norm(rows, gain_vec):
    widened = rows.astype(jnp.float32)
    inv_rms = lax.rsqrt(jnp.mean(widened * widened, axis=-1, keepdims=True) + EPS)
    return (widened * inv_rms * gain_vec).astype(jnp.bfloat16)


def pair_gates(logits, routes):
    picked = jnp.take_along_axis(logits, routes, axis=-1)
    leading = jax.nn.sigmoid(picked[..., 0] - picked[..., 1])
    return jnp.stack([leading, 1.0 - leading], axis=-1)


def slot_targets(placement, expert_ids, replica_ids, live_rows):
    slot_range = jnp.arange(SLOTS, dtype=jnp.int32)
    same_expert = placement[:, None] == placement[None, :]
    earlier = slot_range[:, None] > slot_range[None, :]
    occurrence = jnp.sum((same_expert & earlier).astype(jnp.int32), axis=1)
    hosting = (placement[None, :] == jnp.arange(FEXP, dtype=jnp.int32)[:, None]).astype(jnp.int32)
    copies_all = jnp.sum(hosting, axis=1)
    chosen = (expert_ids[:, None] == jnp.arange(FEXP, dtype=jnp.int32)[None, :]).astype(jnp.int32)
    copies = jnp.sum(chosen * copies_all[None, :], axis=1)
    replica = replica_ids % copies
    slot_hits = (
        (placement[None, :] == expert_ids[:, None])
        & (occurrence[None, :] == replica[:, None])
        & live_rows[:, None]
    )
    slot_hits = slot_hits.astype(jnp.int32)
    before = jnp.cumsum(slot_hits, axis=0) - slot_hits
    ranking = jnp.sum(before * slot_hits, axis=1)
    slot_ids = jnp.sum(slot_hits * slot_range[None, :], axis=1)
    within_cap = (jnp.sum(slot_hits, axis=1) > 0) & (ranking < CAP)
    return jnp.where(within_cap, slot_ids * CAP + ranking, SLOTS * CAP)


def fill_buffer(rows, target):
    positions = jnp.arange(SLOTS * CAP, dtype=jnp.int32)
    hits = (target[None, :] == positions[:, None]).reshape(SLOTS * CAP, -1, TOPK).any(axis=2)
    buffer = jnp.dot(hits.astype(rows.dtype), rows, preferred_element_type=jnp.float32)
    return buffer.astype(rows.dtype).reshape(SLOTS, CAP, rows.shape[1])


def collect(results, target):
    flat_rows = results.reshape(SLOTS * CAP, results.shape[-1])
    positions = jnp.arange(SLOTS * CAP, dtype=jnp.int32)
    hits = (target[:, None] == positions[None, :]).astype(flat_rows.dtype)
    return jnp.dot(hits, flat_rows, preferred_element_type=jnp.float32)


def load_weights(stored, placement):
    dp_groups = lax.axis_size("dp")
    per = SLOTS // dp_groups
    me = lax.axis_index("dp")
    pieces = []
    for shift in range(dp_groups):
        partner = me ^ shift
        ids = lax.dynamic_slice_in_dim(placement, partner * per, per)
        piece = jnp.take(stored, ids, axis=0)
        if shift:
            pairs = [(i, i ^ shift) for i in range(dp_groups)]
            piece = lax.ppermute(piece, "dp", pairs)
        pieces.append(piece)
    return jnp.stack(pieces, axis=1)


def block_order(rows, axis):
    dp_groups = lax.axis_size("dp")
    me = lax.axis_index("dp")
    shape = rows.shape
    split = shape[:axis] + (dp_groups, shape[axis] // dp_groups) + shape[axis + 1 :]
    order = me ^ jnp.arange(dp_groups, dtype=jnp.int32)
    return jnp.take(rows.reshape(split), order, axis=axis).reshape(shape)


def expert_terms(slot_items, loaded):
    per, groups, block, _, cols = loaded.shape
    weights_here = loaded.reshape(per, groups * block, 3, cols)
    slot_items = block_order(slot_items, 3)
    gate_proj = jnp.einsum(
        "gjcd,jdf->gjcf", slot_items, weights_here[:, :, 0, :], preferred_element_type=jnp.float32
    )
    up_proj = jnp.einsum(
        "gjcd,jdf->gjcf", slot_items, weights_here[:, :, 1, :], preferred_element_type=jnp.float32
    )
    hidden = (jax.nn.silu(gate_proj) * up_proj).astype(jnp.bfloat16)
    terms = jnp.einsum(
        "gjcf,jdf->gjcd", hidden, weights_here[:, :, 2, :], preferred_element_type=jnp.float32
    )
    return block_order(terms.astype(jnp.bfloat16), 3)


def ffn_stationary(normed_cols, target, placement, stored):
    dp_groups = lax.axis_size("dp")
    ex_groups = lax.axis_size("expert")
    me_dp = lax.axis_index("dp")
    col_width = normed_cols.shape[1]
    model_width = col_width * ex_groups
    block = model_width // dp_groups
    ratio = dp_groups // ex_groups
    buffer = fill_buffer(normed_cols, target)
    full = lax.all_gather(buffer, "expert", axis=2, tiled=True)
    blocks = full.reshape(SLOTS, CAP, dp_groups, block).transpose(2, 0, 1, 3)
    rows_here = lax.all_to_all(blocks, "dp", split_axis=0, concat_axis=0, tiled=True)
    chosen = stored.at[placement].get(mode="promise_in_bounds")
    partial = jnp.einsum(
        "gscd,sdkf->gsckf", rows_here, chosen[:, :, 0:2, :], preferred_element_type=jnp.float32
    ).astype(jnp.bfloat16)
    summed = lax.psum_scatter(partial, "dp", scatter_dimension=1, tiled=True).astype(jnp.float32)
    hidden = (jax.nn.silu(summed[..., 0, :]) * summed[..., 1, :]).astype(jnp.bfloat16)
    hidden_all = lax.all_gather(hidden, "dp", axis=1, tiled=True)
    terms = jnp.einsum(
        "gscf,sdf->gscd", hidden_all, chosen[:, :, 2, :], preferred_element_type=jnp.float32
    ).astype(jnp.bfloat16)
    reduced = lax.psum_scatter(terms, "expert", scatter_dimension=0, tiled=True)
    pieces = []
    for part in range(ratio):
        got = None
        for lead in range(ratio):
            pairs = []
            for src_dp in range(dp_groups):
                if src_dp % ratio != part:
                    continue
                for src_ex in range(ex_groups):
                    dst = (ratio * src_ex + lead) * ex_groups + src_dp // ratio
                    pairs.append((src_dp * ex_groups + src_ex, dst))
            moved = lax.ppermute(reduced[lead], ("dp", "expert"), pairs)
            moved = jnp.where(me_dp % ratio == lead, moved, jnp.zeros_like(moved))
            got = moved if got is None else got + moved
        pieces.append(got)
    cols = jnp.concatenate(pieces, axis=-1)
    return collect(cols.reshape(SLOTS * CAP, col_width), target)


def attend(
    hidden_cols,
    lens_here,
    routes,
    gain_vec,
    router,
    query_flat,
    key_value_flat,
    output_flat,
    cosine,
    sine_table,
):
    full_rows = lax.all_gather(hidden_cols, "expert", axis=2, tiled=True)
    req_count, seq_len, model_width = full_rows.shape
    token_count = req_count * seq_len
    expert_count = router.shape[1]
    head_width = cosine.shape[1] * 2
    normed = rms_norm(full_rows.reshape(token_count, model_width), gain_vec)
    logits = jnp.dot(normed, router, preferred_element_type=jnp.float32)
    gate_pair = pair_gates(logits, routes)
    every_query = jnp.einsum(
        "td,dehk->tehk", normed, query_flat, preferred_element_type=jnp.float32
    )
    queries = jnp.take_along_axis(every_query, routes[:, :, None, None], axis=1)
    queries = rope_apply(
        queries.reshape(req_count, seq_len, 2, -1, head_width), cosine, sine_table, 1
    ).astype(jnp.bfloat16)
    key_value = jnp.einsum(
        "td,dchk->tchk", normed, key_value_flat, preferred_element_type=jnp.float32
    ).reshape(req_count, seq_len, 2, -1, head_width)
    key_rows = rope_apply(key_value[:, :, 0], cosine, sine_table, 1).astype(jnp.bfloat16)
    values = key_value[:, :, 1].astype(jnp.bfloat16)
    scores = jnp.einsum(
        "rtkhd,ruhd->rkhtu", queries, key_rows, preferred_element_type=jnp.float32
    ) / math.sqrt(head_width)
    positions = jnp.arange(seq_len, dtype=jnp.int32)
    allowed = (positions[None, None, :] <= positions[None, :, None]) & (
        positions[None, None, :] < lens_here[:, None, None]
    )
    raised = jnp.where(allowed[:, None, None], jnp.exp(scores), 0.0)
    probability = (raised / jnp.sum(raised, axis=-1, keepdims=True)).astype(jnp.bfloat16)
    head_out = jnp.einsum(
        "rkhtu,ruhd->rtkhd", probability, values, preferred_element_type=jnp.float32
    )
    head_out = head_out.reshape(token_count, 2, -1, head_width)
    expert_hits = (
        routes[:, :, None] == jnp.arange(expert_count, dtype=jnp.int32)[None, None, :]
    ).astype(jnp.float32) * gate_pair[:, :, None]
    mixed_heads = jnp.einsum(
        "tke,tkhd->tehd", expert_hits, head_out, precision=lax.Precision.HIGHEST
    ).astype(jnp.bfloat16)
    partial_value = jnp.dot(
        mixed_heads.reshape(token_count, -1), output_flat, preferred_element_type=jnp.float32
    )
    attn_cols = lax.psum_scatter(
        partial_value.astype(jnp.bfloat16), "expert", scatter_dimension=1, tiled=True
    ).astype(jnp.float32)
    return (hidden_cols.reshape(token_count, -1).astype(jnp.float32) + attn_cols).astype(
        jnp.bfloat16
    )


def per_device(
    hidden_in,
    request_order,
    request_lengths,
    attention_routes,
    expert_routes,
    replica_picks,
    old_slots,
    new_slots,
    norm_gain_att,
    norm_gain_ffn,
    att_router,
    query_weight,
    key_value_weight,
    output_weight,
    ffn_router,
    expert_weights,
):
    req_count = hidden_in.shape[1]
    seq_len = hidden_in.shape[2]
    col_width = hidden_in.shape[3]
    model_width = norm_gain_att.shape[0]
    token_count = req_count * seq_len
    dp_groups = lax.axis_size("dp")
    slots_here = SLOTS // dp_groups
    head_width = query_weight.shape[3]
    cosine, sine_table = rope_tables(seq_len, head_width)
    query_flat = query_weight
    key_value_flat = key_value_weight
    output_flat = output_weight.reshape(-1, model_width)
    column_start = lax.axis_index("expert") * col_width
    placements = jnp.stack([old_slots, new_slots])
    lens_all = jnp.take_along_axis(request_lengths, request_order, axis=1)
    lens_here = lax.dynamic_slice_in_dim(lens_all, lax.axis_index("dp") * req_count, req_count, 1)

    def one_batch(hidden_b, lens_b, att_b, ffn_b, picks_b, placement):
        live_rows = (jnp.arange(seq_len, dtype=jnp.int32)[None, :] < lens_b[:, None]).reshape(
            token_count
        )
        att_pairs = att_b.reshape(token_count, 2)
        residual = attend(
            hidden_b,
            lens_b,
            att_pairs,
            norm_gain_att,
            att_router,
            query_flat,
            key_value_flat,
            output_flat,
            cosine,
            sine_table,
        )
        ffn_pairs = ffn_b.reshape(token_count, 2)
        routes_flat = ffn_pairs.reshape(-1)
        picks_flat = picks_b.reshape(-1)
        live_assign = jnp.repeat(live_rows, 2)
        target = slot_targets(placement, routes_flat, picks_flat, live_assign)
        widened = residual.astype(jnp.float32)
        gain_cols = lax.dynamic_slice_in_dim(norm_gain_ffn, column_start, col_width)
        router_cols = lax.dynamic_slice_in_dim(ffn_router, column_start, col_width, 0)
        scaled = widened * gain_cols[None, :]
        raw_logits = jnp.dot(
            scaled, router_cols.astype(jnp.float32), precision=lax.Precision.HIGHEST
        )
        both = jnp.concatenate([jnp.sum(widened * widened, axis=1)[:, None], raw_logits], axis=1)
        both = lax.psum(both, "expert")
        inv_rms = lax.rsqrt(both[:, 0] / model_width + EPS)
        normed_cols = (widened * inv_rms[:, None] * gain_cols[None, :]).astype(jnp.bfloat16)
        logits = both[:, 1:] * inv_rms[:, None]
        gate_pair = pair_gates(logits, ffn_pairs)
        expert_out = ffn_stationary(normed_cols, target, placement, expert_weights).astype(
            jnp.float32
        )
        paired = expert_out.reshape(token_count, 2, col_width)
        combined = (
            residual.astype(jnp.float32)
            + gate_pair[:, 0:1] * paired[:, 0]
            + gate_pair[:, 1:2] * paired[:, 1]
        )
        combined = jnp.where(live_rows[:, None], combined, 0.0).astype(jnp.bfloat16)
        return combined.reshape(req_count, seq_len, col_width)

    return jax.vmap(one_batch)(
        hidden_in, lens_here, attention_routes, expert_routes, replica_picks, placements
    )


def solution(mesh):
    in_specs = (
        P(None, "dp", None, "expert"),
        P(),
        P(),
        P(None, "dp", None, None),
        P(None, "dp", None, None),
        P(None, "dp", None, None),
        P(),
        P(),
        P(),
        P(),
        P(),
        P(None, None, "expert", None),
        P(None, None, "expert", None),
        P(None, "expert", None, None),
        P(),
        P(None, "dp", None, "expert"),
    )
    out_specs = P(None, "dp", None, "expert")
    return jax.shard_map(
        per_device, mesh=mesh, in_specs=in_specs, out_specs=out_specs, check_vma=False
    )
```

```python
import math

import jax
import jax.numpy as jnp
from jax import lax
from jax.sharding import PartitionSpec as P

FEXP = 8
TOPK = 2
SLOTS = 16
CAP = 12


EPS = 1e-06
ROPE_BASE = 10000.0


def rope_tables(seq_len, head_width):
    half_width = head_width // 2
    frequency = ROPE_BASE ** (-(jnp.arange(half_width, dtype=jnp.float32) * 2.0 / head_width))
    angles = jnp.arange(seq_len, dtype=jnp.float32)[:, None] * frequency[None, :]
    return (jnp.cos(angles), jnp.sin(angles))


def rope_apply(values, cosine, sine_table, along_axis):
    half_width = values.shape[-1] // 2
    tile_shape = [1] * values.ndim
    tile_shape[along_axis] = cosine.shape[0]
    tile_shape[-1] = half_width
    cos_part = cosine.reshape(tile_shape)
    sin_part = sine_table.reshape(tile_shape)
    front_half = values[..., :half_width]
    back_half = values[..., half_width:]
    return jnp.concatenate(
        [
            front_half * cos_part - back_half * sin_part,
            back_half * cos_part + front_half * sin_part,
        ],
        axis=-1,
    )


def rms_norm(rows, gain_vec):
    widened = rows.astype(jnp.float32)
    inv_rms = lax.rsqrt(jnp.mean(widened * widened, axis=-1, keepdims=True) + EPS)
    return (widened * inv_rms * gain_vec).astype(jnp.bfloat16)


def pair_gates(logits, routes):
    picked = jnp.take_along_axis(logits, routes, axis=-1)
    leading = jax.nn.sigmoid(picked[..., 0] - picked[..., 1])
    return jnp.stack([leading, 1.0 - leading], axis=-1)


def slot_targets(placement, expert_ids, replica_ids, live_rows):
    slot_range = jnp.arange(SLOTS, dtype=jnp.int32)
    same_expert = placement[:, None] == placement[None, :]
    earlier = slot_range[:, None] > slot_range[None, :]
    occurrence = jnp.sum((same_expert & earlier).astype(jnp.int32), axis=1)
    hosting = (placement[None, :] == jnp.arange(FEXP, dtype=jnp.int32)[:, None]).astype(jnp.int32)
    copies_all = jnp.sum(hosting, axis=1)
    chosen = (expert_ids[:, None] == jnp.arange(FEXP, dtype=jnp.int32)[None, :]).astype(jnp.int32)
    copies = jnp.sum(chosen * copies_all[None, :], axis=1)
    replica = replica_ids % copies
    slot_hits = (
        (placement[None, :] == expert_ids[:, None])
        & (occurrence[None, :] == replica[:, None])
        & live_rows[:, None]
    )
    slot_hits = slot_hits.astype(jnp.int32)
    before = jnp.cumsum(slot_hits, axis=0) - slot_hits
    ranking = jnp.sum(before * slot_hits, axis=1)
    slot_ids = jnp.sum(slot_hits * slot_range[None, :], axis=1)
    within_cap = (jnp.sum(slot_hits, axis=1) > 0) & (ranking < CAP)
    return jnp.where(within_cap, slot_ids * CAP + ranking, SLOTS * CAP)


def fill_buffer(rows, target):
    positions = jnp.arange(SLOTS * CAP, dtype=jnp.int32)
    hits = (target[None, :] == positions[:, None]).reshape(SLOTS * CAP, -1, TOPK).any(axis=2)
    buffer = jnp.dot(hits.astype(rows.dtype), rows, preferred_element_type=jnp.float32)
    return buffer.astype(rows.dtype).reshape(SLOTS, CAP, rows.shape[1])


def collect(results, target):
    flat_rows = results.reshape(SLOTS * CAP, results.shape[-1])
    positions = jnp.arange(SLOTS * CAP, dtype=jnp.int32)
    hits = (target[:, None] == positions[None, :]).astype(flat_rows.dtype)
    return jnp.dot(hits, flat_rows, preferred_element_type=jnp.float32)


def load_weights(stored, placement):
    dp_groups = lax.axis_size("dp")
    per = SLOTS // dp_groups
    me = lax.axis_index("dp")
    pieces = []
    for shift in range(dp_groups):
        partner = me ^ shift
        ids = lax.dynamic_slice_in_dim(placement, partner * per, per)
        piece = jnp.take(stored, ids, axis=0)
        if shift:
            pairs = [(i, i ^ shift) for i in range(dp_groups)]
            piece = lax.ppermute(piece, "dp", pairs)
        pieces.append(piece)
    return jnp.stack(pieces, axis=1)


def block_order(rows, axis):
    dp_groups = lax.axis_size("dp")
    me = lax.axis_index("dp")
    shape = rows.shape
    split = shape[:axis] + (dp_groups, shape[axis] // dp_groups) + shape[axis + 1 :]
    order = me ^ jnp.arange(dp_groups, dtype=jnp.int32)
    return jnp.take(rows.reshape(split), order, axis=axis).reshape(shape)


def expert_terms(slot_items, loaded):
    per, groups, block, _, cols = loaded.shape
    weights_here = loaded.reshape(per, groups * block, 3, cols)
    slot_items = block_order(slot_items, 3)
    gate_proj = jnp.einsum(
        "gjcd,jdf->gjcf", slot_items, weights_here[:, :, 0, :], preferred_element_type=jnp.float32
    )
    up_proj = jnp.einsum(
        "gjcd,jdf->gjcf", slot_items, weights_here[:, :, 1, :], preferred_element_type=jnp.float32
    )
    hidden = (jax.nn.silu(gate_proj) * up_proj).astype(jnp.bfloat16)
    terms = jnp.einsum(
        "gjcf,jdf->gjcd", hidden, weights_here[:, :, 2, :], preferred_element_type=jnp.float32
    )
    return block_order(terms.astype(jnp.bfloat16), 3)


def ffn_stationary(normed_rows, target, placement, chosen, col_width):
    dp_groups = lax.axis_size("dp")
    ex_groups = lax.axis_size("expert")
    me_dp = lax.axis_index("dp")
    model_width = normed_rows.shape[1]
    block = model_width // dp_groups
    ratio = dp_groups // ex_groups
    full = fill_buffer(normed_rows, target)
    blocks = full.reshape(SLOTS, CAP, dp_groups, block).transpose(2, 0, 1, 3)
    rows_here = lax.all_to_all(blocks, "dp", split_axis=0, concat_axis=0, tiled=True)
    partial = jnp.einsum(
        "gscd,sdkf->gsckf", rows_here, chosen[:, :, 0:2, :], preferred_element_type=jnp.float32
    ).astype(jnp.bfloat16)
    summed = lax.psum_scatter(partial, "dp", scatter_dimension=1, tiled=True).astype(jnp.float32)
    hidden = (jax.nn.silu(summed[..., 0, :]) * summed[..., 1, :]).astype(jnp.bfloat16)
    hidden_all = lax.all_gather(hidden, "dp", axis=1, tiled=True)
    terms = jnp.einsum(
        "gscf,sdf->gscd", hidden_all, chosen[:, :, 2, :], preferred_element_type=jnp.float32
    ).astype(jnp.bfloat16)
    reduced = lax.psum_scatter(terms, "expert", scatter_dimension=0, tiled=True)
    pieces = []
    for part in range(ratio):
        got = None
        for lead in range(ratio):
            pairs = []
            for src_dp in range(dp_groups):
                if src_dp % ratio != part:
                    continue
                for src_ex in range(ex_groups):
                    dst = (ratio * src_ex + lead) * ex_groups + src_dp // ratio
                    pairs.append((src_dp * ex_groups + src_ex, dst))
            moved = lax.ppermute(reduced[lead], ("dp", "expert"), pairs)
            moved = jnp.where(me_dp % ratio == lead, moved, jnp.zeros_like(moved))
            got = moved if got is None else got + moved
        pieces.append(got)
    cols = jnp.concatenate(pieces, axis=-1)
    return collect(cols.reshape(SLOTS * CAP, col_width), target)


def attend(
    hidden_cols,
    lens_here,
    routes,
    gain_vec,
    router,
    query_flat,
    key_value_flat,
    output_flat,
    cosine,
    sine_table,
):
    full_rows = hidden_cols
    req_count, seq_len, model_width = full_rows.shape
    token_count = req_count * seq_len
    expert_count = router.shape[1]
    head_width = cosine.shape[1] * 2
    normed = rms_norm(full_rows.reshape(token_count, model_width), gain_vec)
    logits = jnp.dot(normed, router, preferred_element_type=jnp.float32)
    gate_pair = pair_gates(logits, routes)
    every_query = jnp.einsum(
        "td,dehk->tehk", normed, query_flat, preferred_element_type=jnp.float32
    )
    queries = jnp.take_along_axis(every_query, routes[:, :, None, None], axis=1)
    queries = rope_apply(
        queries.reshape(req_count, seq_len, 2, -1, head_width), cosine, sine_table, 1
    ).astype(jnp.bfloat16)
    key_value = jnp.einsum(
        "td,dchk->tchk", normed, key_value_flat, preferred_element_type=jnp.float32
    ).reshape(req_count, seq_len, 2, -1, head_width)
    key_rows = rope_apply(key_value[:, :, 0], cosine, sine_table, 1).astype(jnp.bfloat16)
    values = key_value[:, :, 1].astype(jnp.bfloat16)
    scores = jnp.einsum(
        "rtkhd,ruhd->rkhtu", queries, key_rows, preferred_element_type=jnp.float32
    ) / math.sqrt(head_width)
    positions = jnp.arange(seq_len, dtype=jnp.int32)
    allowed = (positions[None, None, :] <= positions[None, :, None]) & (
        positions[None, None, :] < lens_here[:, None, None]
    )
    raised = jnp.where(allowed[:, None, None], jnp.exp(scores), 0.0)
    probability = (raised / jnp.sum(raised, axis=-1, keepdims=True)).astype(jnp.bfloat16)
    head_out = jnp.einsum(
        "rkhtu,ruhd->rtkhd", probability, values, preferred_element_type=jnp.float32
    )
    head_out = head_out.reshape(token_count, 2, -1, head_width)
    expert_hits = (
        routes[:, :, None] == jnp.arange(expert_count, dtype=jnp.int32)[None, None, :]
    ).astype(jnp.float32) * gate_pair[:, :, None]
    mixed_heads = jnp.einsum(
        "tke,tkhd->tehd", expert_hits, head_out, precision=lax.Precision.HIGHEST
    ).astype(jnp.bfloat16)
    partial_value = jnp.dot(
        mixed_heads.reshape(token_count, -1), output_flat, preferred_element_type=jnp.float32
    )
    attn_full = lax.psum(partial_value.astype(jnp.bfloat16), "expert").astype(jnp.float32)
    return (full_rows.reshape(token_count, -1).astype(jnp.float32) + attn_full).astype(
        jnp.bfloat16
    )


def per_device(
    hidden_in,
    request_order,
    request_lengths,
    attention_routes,
    expert_routes,
    replica_picks,
    old_slots,
    new_slots,
    norm_gain_att,
    norm_gain_ffn,
    att_router,
    query_weight,
    key_value_weight,
    output_weight,
    ffn_router,
    expert_weights,
):
    req_count = hidden_in.shape[1]
    seq_len = hidden_in.shape[2]
    col_width = hidden_in.shape[3]
    model_width = norm_gain_att.shape[0]
    token_count = req_count * seq_len
    dp_groups = lax.axis_size("dp")
    slots_here = SLOTS // dp_groups
    head_width = query_weight.shape[3]
    cosine, sine_table = rope_tables(seq_len, head_width)
    query_flat = query_weight
    key_value_flat = key_value_weight
    output_flat = output_weight.reshape(-1, model_width)
    column_start = lax.axis_index("expert") * col_width
    placements = jnp.stack([old_slots, new_slots])
    lens_all = jnp.take_along_axis(request_lengths, request_order, axis=1)
    lens_here = lax.dynamic_slice_in_dim(lens_all, lax.axis_index("dp") * req_count, req_count, 1)

    def one_batch(hidden_b, lens_b, att_b, ffn_b, picks_b, placement):
        live_rows = (jnp.arange(seq_len, dtype=jnp.int32)[None, :] < lens_b[:, None]).reshape(
            token_count
        )
        att_pairs = att_b.reshape(token_count, 2)
        full_rows = lax.all_gather(hidden_b, "expert", axis=2, tiled=True)
        chosen = expert_weights.at[placement].get(mode="promise_in_bounds")
        full_rows, chosen = lax.optimization_barrier((full_rows, chosen))
        residual_full = attend(
            full_rows,
            lens_b,
            att_pairs,
            norm_gain_att,
            att_router,
            query_flat,
            key_value_flat,
            output_flat,
            cosine,
            sine_table,
        )
        ffn_pairs = ffn_b.reshape(token_count, 2)
        routes_flat = ffn_pairs.reshape(-1)
        picks_flat = picks_b.reshape(-1)
        live_assign = jnp.repeat(live_rows, 2)
        target = slot_targets(placement, routes_flat, picks_flat, live_assign)
        normed_rows = rms_norm(residual_full, norm_gain_ffn)
        logits = jnp.dot(normed_rows, ffn_router, preferred_element_type=jnp.float32)
        residual = lax.dynamic_slice_in_dim(residual_full, column_start, col_width, 1)
        gate_pair = pair_gates(logits, ffn_pairs)
        expert_out = ffn_stationary(normed_rows, target, placement, chosen, col_width).astype(
            jnp.float32
        )
        paired = expert_out.reshape(token_count, 2, col_width)
        combined = (
            residual.astype(jnp.float32)
            + gate_pair[:, 0:1] * paired[:, 0]
            + gate_pair[:, 1:2] * paired[:, 1]
        )
        combined = jnp.where(live_rows[:, None], combined, 0.0).astype(jnp.bfloat16)
        return combined.reshape(req_count, seq_len, col_width)

    return jax.vmap(one_batch)(
        hidden_in, lens_here, attention_routes, expert_routes, replica_picks, placements
    )


def solution(mesh):
    in_specs = (
        P(None, "dp", None, "expert"),
        P(),
        P(),
        P(None, "dp", None, None),
        P(None, "dp", None, None),
        P(None, "dp", None, None),
        P(),
        P(),
        P(),
        P(),
        P(),
        P(None, None, "expert", None),
        P(None, None, "expert", None),
        P(None, "expert", None, None),
        P(),
        P(None, "dp", None, "expert"),
    )
    out_specs = P(None, "dp", None, "expert")
    return jax.shard_map(
        per_device, mesh=mesh, in_specs=in_specs, out_specs=out_specs, check_vma=False
    )
```

```python
import math

import jax
import jax.numpy as jnp
from jax import lax
from jax.sharding import PartitionSpec as P

FEXP = 8
TOPK = 2
SLOTS = 16
CAP = 12


EPS = 1e-06
ROPE_BASE = 10000.0


def rope_tables(seq_len, head_width):
    half_width = head_width // 2
    frequency = ROPE_BASE ** (-(jnp.arange(half_width, dtype=jnp.float32) * 2.0 / head_width))
    angles = jnp.arange(seq_len, dtype=jnp.float32)[:, None] * frequency[None, :]
    return (jnp.cos(angles), jnp.sin(angles))


def rope_apply(values, cosine, sine_table, along_axis):
    half_width = values.shape[-1] // 2
    tile_shape = [1] * values.ndim
    tile_shape[along_axis] = cosine.shape[0]
    tile_shape[-1] = half_width
    cos_part = cosine.reshape(tile_shape)
    sin_part = sine_table.reshape(tile_shape)
    front_half = values[..., :half_width]
    back_half = values[..., half_width:]
    return jnp.concatenate(
        [
            front_half * cos_part - back_half * sin_part,
            back_half * cos_part + front_half * sin_part,
        ],
        axis=-1,
    )


def rms_norm(rows, gain_vec):
    widened = rows.astype(jnp.float32)
    inv_rms = lax.rsqrt(jnp.mean(widened * widened, axis=-1, keepdims=True) + EPS)
    return (widened * inv_rms * gain_vec).astype(jnp.bfloat16)


def pair_gates(logits, routes):
    picked = jnp.take_along_axis(logits, routes, axis=-1)
    leading = jax.nn.sigmoid(picked[..., 0] - picked[..., 1])
    return jnp.stack([leading, 1.0 - leading], axis=-1)


def slot_targets(placement, expert_ids, replica_ids, live_rows):
    slot_range = jnp.arange(SLOTS, dtype=jnp.int32)
    same_expert = placement[:, None] == placement[None, :]
    earlier = slot_range[:, None] > slot_range[None, :]
    occurrence = jnp.sum((same_expert & earlier).astype(jnp.int32), axis=1)
    hosting = (placement[None, :] == jnp.arange(FEXP, dtype=jnp.int32)[:, None]).astype(jnp.int32)
    copies_all = jnp.sum(hosting, axis=1)
    chosen = (expert_ids[:, None] == jnp.arange(FEXP, dtype=jnp.int32)[None, :]).astype(jnp.int32)
    copies = jnp.sum(chosen * copies_all[None, :], axis=1)
    replica = replica_ids % copies
    slot_hits = (
        (placement[None, :] == expert_ids[:, None])
        & (occurrence[None, :] == replica[:, None])
        & live_rows[:, None]
    )
    slot_hits = slot_hits.astype(jnp.int32)
    before = jnp.cumsum(slot_hits, axis=0) - slot_hits
    ranking = jnp.sum(before * slot_hits, axis=1)
    slot_ids = jnp.sum(slot_hits * slot_range[None, :], axis=1)
    within_cap = (jnp.sum(slot_hits, axis=1) > 0) & (ranking < CAP)
    return jnp.where(within_cap, slot_ids * CAP + ranking, SLOTS * CAP)


def fill_buffer(rows, target):
    positions = jnp.arange(SLOTS * CAP, dtype=jnp.int32)
    hits = (target[None, :] == positions[:, None]).reshape(SLOTS * CAP, -1, TOPK).any(axis=2)
    buffer = jnp.dot(hits.astype(rows.dtype), rows, preferred_element_type=jnp.float32)
    return buffer.astype(rows.dtype).reshape(SLOTS, CAP, rows.shape[1])


def collect(results, target):
    flat_rows = results.reshape(SLOTS * CAP, results.shape[-1])
    positions = jnp.arange(SLOTS * CAP, dtype=jnp.int32)
    hits = (target[:, None] == positions[None, :]).astype(flat_rows.dtype)
    return jnp.dot(hits, flat_rows, preferred_element_type=jnp.float32)


def load_weights(stored, placement):
    dp_groups = lax.axis_size("dp")
    per = SLOTS // dp_groups
    me = lax.axis_index("dp")
    pieces = []
    for shift in range(dp_groups):
        partner = me ^ shift
        ids = lax.dynamic_slice_in_dim(placement, partner * per, per)
        piece = jnp.take(stored, ids, axis=0)
        if shift:
            pairs = [(i, i ^ shift) for i in range(dp_groups)]
            piece = lax.ppermute(piece, "dp", pairs)
        pieces.append(piece)
    return jnp.stack(pieces, axis=1)


def block_order(rows, axis):
    dp_groups = lax.axis_size("dp")
    me = lax.axis_index("dp")
    shape = rows.shape
    split = shape[:axis] + (dp_groups, shape[axis] // dp_groups) + shape[axis + 1 :]
    order = me ^ jnp.arange(dp_groups, dtype=jnp.int32)
    return jnp.take(rows.reshape(split), order, axis=axis).reshape(shape)


def expert_terms(slot_items, loaded):
    per, groups, block, _, cols = loaded.shape
    weights_here = loaded.reshape(per, groups * block, 3, cols)
    slot_items = block_order(slot_items, 3)
    gate_proj = jnp.einsum(
        "gjcd,jdf->gjcf", slot_items, weights_here[:, :, 0, :], preferred_element_type=jnp.float32
    )
    up_proj = jnp.einsum(
        "gjcd,jdf->gjcf", slot_items, weights_here[:, :, 1, :], preferred_element_type=jnp.float32
    )
    hidden = (jax.nn.silu(gate_proj) * up_proj).astype(jnp.bfloat16)
    terms = jnp.einsum(
        "gjcf,jdf->gjcd", hidden, weights_here[:, :, 2, :], preferred_element_type=jnp.float32
    )
    return block_order(terms.astype(jnp.bfloat16), 3)


def reduce_slots(partial):
    dp_groups = lax.axis_size("dp")
    me = lax.axis_index("dp")
    per = SLOTS // dp_groups
    parity = me % 2
    half = me // 2
    split = partial.reshape((dp_groups // 2, 2, per) + partial.shape[1:])
    keep = lax.dynamic_index_in_dim(split, parity, axis=1, keepdims=False)
    give = lax.dynamic_index_in_dim(split, 1 - parity, axis=1, keepdims=False)
    got = lax.ppermute(give, "dp", [(i, i ^ 1) for i in range(dp_groups)])
    pairs_sum = keep.astype(jnp.float32) + got.astype(jnp.float32)
    total = lax.dynamic_index_in_dim(pairs_sum, half, axis=0, keepdims=False)
    sendable = pairs_sum.astype(jnp.bfloat16)
    for shift in range(1, dp_groups // 2):
        piece = lax.dynamic_index_in_dim(sendable, half ^ shift, axis=0, keepdims=False)
        moved = lax.ppermute(piece, "dp", [(i, i ^ (2 * shift)) for i in range(dp_groups)])
        total = total + moved.astype(jnp.float32)
    return total


def gather_slots(hidden):
    dp_groups = lax.axis_size("dp")
    me = lax.axis_index("dp")
    parity = me % 2
    half = me // 2
    chunks = [hidden]
    for shift in range(1, dp_groups // 2):
        chunks.append(lax.ppermute(hidden, "dp", [(i, i ^ (2 * shift)) for i in range(dp_groups)]))
    stacked = jnp.stack(chunks)
    by_half = jnp.take(stacked, half ^ jnp.arange(dp_groups // 2, dtype=jnp.int32), axis=0)
    other = lax.ppermute(by_half, "dp", [(i, i ^ 1) for i in range(dp_groups)])
    pair = jnp.where(
        parity == 0, jnp.stack([by_half, other], axis=1), jnp.stack([other, by_half], axis=1)
    )
    return pair.reshape((SLOTS,) + hidden.shape[1:])


def ffn_batched(normed_rows, target, chosen, col_width):
    dp_groups = lax.axis_size("dp")
    ex_groups = lax.axis_size("expert")
    me_dp = lax.axis_index("dp")
    batches, _, model_width = normed_rows.shape
    block = model_width // dp_groups
    ratio = dp_groups // ex_groups
    full = jax.vmap(fill_buffer)(normed_rows, target)
    blocks = full.reshape(batches, SLOTS, CAP, dp_groups, block).transpose(3, 1, 0, 2, 4)
    rows_here = lax.all_to_all(blocks, "dp", split_axis=0, concat_axis=0, tiled=True)
    rows_here = rows_here.transpose(1, 2, 0, 3, 4)
    partial = jnp.einsum(
        "sbgcd,sbdkf->sbgckf",
        rows_here,
        chosen[:, :, :, 0:2, :],
        preferred_element_type=jnp.float32,
    ).astype(jnp.bfloat16)
    summed = reduce_slots(partial)
    hidden = (jax.nn.silu(summed[..., 0, :]) * summed[..., 1, :]).astype(jnp.bfloat16)
    hidden_all = gather_slots(hidden)
    terms = jnp.einsum(
        "sbgcf,sbdf->sbgcd", hidden_all, chosen[:, :, :, 2, :], preferred_element_type=jnp.float32
    ).astype(jnp.bfloat16)
    reduced = lax.psum_scatter(terms, "expert", scatter_dimension=2, tiled=True)
    pieces = []
    for part in range(ratio):
        got = None
        for lead in range(ratio):
            pairs = []
            for src_dp in range(dp_groups):
                if src_dp % ratio != part:
                    continue
                for src_ex in range(ex_groups):
                    dst = (ratio * src_ex + lead) * ex_groups + src_dp // ratio
                    pairs.append((src_dp * ex_groups + src_ex, dst))
            moved = lax.ppermute(reduced[:, :, lead], ("dp", "expert"), pairs)
            moved = jnp.where(me_dp % ratio == lead, moved, jnp.zeros_like(moved))
            got = moved if got is None else got + moved
        pieces.append(got)
    cols = jnp.concatenate(pieces, axis=-1).transpose(1, 0, 2, 3)
    return jax.vmap(collect)(cols, target)


def attend(
    hidden_cols,
    lens_here,
    routes,
    gain_vec,
    router,
    query_flat,
    key_value_flat,
    output_flat,
    cosine,
    sine_table,
):
    full_rows = hidden_cols
    req_count, seq_len, model_width = full_rows.shape
    token_count = req_count * seq_len
    expert_count = router.shape[1]
    head_width = cosine.shape[1] * 2
    normed = rms_norm(full_rows.reshape(token_count, model_width), gain_vec)
    logits = jnp.dot(normed, router, preferred_element_type=jnp.float32)
    gate_pair = pair_gates(logits, routes)
    every_query = jnp.einsum(
        "td,dehk->tehk", normed, query_flat, preferred_element_type=jnp.float32
    )
    queries = jnp.take_along_axis(every_query, routes[:, :, None, None], axis=1)
    queries = rope_apply(
        queries.reshape(req_count, seq_len, 2, -1, head_width), cosine, sine_table, 1
    ).astype(jnp.bfloat16)
    key_value = jnp.einsum(
        "td,dchk->tchk", normed, key_value_flat, preferred_element_type=jnp.float32
    ).reshape(req_count, seq_len, 2, -1, head_width)
    key_rows = rope_apply(key_value[:, :, 0], cosine, sine_table, 1).astype(jnp.bfloat16)
    values = key_value[:, :, 1].astype(jnp.bfloat16)
    scores = jnp.einsum(
        "rtkhd,ruhd->rkhtu", queries, key_rows, preferred_element_type=jnp.float32
    ) / math.sqrt(head_width)
    positions = jnp.arange(seq_len, dtype=jnp.int32)
    allowed = (positions[None, None, :] <= positions[None, :, None]) & (
        positions[None, None, :] < lens_here[:, None, None]
    )
    raised = jnp.where(allowed[:, None, None], jnp.exp(scores), 0.0)
    probability = (raised / jnp.sum(raised, axis=-1, keepdims=True)).astype(jnp.bfloat16)
    head_out = jnp.einsum(
        "rkhtu,ruhd->rtkhd", probability, values, preferred_element_type=jnp.float32
    )
    head_out = head_out.reshape(token_count, 2, -1, head_width)
    expert_hits = (
        routes[:, :, None] == jnp.arange(expert_count, dtype=jnp.int32)[None, None, :]
    ).astype(jnp.float32) * gate_pair[:, :, None]
    mixed_heads = jnp.einsum(
        "tke,tkhd->tehd", expert_hits, head_out, precision=lax.Precision.HIGHEST
    ).astype(jnp.bfloat16)
    partial_value = jnp.dot(
        mixed_heads.reshape(token_count, -1), output_flat, preferred_element_type=jnp.float32
    )
    attn_full = lax.psum(partial_value.astype(jnp.bfloat16), "expert").astype(jnp.float32)
    return (full_rows.reshape(token_count, -1).astype(jnp.float32) + attn_full).astype(
        jnp.bfloat16
    )


def per_device(
    hidden_in,
    request_order,
    request_lengths,
    attention_routes,
    expert_routes,
    replica_picks,
    old_slots,
    new_slots,
    norm_gain_att,
    norm_gain_ffn,
    att_router,
    query_weight,
    key_value_weight,
    output_weight,
    ffn_router,
    expert_weights,
):
    req_count = hidden_in.shape[1]
    seq_len = hidden_in.shape[2]
    col_width = hidden_in.shape[3]
    model_width = norm_gain_att.shape[0]
    token_count = req_count * seq_len
    dp_groups = lax.axis_size("dp")
    slots_here = SLOTS // dp_groups
    head_width = query_weight.shape[3]
    cosine, sine_table = rope_tables(seq_len, head_width)
    query_flat = query_weight
    key_value_flat = key_value_weight
    output_flat = output_weight.reshape(-1, model_width)
    column_start = lax.axis_index("expert") * col_width
    placements = jnp.stack([old_slots, new_slots])
    lens_all = jnp.take_along_axis(request_lengths, request_order, axis=1)
    lens_here = lax.dynamic_slice_in_dim(lens_all, lax.axis_index("dp") * req_count, req_count, 1)

    full_in = lax.all_gather(hidden_in, "expert", axis=3, tiled=True)
    chosen = expert_weights.at[placements.T].get(mode="promise_in_bounds")
    full_in, chosen = lax.optimization_barrier((full_in, chosen))

    def front(full_rows, lens_b, att_b, ffn_b, picks_b, placement):
        live_rows = (jnp.arange(seq_len, dtype=jnp.int32)[None, :] < lens_b[:, None]).reshape(
            token_count
        )
        att_pairs = att_b.reshape(token_count, 2)
        residual_full = attend(
            full_rows,
            lens_b,
            att_pairs,
            norm_gain_att,
            att_router,
            query_flat,
            key_value_flat,
            output_flat,
            cosine,
            sine_table,
        )
        ffn_pairs = ffn_b.reshape(token_count, 2)
        live_assign = jnp.repeat(live_rows, 2)
        target = slot_targets(placement, ffn_pairs.reshape(-1), picks_b.reshape(-1), live_assign)
        normed_rows = rms_norm(residual_full, norm_gain_ffn)
        logits = jnp.dot(normed_rows, ffn_router, preferred_element_type=jnp.float32)
        gate_pair = pair_gates(logits, ffn_pairs)
        residual = lax.dynamic_slice_in_dim(residual_full, column_start, col_width, 1)
        return residual, normed_rows, target, gate_pair, live_rows

    residual, normed_rows, target, gate_pair, live_rows = jax.vmap(front)(
        full_in, lens_here, attention_routes, expert_routes, replica_picks, placements
    )
    expert_out = ffn_batched(normed_rows, target, chosen, col_width)
    batches = expert_out.shape[0]
    paired = expert_out.reshape(batches, token_count, 2, col_width)
    combined = (
        residual.astype(jnp.float32)
        + gate_pair[..., 0:1] * paired[:, :, 0]
        + gate_pair[..., 1:2] * paired[:, :, 1]
    )
    combined = jnp.where(live_rows[..., None], combined, 0.0).astype(jnp.bfloat16)
    return combined.reshape(batches, req_count, seq_len, col_width)


def solution(mesh):
    in_specs = (
        P(None, "dp", None, "expert"),
        P(),
        P(),
        P(None, "dp", None, None),
        P(None, "dp", None, None),
        P(None, "dp", None, None),
        P(),
        P(),
        P(),
        P(),
        P(),
        P(None, None, "expert", None),
        P(None, None, "expert", None),
        P(None, "expert", None, None),
        P(),
        P(None, "dp", None, "expert"),
    )
    out_specs = P(None, "dp", None, "expert")
    return jax.shard_map(
        per_device, mesh=mesh, in_specs=in_specs, out_specs=out_specs, check_vma=False
    )
```

```python
import math

import jax
import jax.numpy as jnp
from jax import lax
from jax.sharding import PartitionSpec as P

FEXP = 8
TOPK = 2
SLOTS = 16
CAP = 12


EPS = 1e-06
ROPE_BASE = 10000.0


def rope_tables(seq_len, head_width):
    half_width = head_width // 2
    frequency = ROPE_BASE ** (-(jnp.arange(half_width, dtype=jnp.float32) * 2.0 / head_width))
    angles = jnp.arange(seq_len, dtype=jnp.float32)[:, None] * frequency[None, :]
    return (jnp.cos(angles), jnp.sin(angles))


def rope_apply(values, cosine, sine_table, along_axis):
    half_width = values.shape[-1] // 2
    tile_shape = [1] * values.ndim
    tile_shape[along_axis] = cosine.shape[0]
    tile_shape[-1] = half_width
    cos_part = cosine.reshape(tile_shape)
    sin_part = sine_table.reshape(tile_shape)
    front_half = values[..., :half_width]
    back_half = values[..., half_width:]
    return jnp.concatenate(
        [
            front_half * cos_part - back_half * sin_part,
            back_half * cos_part + front_half * sin_part,
        ],
        axis=-1,
    )


def rms_norm(rows, gain_vec):
    widened = rows.astype(jnp.float32)
    inv_rms = lax.rsqrt(jnp.mean(widened * widened, axis=-1, keepdims=True) + EPS)
    return (widened * inv_rms * gain_vec).astype(jnp.bfloat16)


def pair_gates(logits, routes):
    picked = jnp.take_along_axis(logits, routes, axis=-1)
    leading = jax.nn.sigmoid(picked[..., 0] - picked[..., 1])
    return jnp.stack([leading, 1.0 - leading], axis=-1)


def slot_targets(placement, expert_ids, replica_ids, live_rows):
    slot_range = jnp.arange(SLOTS, dtype=jnp.int32)
    same_expert = placement[:, None] == placement[None, :]
    earlier = slot_range[:, None] > slot_range[None, :]
    occurrence = jnp.sum((same_expert & earlier).astype(jnp.int32), axis=1)
    hosting = (placement[None, :] == jnp.arange(FEXP, dtype=jnp.int32)[:, None]).astype(jnp.int32)
    copies_all = jnp.sum(hosting, axis=1)
    chosen = (expert_ids[:, None] == jnp.arange(FEXP, dtype=jnp.int32)[None, :]).astype(jnp.int32)
    copies = jnp.sum(chosen * copies_all[None, :], axis=1)
    replica = replica_ids % copies
    slot_hits = (
        (placement[None, :] == expert_ids[:, None])
        & (occurrence[None, :] == replica[:, None])
        & live_rows[:, None]
    )
    slot_hits = slot_hits.astype(jnp.int32)
    before = jnp.cumsum(slot_hits, axis=0) - slot_hits
    ranking = jnp.sum(before * slot_hits, axis=1)
    slot_ids = jnp.sum(slot_hits * slot_range[None, :], axis=1)
    within_cap = (jnp.sum(slot_hits, axis=1) > 0) & (ranking < CAP)
    return jnp.where(within_cap, slot_ids * CAP + ranking, SLOTS * CAP)


def fill_buffer(rows, target):
    positions = jnp.arange(SLOTS * CAP, dtype=jnp.int32)
    hits = (target[None, :] == positions[:, None]).reshape(SLOTS * CAP, -1, TOPK).any(axis=2)
    buffer = jnp.dot(hits.astype(rows.dtype), rows, preferred_element_type=jnp.float32)
    return buffer.astype(rows.dtype).reshape(SLOTS, CAP, rows.shape[1])


def collect(results, target):
    flat_rows = results.reshape(SLOTS * CAP, results.shape[-1])
    positions = jnp.arange(SLOTS * CAP, dtype=jnp.int32)
    hits = (target[:, None] == positions[None, :]).astype(flat_rows.dtype)
    return jnp.dot(hits, flat_rows, preferred_element_type=jnp.float32)


def load_weights(stored, placement):
    dp_groups = lax.axis_size("dp")
    per = SLOTS // dp_groups
    me = lax.axis_index("dp")
    pieces = []
    for shift in range(dp_groups):
        partner = me ^ shift
        ids = lax.dynamic_slice_in_dim(placement, partner * per, per)
        piece = jnp.take(stored, ids, axis=0)
        if shift:
            pairs = [(i, i ^ shift) for i in range(dp_groups)]
            piece = lax.ppermute(piece, "dp", pairs)
        pieces.append(piece)
    return jnp.stack(pieces, axis=1)


def block_order(rows, axis):
    dp_groups = lax.axis_size("dp")
    me = lax.axis_index("dp")
    shape = rows.shape
    split = shape[:axis] + (dp_groups, shape[axis] // dp_groups) + shape[axis + 1 :]
    order = me ^ jnp.arange(dp_groups, dtype=jnp.int32)
    return jnp.take(rows.reshape(split), order, axis=axis).reshape(shape)


def expert_terms(slot_items, loaded):
    per, groups, block, _, cols = loaded.shape
    weights_here = loaded.reshape(per, groups * block, 3, cols)
    slot_items = block_order(slot_items, 3)
    gate_proj = jnp.einsum(
        "gjcd,jdf->gjcf", slot_items, weights_here[:, :, 0, :], preferred_element_type=jnp.float32
    )
    up_proj = jnp.einsum(
        "gjcd,jdf->gjcf", slot_items, weights_here[:, :, 1, :], preferred_element_type=jnp.float32
    )
    hidden = (jax.nn.silu(gate_proj) * up_proj).astype(jnp.bfloat16)
    terms = jnp.einsum(
        "gjcf,jdf->gjcd", hidden, weights_here[:, :, 2, :], preferred_element_type=jnp.float32
    )
    return block_order(terms.astype(jnp.bfloat16), 3)


def reduce_slots(partial):
    dp_groups = lax.axis_size("dp")
    me = lax.axis_index("dp")
    per = SLOTS // dp_groups
    parity = me % 2
    half = me // 2
    split = partial.reshape((dp_groups // 2, 2, per) + partial.shape[1:])
    keep = lax.dynamic_index_in_dim(split, parity, axis=1, keepdims=False)
    give = lax.dynamic_index_in_dim(split, 1 - parity, axis=1, keepdims=False)
    got = lax.ppermute(give, "dp", [(i, i ^ 1) for i in range(dp_groups)])
    pairs_sum = keep.astype(jnp.float32) + got.astype(jnp.float32)
    total = lax.dynamic_index_in_dim(pairs_sum, half, axis=0, keepdims=False)
    sendable = pairs_sum.astype(jnp.bfloat16)
    for shift in range(1, dp_groups // 2):
        piece = lax.dynamic_index_in_dim(sendable, half ^ shift, axis=0, keepdims=False)
        moved = lax.ppermute(piece, "dp", [(i, i ^ (2 * shift)) for i in range(dp_groups)])
        total = total + moved.astype(jnp.float32)
    return total


def gather_slots(hidden):
    dp_groups = lax.axis_size("dp")
    me = lax.axis_index("dp")
    parity = me % 2
    half = me // 2
    chunks = [hidden]
    for shift in range(1, dp_groups // 2):
        chunks.append(lax.ppermute(hidden, "dp", [(i, i ^ (2 * shift)) for i in range(dp_groups)]))
    stacked = jnp.stack(chunks)
    by_half = jnp.take(stacked, half ^ jnp.arange(dp_groups // 2, dtype=jnp.int32), axis=0)
    other = lax.ppermute(by_half, "dp", [(i, i ^ 1) for i in range(dp_groups)])
    pair = jnp.where(
        parity == 0, jnp.stack([by_half, other], axis=1), jnp.stack([other, by_half], axis=1)
    )
    return pair.reshape((SLOTS,) + hidden.shape[1:])


def ffn_batched(normed_rows, target, chosen, col_width):
    dp_groups = lax.axis_size("dp")
    ex_groups = lax.axis_size("expert")
    me_dp = lax.axis_index("dp")
    batches, _, model_width = normed_rows.shape
    block = model_width // dp_groups
    ratio = dp_groups // ex_groups
    full = jax.vmap(fill_buffer)(normed_rows, target)
    blocks = full.reshape(batches, SLOTS, CAP, dp_groups, block).transpose(3, 1, 0, 2, 4)
    rows_here = lax.all_to_all(blocks, "dp", split_axis=0, concat_axis=0, tiled=True)
    rows_here = rows_here.transpose(1, 2, 0, 3, 4)
    partial = jnp.einsum(
        "sbgcd,sbdkf->sbgckf",
        rows_here,
        chosen[:, :, :, 0:2, :],
        preferred_element_type=jnp.float32,
    ).astype(jnp.bfloat16)
    summed = lax.psum_scatter(partial, "dp", scatter_dimension=0, tiled=True).astype(jnp.float32)
    hidden = (jax.nn.silu(summed[..., 0, :]) * summed[..., 1, :]).astype(jnp.bfloat16)
    hidden_all = gather_slots(hidden)
    terms = jnp.einsum(
        "sbgcf,sbdf->sbgcd", hidden_all, chosen[:, :, :, 2, :], preferred_element_type=jnp.float32
    ).astype(jnp.bfloat16)
    reduced = lax.psum_scatter(terms, "expert", scatter_dimension=2, tiled=True)
    pieces = []
    for part in range(ratio):
        got = None
        for lead in range(ratio):
            pairs = []
            for src_dp in range(dp_groups):
                if src_dp % ratio != part:
                    continue
                for src_ex in range(ex_groups):
                    dst = (ratio * src_ex + lead) * ex_groups + src_dp // ratio
                    pairs.append((src_dp * ex_groups + src_ex, dst))
            moved = lax.ppermute(reduced[:, :, lead], ("dp", "expert"), pairs)
            moved = jnp.where(me_dp % ratio == lead, moved, jnp.zeros_like(moved))
            got = moved if got is None else got + moved
        pieces.append(got)
    cols = jnp.concatenate(pieces, axis=-1).transpose(1, 0, 2, 3)
    return jax.vmap(collect)(cols, target)


def attend(
    hidden_cols,
    lens_here,
    routes,
    gain_vec,
    router,
    query_flat,
    key_value_flat,
    output_flat,
    cosine,
    sine_table,
):
    full_rows = hidden_cols
    req_count, seq_len, model_width = full_rows.shape
    token_count = req_count * seq_len
    expert_count = router.shape[1]
    head_width = cosine.shape[1] * 2
    normed = rms_norm(full_rows.reshape(token_count, model_width), gain_vec)
    logits = jnp.dot(normed, router, preferred_element_type=jnp.float32)
    gate_pair = pair_gates(logits, routes)
    every_query = jnp.einsum(
        "td,dehk->tehk", normed, query_flat, preferred_element_type=jnp.float32
    )
    queries = jnp.take_along_axis(every_query, routes[:, :, None, None], axis=1)
    queries = rope_apply(
        queries.reshape(req_count, seq_len, 2, -1, head_width), cosine, sine_table, 1
    ).astype(jnp.bfloat16)
    key_value = jnp.einsum(
        "td,dchk->tchk", normed, key_value_flat, preferred_element_type=jnp.float32
    ).reshape(req_count, seq_len, 2, -1, head_width)
    key_rows = rope_apply(key_value[:, :, 0], cosine, sine_table, 1).astype(jnp.bfloat16)
    values = key_value[:, :, 1].astype(jnp.bfloat16)
    scores = jnp.einsum(
        "rtkhd,ruhd->rkhtu", queries, key_rows, preferred_element_type=jnp.float32
    ) / math.sqrt(head_width)
    positions = jnp.arange(seq_len, dtype=jnp.int32)
    allowed = (positions[None, None, :] <= positions[None, :, None]) & (
        positions[None, None, :] < lens_here[:, None, None]
    )
    raised = jnp.where(allowed[:, None, None], jnp.exp(scores), 0.0)
    probability = (raised / jnp.sum(raised, axis=-1, keepdims=True)).astype(jnp.bfloat16)
    head_out = jnp.einsum(
        "rkhtu,ruhd->rtkhd", probability, values, preferred_element_type=jnp.float32
    )
    head_out = head_out.reshape(token_count, 2, -1, head_width)
    expert_hits = (
        routes[:, :, None] == jnp.arange(expert_count, dtype=jnp.int32)[None, None, :]
    ).astype(jnp.float32) * gate_pair[:, :, None]
    mixed_heads = jnp.einsum(
        "tke,tkhd->tehd", expert_hits, head_out, precision=lax.Precision.HIGHEST
    ).astype(jnp.bfloat16)
    partial_value = jnp.dot(
        mixed_heads.reshape(token_count, -1), output_flat, preferred_element_type=jnp.float32
    )
    attn_full = lax.psum(partial_value.astype(jnp.bfloat16), "expert").astype(jnp.float32)
    return (full_rows.reshape(token_count, -1).astype(jnp.float32) + attn_full).astype(
        jnp.bfloat16
    )


def per_device(
    hidden_in,
    request_order,
    request_lengths,
    attention_routes,
    expert_routes,
    replica_picks,
    old_slots,
    new_slots,
    norm_gain_att,
    norm_gain_ffn,
    att_router,
    query_weight,
    key_value_weight,
    output_weight,
    ffn_router,
    expert_weights,
):
    req_count = hidden_in.shape[1]
    seq_len = hidden_in.shape[2]
    col_width = hidden_in.shape[3]
    model_width = norm_gain_att.shape[0]
    token_count = req_count * seq_len
    dp_groups = lax.axis_size("dp")
    slots_here = SLOTS // dp_groups
    head_width = query_weight.shape[3]
    cosine, sine_table = rope_tables(seq_len, head_width)
    query_flat = query_weight
    key_value_flat = key_value_weight
    output_flat = output_weight.reshape(-1, model_width)
    column_start = lax.axis_index("expert") * col_width
    placements = jnp.stack([old_slots, new_slots])
    lens_all = jnp.take_along_axis(request_lengths, request_order, axis=1)
    lens_here = lax.dynamic_slice_in_dim(lens_all, lax.axis_index("dp") * req_count, req_count, 1)

    full_in = lax.all_gather(hidden_in, "expert", axis=3, tiled=True)
    chosen = expert_weights.at[placements.T].get(mode="promise_in_bounds")
    full_in, chosen = lax.optimization_barrier((full_in, chosen))

    def front(full_rows, lens_b, att_b, ffn_b, picks_b, placement):
        live_rows = (jnp.arange(seq_len, dtype=jnp.int32)[None, :] < lens_b[:, None]).reshape(
            token_count
        )
        att_pairs = att_b.reshape(token_count, 2)
        residual_full = attend(
            full_rows,
            lens_b,
            att_pairs,
            norm_gain_att,
            att_router,
            query_flat,
            key_value_flat,
            output_flat,
            cosine,
            sine_table,
        )
        ffn_pairs = ffn_b.reshape(token_count, 2)
        live_assign = jnp.repeat(live_rows, 2)
        target = slot_targets(placement, ffn_pairs.reshape(-1), picks_b.reshape(-1), live_assign)
        normed_rows = rms_norm(residual_full, norm_gain_ffn)
        logits = jnp.dot(normed_rows, ffn_router, preferred_element_type=jnp.float32)
        gate_pair = pair_gates(logits, ffn_pairs)
        residual = lax.dynamic_slice_in_dim(residual_full, column_start, col_width, 1)
        return residual, normed_rows, target, gate_pair, live_rows

    residual, normed_rows, target, gate_pair, live_rows = jax.vmap(front)(
        full_in, lens_here, attention_routes, expert_routes, replica_picks, placements
    )
    expert_out = ffn_batched(normed_rows, target, chosen, col_width)
    batches = expert_out.shape[0]
    paired = expert_out.reshape(batches, token_count, 2, col_width)
    combined = (
        residual.astype(jnp.float32)
        + gate_pair[..., 0:1] * paired[:, :, 0]
        + gate_pair[..., 1:2] * paired[:, :, 1]
    )
    combined = jnp.where(live_rows[..., None], combined, 0.0).astype(jnp.bfloat16)
    return combined.reshape(batches, req_count, seq_len, col_width)


def solution(mesh):
    in_specs = (
        P(None, "dp", None, "expert"),
        P(),
        P(),
        P(None, "dp", None, None),
        P(None, "dp", None, None),
        P(None, "dp", None, None),
        P(),
        P(),
        P(),
        P(),
        P(),
        P(None, None, "expert", None),
        P(None, None, "expert", None),
        P(None, "expert", None, None),
        P(),
        P(None, "dp", None, "expert"),
    )
    out_specs = P(None, "dp", None, "expert")
    return jax.shard_map(
        per_device, mesh=mesh, in_specs=in_specs, out_specs=out_specs, check_vma=False
    )
```

```python
import math

import jax
import jax.numpy as jnp
from jax import lax
from jax.sharding import PartitionSpec as P

FEXP = 8
TOPK = 2
SLOTS = 16
CAP = 12


EPS = 1e-06
ROPE_BASE = 10000.0


def rope_tables(seq_len, head_width):
    half_width = head_width // 2
    frequency = ROPE_BASE ** (-(jnp.arange(half_width, dtype=jnp.float32) * 2.0 / head_width))
    angles = jnp.arange(seq_len, dtype=jnp.float32)[:, None] * frequency[None, :]
    return (jnp.cos(angles), jnp.sin(angles))


def rope_apply(values, cosine, sine_table, along_axis):
    half_width = values.shape[-1] // 2
    tile_shape = [1] * values.ndim
    tile_shape[along_axis] = cosine.shape[0]
    tile_shape[-1] = half_width
    cos_part = cosine.reshape(tile_shape)
    sin_part = sine_table.reshape(tile_shape)
    front_half = values[..., :half_width]
    back_half = values[..., half_width:]
    return jnp.concatenate(
        [
            front_half * cos_part - back_half * sin_part,
            back_half * cos_part + front_half * sin_part,
        ],
        axis=-1,
    )


def rms_norm(rows, gain_vec):
    widened = rows.astype(jnp.float32)
    inv_rms = lax.rsqrt(jnp.mean(widened * widened, axis=-1, keepdims=True) + EPS)
    return (widened * inv_rms * gain_vec).astype(jnp.bfloat16)


def pair_gates(logits, routes):
    picked = jnp.take_along_axis(logits, routes, axis=-1)
    leading = jax.nn.sigmoid(picked[..., 0] - picked[..., 1])
    return jnp.stack([leading, 1.0 - leading], axis=-1)


def slot_targets(placement, expert_ids, replica_ids, live_rows):
    slot_range = jnp.arange(SLOTS, dtype=jnp.int32)
    same_expert = placement[:, None] == placement[None, :]
    earlier = slot_range[:, None] > slot_range[None, :]
    occurrence = jnp.sum((same_expert & earlier).astype(jnp.int32), axis=1)
    hosting = (placement[None, :] == jnp.arange(FEXP, dtype=jnp.int32)[:, None]).astype(jnp.int32)
    copies_all = jnp.sum(hosting, axis=1)
    chosen = (expert_ids[:, None] == jnp.arange(FEXP, dtype=jnp.int32)[None, :]).astype(jnp.int32)
    copies = jnp.sum(chosen * copies_all[None, :], axis=1)
    replica = replica_ids % copies
    slot_hits = (
        (placement[None, :] == expert_ids[:, None])
        & (occurrence[None, :] == replica[:, None])
        & live_rows[:, None]
    )
    slot_hits = slot_hits.astype(jnp.int32)
    before = jnp.cumsum(slot_hits, axis=0) - slot_hits
    ranking = jnp.sum(before * slot_hits, axis=1)
    slot_ids = jnp.sum(slot_hits * slot_range[None, :], axis=1)
    within_cap = (jnp.sum(slot_hits, axis=1) > 0) & (ranking < CAP)
    return jnp.where(within_cap, slot_ids * CAP + ranking, SLOTS * CAP)


def fill_buffer(rows, target):
    positions = jnp.arange(SLOTS * CAP, dtype=jnp.int32)
    hits = (target[None, :] == positions[:, None]).reshape(SLOTS * CAP, -1, TOPK).any(axis=2)
    buffer = jnp.dot(hits.astype(rows.dtype), rows, preferred_element_type=jnp.float32)
    return buffer.astype(rows.dtype).reshape(SLOTS, CAP, rows.shape[1])


def collect(results, target):
    flat_rows = results.reshape(SLOTS * CAP, results.shape[-1])
    positions = jnp.arange(SLOTS * CAP, dtype=jnp.int32)
    hits = (target[:, None] == positions[None, :]).astype(flat_rows.dtype)
    return jnp.dot(hits, flat_rows, preferred_element_type=jnp.float32)


def load_weights(stored, placement):
    dp_groups = lax.axis_size("dp")
    per = SLOTS // dp_groups
    me = lax.axis_index("dp")
    pieces = []
    for shift in range(dp_groups):
        partner = me ^ shift
        ids = lax.dynamic_slice_in_dim(placement, partner * per, per)
        piece = jnp.take(stored, ids, axis=0)
        if shift:
            pairs = [(i, i ^ shift) for i in range(dp_groups)]
            piece = lax.ppermute(piece, "dp", pairs)
        pieces.append(piece)
    return jnp.stack(pieces, axis=1)


def block_order(rows, axis):
    dp_groups = lax.axis_size("dp")
    me = lax.axis_index("dp")
    shape = rows.shape
    split = shape[:axis] + (dp_groups, shape[axis] // dp_groups) + shape[axis + 1 :]
    order = me ^ jnp.arange(dp_groups, dtype=jnp.int32)
    return jnp.take(rows.reshape(split), order, axis=axis).reshape(shape)


def expert_terms(slot_items, loaded):
    per, groups, block, _, cols = loaded.shape
    weights_here = loaded.reshape(per, groups * block, 3, cols)
    slot_items = block_order(slot_items, 3)
    gate_proj = jnp.einsum(
        "gjcd,jdf->gjcf", slot_items, weights_here[:, :, 0, :], preferred_element_type=jnp.float32
    )
    up_proj = jnp.einsum(
        "gjcd,jdf->gjcf", slot_items, weights_here[:, :, 1, :], preferred_element_type=jnp.float32
    )
    hidden = (jax.nn.silu(gate_proj) * up_proj).astype(jnp.bfloat16)
    terms = jnp.einsum(
        "gjcf,jdf->gjcd", hidden, weights_here[:, :, 2, :], preferred_element_type=jnp.float32
    )
    return block_order(terms.astype(jnp.bfloat16), 3)


def ffn_stationary(normed_rows, target, placement, chosen, col_width):
    dp_groups = lax.axis_size("dp")
    ex_groups = lax.axis_size("expert")
    me_dp = lax.axis_index("dp")
    model_width = normed_rows.shape[1]
    block = model_width // dp_groups
    ratio = dp_groups // ex_groups
    full = fill_buffer(normed_rows, target)
    blocks = full.reshape(SLOTS, CAP, dp_groups, block).transpose(2, 0, 1, 3)
    rows_here = lax.all_to_all(blocks, "dp", split_axis=0, concat_axis=0, tiled=True)
    partial = jnp.einsum(
        "gscd,sdkf->gsckf", rows_here, chosen[:, :, 0:2, :], preferred_element_type=jnp.float32
    ).astype(jnp.bfloat16)
    summed = lax.psum_scatter(partial, "dp", scatter_dimension=1, tiled=True).astype(jnp.float32)
    hidden = (jax.nn.silu(summed[..., 0, :]) * summed[..., 1, :]).astype(jnp.bfloat16)
    hidden_all = lax.all_gather(hidden, "dp", axis=1, tiled=True)
    terms = jnp.einsum(
        "gscf,sdf->gscd", hidden_all, chosen[:, :, 2, :], preferred_element_type=jnp.float32
    ).astype(jnp.bfloat16)
    reduced = lax.psum_scatter(terms, "expert", scatter_dimension=0, tiled=True)
    pieces = []
    for part in range(ratio):
        got = None
        for lead in range(ratio):
            pairs = []
            for src_dp in range(dp_groups):
                if src_dp % ratio != part:
                    continue
                for src_ex in range(ex_groups):
                    dst = (ratio * src_ex + lead) * ex_groups + src_dp // ratio
                    pairs.append((src_dp * ex_groups + src_ex, dst))
            moved = lax.ppermute(reduced[lead], ("dp", "expert"), pairs)
            moved = jnp.where(me_dp % ratio == lead, moved, jnp.zeros_like(moved))
            got = moved if got is None else got + moved
        pieces.append(got)
    cols = jnp.concatenate(pieces, axis=-1)
    return collect(cols.reshape(SLOTS * CAP, col_width), target)


def attend(
    hidden_cols,
    lens_here,
    routes,
    gain_vec,
    router,
    query_flat,
    key_value_flat,
    output_flat,
    cosine,
    sine_table,
    placement,
    stored,
):
    full_rows = hidden_cols
    req_count, seq_len, model_width = full_rows.shape
    token_count = req_count * seq_len
    expert_count = router.shape[1]
    head_width = cosine.shape[1] * 2
    normed = rms_norm(full_rows.reshape(token_count, model_width), gain_vec)
    logits = jnp.dot(normed, router, preferred_element_type=jnp.float32)
    gate_pair = pair_gates(logits, routes)
    every_query = jnp.einsum(
        "td,dehk->tehk", normed, query_flat, preferred_element_type=jnp.float32
    )
    queries = jnp.take_along_axis(every_query, routes[:, :, None, None], axis=1)
    queries = rope_apply(
        queries.reshape(req_count, seq_len, 2, -1, head_width), cosine, sine_table, 1
    ).astype(jnp.bfloat16)
    key_value = jnp.einsum(
        "td,dchk->tchk", normed, key_value_flat, preferred_element_type=jnp.float32
    ).reshape(req_count, seq_len, 2, -1, head_width)
    key_rows = rope_apply(key_value[:, :, 0], cosine, sine_table, 1).astype(jnp.bfloat16)
    values = key_value[:, :, 1].astype(jnp.bfloat16)
    scores = jnp.einsum(
        "rtkhd,ruhd->rkhtu", queries, key_rows, preferred_element_type=jnp.float32
    ) / math.sqrt(head_width)
    positions = jnp.arange(seq_len, dtype=jnp.int32)
    allowed = (positions[None, None, :] <= positions[None, :, None]) & (
        positions[None, None, :] < lens_here[:, None, None]
    )
    raised = jnp.where(allowed[:, None, None], jnp.exp(scores), 0.0)
    probability = (raised / jnp.sum(raised, axis=-1, keepdims=True)).astype(jnp.bfloat16)
    head_out = jnp.einsum(
        "rkhtu,ruhd->rtkhd", probability, values, preferred_element_type=jnp.float32
    )
    head_out = head_out.reshape(token_count, 2, -1, head_width)
    expert_hits = (
        routes[:, :, None] == jnp.arange(expert_count, dtype=jnp.int32)[None, None, :]
    ).astype(jnp.float32) * gate_pair[:, :, None]
    mixed_heads = jnp.einsum(
        "tke,tkhd->tehd", expert_hits, head_out, precision=lax.Precision.HIGHEST
    ).astype(jnp.bfloat16)
    partial_value = jnp.dot(
        mixed_heads.reshape(token_count, -1), output_flat, preferred_element_type=jnp.float32
    )
    partial_value, placement = lax.optimization_barrier(
        (partial_value.astype(jnp.bfloat16), placement)
    )
    attn_full = lax.psum(partial_value, "expert").astype(jnp.float32)
    chosen = stored.at[placement].get(mode="promise_in_bounds")
    residual = (full_rows.reshape(token_count, -1).astype(jnp.float32) + attn_full).astype(
        jnp.bfloat16
    )
    return residual, chosen


def per_device(
    hidden_in,
    request_order,
    request_lengths,
    attention_routes,
    expert_routes,
    replica_picks,
    old_slots,
    new_slots,
    norm_gain_att,
    norm_gain_ffn,
    att_router,
    query_weight,
    key_value_weight,
    output_weight,
    ffn_router,
    expert_weights,
):
    req_count = hidden_in.shape[1]
    seq_len = hidden_in.shape[2]
    col_width = hidden_in.shape[3]
    model_width = norm_gain_att.shape[0]
    token_count = req_count * seq_len
    dp_groups = lax.axis_size("dp")
    slots_here = SLOTS // dp_groups
    head_width = query_weight.shape[3]
    cosine, sine_table = rope_tables(seq_len, head_width)
    query_flat = query_weight
    key_value_flat = key_value_weight
    output_flat = output_weight.reshape(-1, model_width)
    column_start = lax.axis_index("expert") * col_width
    placements = jnp.stack([old_slots, new_slots])
    lens_all = jnp.take_along_axis(request_lengths, request_order, axis=1)
    lens_here = lax.dynamic_slice_in_dim(lens_all, lax.axis_index("dp") * req_count, req_count, 1)

    def one_batch(hidden_b, lens_b, att_b, ffn_b, picks_b, placement):
        live_rows = (jnp.arange(seq_len, dtype=jnp.int32)[None, :] < lens_b[:, None]).reshape(
            token_count
        )
        att_pairs = att_b.reshape(token_count, 2)
        full_rows = lax.all_gather(hidden_b, "expert", axis=2, tiled=True)
        residual_full, chosen = attend(
            full_rows,
            lens_b,
            att_pairs,
            norm_gain_att,
            att_router,
            query_flat,
            key_value_flat,
            output_flat,
            cosine,
            sine_table,
            placement,
            expert_weights,
        )
        ffn_pairs = ffn_b.reshape(token_count, 2)
        routes_flat = ffn_pairs.reshape(-1)
        picks_flat = picks_b.reshape(-1)
        live_assign = jnp.repeat(live_rows, 2)
        target = slot_targets(placement, routes_flat, picks_flat, live_assign)
        normed_rows = rms_norm(residual_full, norm_gain_ffn)
        logits = jnp.dot(normed_rows, ffn_router, preferred_element_type=jnp.float32)
        residual = lax.dynamic_slice_in_dim(residual_full, column_start, col_width, 1)
        gate_pair = pair_gates(logits, ffn_pairs)
        expert_out = ffn_stationary(normed_rows, target, placement, chosen, col_width).astype(
            jnp.float32
        )
        paired = expert_out.reshape(token_count, 2, col_width)
        combined = (
            residual.astype(jnp.float32)
            + gate_pair[:, 0:1] * paired[:, 0]
            + gate_pair[:, 1:2] * paired[:, 1]
        )
        combined = jnp.where(live_rows[:, None], combined, 0.0).astype(jnp.bfloat16)
        return combined.reshape(req_count, seq_len, col_width)

    return jax.vmap(one_batch)(
        hidden_in, lens_here, attention_routes, expert_routes, replica_picks, placements
    )


def solution(mesh):
    in_specs = (
        P(None, "dp", None, "expert"),
        P(),
        P(),
        P(None, "dp", None, None),
        P(None, "dp", None, None),
        P(None, "dp", None, None),
        P(),
        P(),
        P(),
        P(),
        P(),
        P(None, None, "expert", None),
        P(None, None, "expert", None),
        P(None, "expert", None, None),
        P(),
        P(None, "dp", None, "expert"),
    )
    out_specs = P(None, "dp", None, "expert")
    return jax.shard_map(
        per_device, mesh=mesh, in_specs=in_specs, out_specs=out_specs, check_vma=False
    )
```

```python
import math

import jax
import jax.numpy as jnp
from jax import lax
from jax.sharding import PartitionSpec as P

FEXP = 8
TOPK = 2
SLOTS = 16
CAP = 12


EPS = 1e-06
ROPE_BASE = 10000.0


def rope_tables(seq_len, head_width):
    half_width = head_width // 2
    frequency = ROPE_BASE ** (-(jnp.arange(half_width, dtype=jnp.float32) * 2.0 / head_width))
    angles = jnp.arange(seq_len, dtype=jnp.float32)[:, None] * frequency[None, :]
    return (jnp.cos(angles), jnp.sin(angles))


def rope_apply(values, cosine, sine_table, along_axis):
    half_width = values.shape[-1] // 2
    tile_shape = [1] * values.ndim
    tile_shape[along_axis] = cosine.shape[0]
    tile_shape[-1] = half_width
    cos_part = cosine.reshape(tile_shape)
    sin_part = sine_table.reshape(tile_shape)
    front_half = values[..., :half_width]
    back_half = values[..., half_width:]
    return jnp.concatenate(
        [
            front_half * cos_part - back_half * sin_part,
            back_half * cos_part + front_half * sin_part,
        ],
        axis=-1,
    )


def rms_norm(rows, gain_vec):
    widened = rows.astype(jnp.float32)
    inv_rms = lax.rsqrt(jnp.mean(widened * widened, axis=-1, keepdims=True) + EPS)
    return (widened * inv_rms * gain_vec).astype(jnp.bfloat16)


def pair_gates(logits, routes):
    picked = jnp.take_along_axis(logits, routes, axis=-1)
    leading = jax.nn.sigmoid(picked[..., 0] - picked[..., 1])
    return jnp.stack([leading, 1.0 - leading], axis=-1)


def slot_targets(placement, expert_ids, replica_ids, live_rows):
    slot_range = jnp.arange(SLOTS, dtype=jnp.int32)
    same_expert = placement[:, None] == placement[None, :]
    earlier = slot_range[:, None] > slot_range[None, :]
    occurrence = jnp.sum((same_expert & earlier).astype(jnp.int32), axis=1)
    hosting = (placement[None, :] == jnp.arange(FEXP, dtype=jnp.int32)[:, None]).astype(jnp.int32)
    copies_all = jnp.sum(hosting, axis=1)
    chosen = (expert_ids[:, None] == jnp.arange(FEXP, dtype=jnp.int32)[None, :]).astype(jnp.int32)
    copies = jnp.sum(chosen * copies_all[None, :], axis=1)
    replica = replica_ids % copies
    slot_hits = (
        (placement[None, :] == expert_ids[:, None])
        & (occurrence[None, :] == replica[:, None])
        & live_rows[:, None]
    )
    slot_hits = slot_hits.astype(jnp.int32)
    before = jnp.cumsum(slot_hits, axis=0) - slot_hits
    ranking = jnp.sum(before * slot_hits, axis=1)
    slot_ids = jnp.sum(slot_hits * slot_range[None, :], axis=1)
    within_cap = (jnp.sum(slot_hits, axis=1) > 0) & (ranking < CAP)
    return jnp.where(within_cap, slot_ids * CAP + ranking, SLOTS * CAP)


def fill_buffer(rows, target):
    positions = jnp.arange(SLOTS * CAP, dtype=jnp.int32)
    hits = (target[None, :] == positions[:, None]).reshape(SLOTS * CAP, -1, TOPK).any(axis=2)
    buffer = jnp.dot(hits.astype(rows.dtype), rows, preferred_element_type=jnp.float32)
    return buffer.astype(rows.dtype).reshape(SLOTS, CAP, rows.shape[1])


def collect(results, target):
    flat_rows = results.reshape(SLOTS * CAP, results.shape[-1])
    positions = jnp.arange(SLOTS * CAP, dtype=jnp.int32)
    hits = (target[:, None] == positions[None, :]).astype(flat_rows.dtype)
    return jnp.dot(hits, flat_rows, preferred_element_type=jnp.float32)


def load_weights(stored, placement):
    dp_groups = lax.axis_size("dp")
    per = SLOTS // dp_groups
    me = lax.axis_index("dp")
    pieces = []
    for shift in range(dp_groups):
        partner = me ^ shift
        ids = lax.dynamic_slice_in_dim(placement, partner * per, per)
        piece = jnp.take(stored, ids, axis=0)
        if shift:
            pairs = [(i, i ^ shift) for i in range(dp_groups)]
            piece = lax.ppermute(piece, "dp", pairs)
        pieces.append(piece)
    return jnp.stack(pieces, axis=1)


def block_order(rows, axis):
    dp_groups = lax.axis_size("dp")
    me = lax.axis_index("dp")
    shape = rows.shape
    split = shape[:axis] + (dp_groups, shape[axis] // dp_groups) + shape[axis + 1 :]
    order = me ^ jnp.arange(dp_groups, dtype=jnp.int32)
    return jnp.take(rows.reshape(split), order, axis=axis).reshape(shape)


def expert_terms(slot_items, loaded):
    per, groups, block, _, cols = loaded.shape
    weights_here = loaded.reshape(per, groups * block, 3, cols)
    slot_items = block_order(slot_items, 3)
    gate_proj = jnp.einsum(
        "gjcd,jdf->gjcf", slot_items, weights_here[:, :, 0, :], preferred_element_type=jnp.float32
    )
    up_proj = jnp.einsum(
        "gjcd,jdf->gjcf", slot_items, weights_here[:, :, 1, :], preferred_element_type=jnp.float32
    )
    hidden = (jax.nn.silu(gate_proj) * up_proj).astype(jnp.bfloat16)
    terms = jnp.einsum(
        "gjcf,jdf->gjcd", hidden, weights_here[:, :, 2, :], preferred_element_type=jnp.float32
    )
    return block_order(terms.astype(jnp.bfloat16), 3)


def ffn_stationary(normed_rows, target, placement, chosen, col_width):
    dp_groups = lax.axis_size("dp")
    ex_groups = lax.axis_size("expert")
    me_dp = lax.axis_index("dp")
    model_width = normed_rows.shape[1]
    block = model_width // dp_groups
    ratio = dp_groups // ex_groups
    full = fill_buffer(normed_rows, target)
    blocks = full.reshape(SLOTS, CAP, dp_groups, block).transpose(2, 0, 1, 3)
    rows_here = lax.all_to_all(blocks, "dp", split_axis=0, concat_axis=0, tiled=True)
    partial = jnp.einsum(
        "gscd,sdkf->gsckf", rows_here, chosen[:, :, 0:2, :], preferred_element_type=jnp.float32
    ).astype(jnp.bfloat16)
    summed = lax.psum_scatter(partial, "dp", scatter_dimension=1, tiled=True).astype(jnp.float32)
    hidden = (jax.nn.silu(summed[..., 0, :]) * summed[..., 1, :]).astype(jnp.bfloat16)
    hidden_all = lax.all_gather(hidden, "dp", axis=1, tiled=True)
    terms = jnp.einsum(
        "gscf,sdf->gscd", hidden_all, chosen[:, :, 2, :], preferred_element_type=jnp.float32
    ).astype(jnp.bfloat16)
    reduced = lax.psum_scatter(terms, "expert", scatter_dimension=0, tiled=True)
    pieces = []
    for part in range(ratio):
        got = None
        for lead in range(ratio):
            pairs = []
            for src_dp in range(dp_groups):
                if src_dp % ratio != part:
                    continue
                for src_ex in range(ex_groups):
                    dst = (ratio * src_ex + lead) * ex_groups + src_dp // ratio
                    pairs.append((src_dp * ex_groups + src_ex, dst))
            moved = lax.ppermute(reduced[lead], ("dp", "expert"), pairs)
            moved = jnp.where(me_dp % ratio == lead, moved, jnp.zeros_like(moved))
            got = moved if got is None else got + moved
        pieces.append(got)
    cols = jnp.concatenate(pieces, axis=-1)
    return collect(cols.reshape(SLOTS * CAP, col_width), target)


def attend(
    hidden_cols,
    lens_here,
    routes,
    gain_vec,
    router,
    query_flat,
    key_value_flat,
    output_flat,
    cosine,
    sine_table,
    placement,
    stored,
):
    full_rows = hidden_cols
    req_count, seq_len, model_width = full_rows.shape
    token_count = req_count * seq_len
    expert_count = router.shape[1]
    head_width = cosine.shape[1] * 2
    normed = rms_norm(full_rows.reshape(token_count, model_width), gain_vec)
    logits = jnp.dot(normed, router, preferred_element_type=jnp.float32)
    gate_pair = pair_gates(logits, routes)
    every_query = jnp.einsum(
        "td,dehk->tehk", normed, query_flat, preferred_element_type=jnp.float32
    )
    queries = jnp.take_along_axis(every_query, routes[:, :, None, None], axis=1)
    queries = rope_apply(
        queries.reshape(req_count, seq_len, 2, -1, head_width), cosine, sine_table, 1
    ).astype(jnp.bfloat16)
    key_value = jnp.einsum(
        "td,dchk->tchk", normed, key_value_flat, preferred_element_type=jnp.float32
    ).reshape(req_count, seq_len, 2, -1, head_width)
    key_rows = rope_apply(key_value[:, :, 0], cosine, sine_table, 1).astype(jnp.bfloat16)
    values = key_value[:, :, 1].astype(jnp.bfloat16)
    scores = jnp.einsum(
        "rtkhd,ruhd->rkhtu", queries, key_rows, preferred_element_type=jnp.float32
    ) / math.sqrt(head_width)
    positions = jnp.arange(seq_len, dtype=jnp.int32)
    allowed = (positions[None, None, :] <= positions[None, :, None]) & (
        positions[None, None, :] < lens_here[:, None, None]
    )
    raised = jnp.where(allowed[:, None, None], jnp.exp(scores), 0.0)
    probability = (raised / jnp.sum(raised, axis=-1, keepdims=True)).astype(jnp.bfloat16)
    head_out = jnp.einsum(
        "rkhtu,ruhd->rtkhd", probability, values, preferred_element_type=jnp.float32
    )
    head_out = head_out.reshape(token_count, 2, -1, head_width)
    expert_hits = (
        routes[:, :, None] == jnp.arange(expert_count, dtype=jnp.int32)[None, None, :]
    ).astype(jnp.float32) * gate_pair[:, :, None]
    mixed_heads = jnp.einsum(
        "tke,tkhd->tehd", expert_hits, head_out, precision=lax.Precision.HIGHEST
    ).astype(jnp.bfloat16)
    partial_value = jnp.dot(
        mixed_heads.reshape(token_count, -1), output_flat, preferred_element_type=jnp.float32
    )
    partial_value, placement = lax.optimization_barrier(
        (partial_value.astype(jnp.bfloat16), placement)
    )
    attn_full = lax.psum(partial_value, "expert").astype(jnp.float32)
    chosen = stored.at[placement].get(mode="promise_in_bounds")
    residual = (full_rows.reshape(token_count, -1).astype(jnp.float32) + attn_full).astype(
        jnp.bfloat16
    )
    return residual, chosen


def per_device(
    hidden_in,
    request_order,
    request_lengths,
    attention_routes,
    expert_routes,
    replica_picks,
    old_slots,
    new_slots,
    norm_gain_att,
    norm_gain_ffn,
    att_router,
    query_weight,
    key_value_weight,
    output_weight,
    ffn_router,
    expert_weights,
):
    req_count = hidden_in.shape[1]
    seq_len = hidden_in.shape[2]
    col_width = hidden_in.shape[3]
    model_width = norm_gain_att.shape[0]
    token_count = req_count * seq_len
    dp_groups = lax.axis_size("dp")
    slots_here = SLOTS // dp_groups
    head_width = query_weight.shape[3]
    cosine, sine_table = rope_tables(seq_len, head_width)
    query_flat = query_weight
    key_value_flat = key_value_weight
    output_flat = output_weight.reshape(-1, model_width)
    column_start = lax.axis_index("expert") * col_width
    placements = jnp.stack([old_slots, new_slots])
    lens_all = jnp.take_along_axis(request_lengths, request_order, axis=1)
    lens_here = lax.dynamic_slice_in_dim(lens_all, lax.axis_index("dp") * req_count, req_count, 1)

    def one_batch(hidden_b, lens_b, att_b, ffn_b, picks_b, placement):
        live_rows = (jnp.arange(seq_len, dtype=jnp.int32)[None, :] < lens_b[:, None]).reshape(
            token_count
        )
        att_pairs = att_b.reshape(token_count, 2)
        full_rows = lax.all_gather(hidden_b, "expert", axis=2, tiled=True)
        residual_full, chosen = attend(
            full_rows,
            lens_b,
            att_pairs,
            norm_gain_att,
            att_router,
            query_flat,
            key_value_flat,
            output_flat,
            cosine,
            sine_table,
            placement,
            expert_weights,
        )
        ffn_pairs = ffn_b.reshape(token_count, 2)
        routes_flat = ffn_pairs.reshape(-1)
        picks_flat = picks_b.reshape(-1)
        live_assign = jnp.repeat(live_rows, 2)
        target = slot_targets(placement, routes_flat, picks_flat, live_assign)
        normed_rows = rms_norm(residual_full, norm_gain_ffn)
        logits = jnp.dot(normed_rows, ffn_router, preferred_element_type=jnp.float32)
        residual = lax.dynamic_slice_in_dim(residual_full, column_start, col_width, 1)
        gate_pair = pair_gates(logits, ffn_pairs)
        return residual, normed_rows, target, chosen, gate_pair, live_rows

    residual, normed_rows, target, chosen, gate_pair, live_rows = jax.vmap(one_batch)(
        hidden_in, lens_here, attention_routes, expert_routes, replica_picks, placements
    )
    results = []
    for batch_index in range(hidden_in.shape[0]):
        expert_out = ffn_stationary(
            normed_rows[batch_index],
            target[batch_index],
            placements[batch_index],
            chosen[batch_index],
            col_width,
        ).astype(jnp.float32)
        paired = expert_out.reshape(token_count, 2, col_width)
        gates = gate_pair[batch_index]
        combined = (
            residual[batch_index].astype(jnp.float32)
            + gates[:, 0:1] * paired[:, 0]
            + gates[:, 1:2] * paired[:, 1]
        )
        combined = jnp.where(live_rows[batch_index][:, None], combined, 0.0)
        results.append(combined.astype(jnp.bfloat16).reshape(req_count, seq_len, col_width))
    return jnp.stack(results, axis=0)


def solution(mesh):
    in_specs = (
        P(None, "dp", None, "expert"),
        P(),
        P(),
        P(None, "dp", None, None),
        P(None, "dp", None, None),
        P(None, "dp", None, None),
        P(),
        P(),
        P(),
        P(),
        P(),
        P(None, None, "expert", None),
        P(None, None, "expert", None),
        P(None, "expert", None, None),
        P(),
        P(None, "dp", None, "expert"),
    )
    out_specs = P(None, "dp", None, "expert")
    return jax.shard_map(
        per_device, mesh=mesh, in_specs=in_specs, out_specs=out_specs, check_vma=False
    )
```

```python
import math

import jax
import jax.numpy as jnp
from jax import lax
from jax.sharding import PartitionSpec as P

FEXP = 8
TOPK = 2
SLOTS = 16
CAP = 12


EPS = 1e-06
ROPE_BASE = 10000.0


def rope_tables(seq_len, head_width):
    half_width = head_width // 2
    frequency = ROPE_BASE ** (-(jnp.arange(half_width, dtype=jnp.float32) * 2.0 / head_width))
    angles = jnp.arange(seq_len, dtype=jnp.float32)[:, None] * frequency[None, :]
    return (jnp.cos(angles), jnp.sin(angles))


def rope_apply(values, cosine, sine_table, along_axis):
    half_width = values.shape[-1] // 2
    tile_shape = [1] * values.ndim
    tile_shape[along_axis] = cosine.shape[0]
    tile_shape[-1] = half_width
    cos_part = cosine.reshape(tile_shape)
    sin_part = sine_table.reshape(tile_shape)
    front_half = values[..., :half_width]
    back_half = values[..., half_width:]
    return jnp.concatenate(
        [
            front_half * cos_part - back_half * sin_part,
            back_half * cos_part + front_half * sin_part,
        ],
        axis=-1,
    )


def rms_norm(rows, gain_vec):
    widened = rows.astype(jnp.float32)
    inv_rms = lax.rsqrt(jnp.mean(widened * widened, axis=-1, keepdims=True) + EPS)
    return (widened * inv_rms * gain_vec).astype(jnp.bfloat16)


def pair_gates(logits, routes):
    picked = jnp.take_along_axis(logits, routes, axis=-1)
    leading = jax.nn.sigmoid(picked[..., 0] - picked[..., 1])
    return jnp.stack([leading, 1.0 - leading], axis=-1)


def slot_targets(placement, expert_ids, replica_ids, live_rows):
    slot_range = jnp.arange(SLOTS, dtype=jnp.int32)
    same_expert = placement[:, None] == placement[None, :]
    earlier = slot_range[:, None] > slot_range[None, :]
    occurrence = jnp.sum((same_expert & earlier).astype(jnp.int32), axis=1)
    hosting = (placement[None, :] == jnp.arange(FEXP, dtype=jnp.int32)[:, None]).astype(jnp.int32)
    copies_all = jnp.sum(hosting, axis=1)
    chosen = (expert_ids[:, None] == jnp.arange(FEXP, dtype=jnp.int32)[None, :]).astype(jnp.int32)
    copies = jnp.sum(chosen * copies_all[None, :], axis=1)
    replica = replica_ids % copies
    slot_hits = (
        (placement[None, :] == expert_ids[:, None])
        & (occurrence[None, :] == replica[:, None])
        & live_rows[:, None]
    )
    slot_hits = slot_hits.astype(jnp.int32)
    before = jnp.cumsum(slot_hits, axis=0) - slot_hits
    ranking = jnp.sum(before * slot_hits, axis=1)
    slot_ids = jnp.sum(slot_hits * slot_range[None, :], axis=1)
    within_cap = (jnp.sum(slot_hits, axis=1) > 0) & (ranking < CAP)
    return jnp.where(within_cap, slot_ids * CAP + ranking, SLOTS * CAP)


def fill_buffer(rows, target):
    positions = jnp.arange(SLOTS * CAP, dtype=jnp.int32)
    hits = (target[None, :] == positions[:, None]).reshape(SLOTS * CAP, -1, TOPK).any(axis=2)
    buffer = jnp.dot(hits.astype(rows.dtype), rows, preferred_element_type=jnp.float32)
    return buffer.astype(rows.dtype).reshape(SLOTS, CAP, rows.shape[1])


def collect(results, target):
    flat_rows = results.reshape(SLOTS * CAP, results.shape[-1])
    positions = jnp.arange(SLOTS * CAP, dtype=jnp.int32)
    hits = (target[:, None] == positions[None, :]).astype(flat_rows.dtype)
    return jnp.dot(hits, flat_rows, preferred_element_type=jnp.float32)


def load_weights(stored, placement):
    dp_groups = lax.axis_size("dp")
    per = SLOTS // dp_groups
    me = lax.axis_index("dp")
    pieces = []
    for shift in range(dp_groups):
        partner = me ^ shift
        ids = lax.dynamic_slice_in_dim(placement, partner * per, per)
        piece = jnp.take(stored, ids, axis=0)
        if shift:
            pairs = [(i, i ^ shift) for i in range(dp_groups)]
            piece = lax.ppermute(piece, "dp", pairs)
        pieces.append(piece)
    return jnp.stack(pieces, axis=1)


def block_order(rows, axis):
    dp_groups = lax.axis_size("dp")
    me = lax.axis_index("dp")
    shape = rows.shape
    split = shape[:axis] + (dp_groups, shape[axis] // dp_groups) + shape[axis + 1 :]
    order = me ^ jnp.arange(dp_groups, dtype=jnp.int32)
    return jnp.take(rows.reshape(split), order, axis=axis).reshape(shape)


def expert_terms(slot_items, loaded):
    per, groups, block, _, cols = loaded.shape
    weights_here = loaded.reshape(per, groups * block, 3, cols)
    slot_items = block_order(slot_items, 3)
    gate_proj = jnp.einsum(
        "gjcd,jdf->gjcf", slot_items, weights_here[:, :, 0, :], preferred_element_type=jnp.float32
    )
    up_proj = jnp.einsum(
        "gjcd,jdf->gjcf", slot_items, weights_here[:, :, 1, :], preferred_element_type=jnp.float32
    )
    hidden = (jax.nn.silu(gate_proj) * up_proj).astype(jnp.bfloat16)
    terms = jnp.einsum(
        "gjcf,jdf->gjcd", hidden, weights_here[:, :, 2, :], preferred_element_type=jnp.float32
    )
    return block_order(terms.astype(jnp.bfloat16), 3)


def gather_slots(hidden):
    dp_groups = lax.axis_size("dp")
    me = lax.axis_index("dp")
    parity = me % 2
    half = me // 2
    chunks = [hidden]
    for shift in range(1, dp_groups // 2):
        chunks.append(lax.ppermute(hidden, "dp", [(i, i ^ (2 * shift)) for i in range(dp_groups)]))
    stacked = jnp.stack(chunks)
    by_half = jnp.take(stacked, half ^ jnp.arange(dp_groups // 2, dtype=jnp.int32), axis=0)
    other = lax.ppermute(by_half, "dp", [(i, i ^ 1) for i in range(dp_groups)])
    pair = jnp.where(
        parity == 0, jnp.stack([by_half, other], axis=1), jnp.stack([other, by_half], axis=1)
    )
    return pair.reshape((SLOTS,) + hidden.shape[1:])


def ffn_stationary(normed_rows, target, placement, chosen, col_width):
    dp_groups = lax.axis_size("dp")
    ex_groups = lax.axis_size("expert")
    me_dp = lax.axis_index("dp")
    model_width = normed_rows.shape[1]
    block = model_width // dp_groups
    ratio = dp_groups // ex_groups
    full = fill_buffer(normed_rows, target)
    blocks = full.reshape(SLOTS, CAP, dp_groups, block).transpose(2, 0, 1, 3)
    rows_here = lax.all_to_all(blocks, "dp", split_axis=0, concat_axis=0, tiled=True)
    partial = jnp.einsum(
        "gscd,sdkf->gsckf", rows_here, chosen[:, :, 0:2, :], preferred_element_type=jnp.float32
    ).astype(jnp.bfloat16)
    summed = lax.psum_scatter(partial, "dp", scatter_dimension=1, tiled=True).astype(jnp.float32)
    hidden = (jax.nn.silu(summed[..., 0, :]) * summed[..., 1, :]).astype(jnp.bfloat16)
    hidden_all = gather_slots(hidden.transpose(1, 0, 2, 3)).transpose(1, 0, 2, 3)
    terms = jnp.einsum(
        "gscf,sdf->gscd", hidden_all, chosen[:, :, 2, :], preferred_element_type=jnp.float32
    ).astype(jnp.bfloat16)
    reduced = lax.psum_scatter(terms, "expert", scatter_dimension=0, tiled=True)
    pieces = []
    for part in range(ratio):
        got = None
        for lead in range(ratio):
            pairs = []
            for src_dp in range(dp_groups):
                if src_dp % ratio != part:
                    continue
                for src_ex in range(ex_groups):
                    dst = (ratio * src_ex + lead) * ex_groups + src_dp // ratio
                    pairs.append((src_dp * ex_groups + src_ex, dst))
            moved = lax.ppermute(reduced[lead], ("dp", "expert"), pairs)
            moved = jnp.where(me_dp % ratio == lead, moved, jnp.zeros_like(moved))
            got = moved if got is None else got + moved
        pieces.append(got)
    cols = jnp.concatenate(pieces, axis=-1)
    return collect(cols.reshape(SLOTS * CAP, col_width), target)


def attend(
    hidden_cols,
    lens_here,
    routes,
    gain_vec,
    router,
    query_flat,
    key_value_flat,
    output_flat,
    cosine,
    sine_table,
    placement,
    stored,
):
    full_rows = hidden_cols
    req_count, seq_len, model_width = full_rows.shape
    token_count = req_count * seq_len
    expert_count = router.shape[1]
    head_width = cosine.shape[1] * 2
    normed = rms_norm(full_rows.reshape(token_count, model_width), gain_vec)
    logits = jnp.dot(normed, router, preferred_element_type=jnp.float32)
    gate_pair = pair_gates(logits, routes)
    every_query = jnp.einsum(
        "td,dehk->tehk", normed, query_flat, preferred_element_type=jnp.float32
    )
    queries = jnp.take_along_axis(every_query, routes[:, :, None, None], axis=1)
    queries = rope_apply(
        queries.reshape(req_count, seq_len, 2, -1, head_width), cosine, sine_table, 1
    ).astype(jnp.bfloat16)
    key_value = jnp.einsum(
        "td,dchk->tchk", normed, key_value_flat, preferred_element_type=jnp.float32
    ).reshape(req_count, seq_len, 2, -1, head_width)
    key_rows = rope_apply(key_value[:, :, 0], cosine, sine_table, 1).astype(jnp.bfloat16)
    values = key_value[:, :, 1].astype(jnp.bfloat16)
    scores = jnp.einsum(
        "rtkhd,ruhd->rkhtu", queries, key_rows, preferred_element_type=jnp.float32
    ) / math.sqrt(head_width)
    positions = jnp.arange(seq_len, dtype=jnp.int32)
    allowed = (positions[None, None, :] <= positions[None, :, None]) & (
        positions[None, None, :] < lens_here[:, None, None]
    )
    raised = jnp.where(allowed[:, None, None], jnp.exp(scores), 0.0)
    probability = (raised / jnp.sum(raised, axis=-1, keepdims=True)).astype(jnp.bfloat16)
    head_out = jnp.einsum(
        "rkhtu,ruhd->rtkhd", probability, values, preferred_element_type=jnp.float32
    )
    head_out = head_out.reshape(token_count, 2, -1, head_width)
    expert_hits = (
        routes[:, :, None] == jnp.arange(expert_count, dtype=jnp.int32)[None, None, :]
    ).astype(jnp.float32) * gate_pair[:, :, None]
    mixed_heads = jnp.einsum(
        "tke,tkhd->tehd", expert_hits, head_out, precision=lax.Precision.HIGHEST
    ).astype(jnp.bfloat16)
    partial_value = jnp.dot(
        mixed_heads.reshape(token_count, -1), output_flat, preferred_element_type=jnp.float32
    )
    partial_value, placement = lax.optimization_barrier(
        (partial_value.astype(jnp.bfloat16), placement)
    )
    attn_full = lax.psum(partial_value, "expert").astype(jnp.float32)
    chosen = stored.at[placement].get(mode="promise_in_bounds")
    residual = (full_rows.reshape(token_count, -1).astype(jnp.float32) + attn_full).astype(
        jnp.bfloat16
    )
    return residual, chosen


def per_device(
    hidden_in,
    request_order,
    request_lengths,
    attention_routes,
    expert_routes,
    replica_picks,
    old_slots,
    new_slots,
    norm_gain_att,
    norm_gain_ffn,
    att_router,
    query_weight,
    key_value_weight,
    output_weight,
    ffn_router,
    expert_weights,
):
    req_count = hidden_in.shape[1]
    seq_len = hidden_in.shape[2]
    col_width = hidden_in.shape[3]
    model_width = norm_gain_att.shape[0]
    token_count = req_count * seq_len
    dp_groups = lax.axis_size("dp")
    slots_here = SLOTS // dp_groups
    head_width = query_weight.shape[3]
    cosine, sine_table = rope_tables(seq_len, head_width)
    query_flat = query_weight
    key_value_flat = key_value_weight
    output_flat = output_weight.reshape(-1, model_width)
    column_start = lax.axis_index("expert") * col_width
    placements = jnp.stack([old_slots, new_slots])
    lens_all = jnp.take_along_axis(request_lengths, request_order, axis=1)
    lens_here = lax.dynamic_slice_in_dim(lens_all, lax.axis_index("dp") * req_count, req_count, 1)

    def one_batch(hidden_b, lens_b, att_b, ffn_b, picks_b, placement):
        live_rows = (jnp.arange(seq_len, dtype=jnp.int32)[None, :] < lens_b[:, None]).reshape(
            token_count
        )
        att_pairs = att_b.reshape(token_count, 2)
        full_rows = lax.all_gather(hidden_b, "expert", axis=2, tiled=True)
        residual_full, chosen = attend(
            full_rows,
            lens_b,
            att_pairs,
            norm_gain_att,
            att_router,
            query_flat,
            key_value_flat,
            output_flat,
            cosine,
            sine_table,
            placement,
            expert_weights,
        )
        ffn_pairs = ffn_b.reshape(token_count, 2)
        routes_flat = ffn_pairs.reshape(-1)
        picks_flat = picks_b.reshape(-1)
        live_assign = jnp.repeat(live_rows, 2)
        target = slot_targets(placement, routes_flat, picks_flat, live_assign)
        normed_rows = rms_norm(residual_full, norm_gain_ffn)
        logits = jnp.dot(normed_rows, ffn_router, preferred_element_type=jnp.float32)
        residual = lax.dynamic_slice_in_dim(residual_full, column_start, col_width, 1)
        gate_pair = pair_gates(logits, ffn_pairs)
        expert_out = ffn_stationary(normed_rows, target, placement, chosen, col_width).astype(
            jnp.float32
        )
        paired = expert_out.reshape(token_count, 2, col_width)
        combined = (
            residual.astype(jnp.float32)
            + gate_pair[:, 0:1] * paired[:, 0]
            + gate_pair[:, 1:2] * paired[:, 1]
        )
        combined = jnp.where(live_rows[:, None], combined, 0.0).astype(jnp.bfloat16)
        return combined.reshape(req_count, seq_len, col_width)

    return jax.vmap(one_batch)(
        hidden_in, lens_here, attention_routes, expert_routes, replica_picks, placements
    )


def solution(mesh):
    in_specs = (
        P(None, "dp", None, "expert"),
        P(),
        P(),
        P(None, "dp", None, None),
        P(None, "dp", None, None),
        P(None, "dp", None, None),
        P(),
        P(),
        P(),
        P(),
        P(),
        P(None, None, "expert", None),
        P(None, None, "expert", None),
        P(None, "expert", None, None),
        P(),
        P(None, "dp", None, "expert"),
    )
    out_specs = P(None, "dp", None, "expert")
    return jax.shard_map(
        per_device, mesh=mesh, in_specs=in_specs, out_specs=out_specs, check_vma=False
    )
```

```python
import math

import jax
import jax.numpy as jnp
from jax import lax
from jax.sharding import PartitionSpec as P

FEXP = 8
TOPK = 2
SLOTS = 16
CAP = 12


EPS = 1e-06
ROPE_BASE = 10000.0


def rope_tables(seq_len, head_width):
    half_width = head_width // 2
    frequency = ROPE_BASE ** (-(jnp.arange(half_width, dtype=jnp.float32) * 2.0 / head_width))
    angles = jnp.arange(seq_len, dtype=jnp.float32)[:, None] * frequency[None, :]
    return (jnp.cos(angles), jnp.sin(angles))


def rope_apply(values, cosine, sine_table, along_axis):
    half_width = values.shape[-1] // 2
    tile_shape = [1] * values.ndim
    tile_shape[along_axis] = cosine.shape[0]
    tile_shape[-1] = half_width
    cos_part = cosine.reshape(tile_shape)
    sin_part = sine_table.reshape(tile_shape)
    front_half = values[..., :half_width]
    back_half = values[..., half_width:]
    return jnp.concatenate(
        [
            front_half * cos_part - back_half * sin_part,
            back_half * cos_part + front_half * sin_part,
        ],
        axis=-1,
    )


def rms_norm(rows, gain_vec):
    widened = rows.astype(jnp.float32)
    inv_rms = lax.rsqrt(jnp.mean(widened * widened, axis=-1, keepdims=True) + EPS)
    return (widened * inv_rms * gain_vec).astype(jnp.bfloat16)


def pair_gates(logits, routes):
    picked = jnp.take_along_axis(logits, routes, axis=-1)
    leading = jax.nn.sigmoid(picked[..., 0] - picked[..., 1])
    return jnp.stack([leading, 1.0 - leading], axis=-1)


def slot_targets(placement, expert_ids, replica_ids, live_rows):
    slot_range = jnp.arange(SLOTS, dtype=jnp.int32)
    same_expert = placement[:, None] == placement[None, :]
    earlier = slot_range[:, None] > slot_range[None, :]
    occurrence = jnp.sum((same_expert & earlier).astype(jnp.int32), axis=1)
    hosting = (placement[None, :] == jnp.arange(FEXP, dtype=jnp.int32)[:, None]).astype(jnp.int32)
    copies_all = jnp.sum(hosting, axis=1)
    chosen = (expert_ids[:, None] == jnp.arange(FEXP, dtype=jnp.int32)[None, :]).astype(jnp.int32)
    copies = jnp.sum(chosen * copies_all[None, :], axis=1)
    replica = replica_ids % copies
    slot_hits = (
        (placement[None, :] == expert_ids[:, None])
        & (occurrence[None, :] == replica[:, None])
        & live_rows[:, None]
    )
    slot_hits = slot_hits.astype(jnp.int32)
    before = jnp.cumsum(slot_hits, axis=0) - slot_hits
    ranking = jnp.sum(before * slot_hits, axis=1)
    slot_ids = jnp.sum(slot_hits * slot_range[None, :], axis=1)
    within_cap = (jnp.sum(slot_hits, axis=1) > 0) & (ranking < CAP)
    return jnp.where(within_cap, slot_ids * CAP + ranking, SLOTS * CAP)


def fill_buffer(rows, target):
    positions = jnp.arange(SLOTS * CAP, dtype=jnp.int32)
    hits = (target[None, :] == positions[:, None]).reshape(SLOTS * CAP, -1, TOPK).any(axis=2)
    buffer = jnp.dot(hits.astype(rows.dtype), rows, preferred_element_type=jnp.float32)
    return buffer.astype(rows.dtype).reshape(SLOTS, CAP, rows.shape[1])


def collect(results, target):
    flat_rows = results.reshape(SLOTS * CAP, results.shape[-1])
    positions = jnp.arange(SLOTS * CAP, dtype=jnp.int32)
    hits = (target[:, None] == positions[None, :]).astype(flat_rows.dtype)
    return jnp.dot(hits, flat_rows, preferred_element_type=jnp.float32)


def load_weights(stored, placement):
    dp_groups = lax.axis_size("dp")
    per = SLOTS // dp_groups
    me = lax.axis_index("dp")
    pieces = []
    for shift in range(dp_groups):
        partner = me ^ shift
        ids = lax.dynamic_slice_in_dim(placement, partner * per, per)
        piece = jnp.take(stored, ids, axis=0)
        if shift:
            pairs = [(i, i ^ shift) for i in range(dp_groups)]
            piece = lax.ppermute(piece, "dp", pairs)
        pieces.append(piece)
    return jnp.stack(pieces, axis=1)


def block_order(rows, axis):
    dp_groups = lax.axis_size("dp")
    me = lax.axis_index("dp")
    shape = rows.shape
    split = shape[:axis] + (dp_groups, shape[axis] // dp_groups) + shape[axis + 1 :]
    order = me ^ jnp.arange(dp_groups, dtype=jnp.int32)
    return jnp.take(rows.reshape(split), order, axis=axis).reshape(shape)


def expert_terms(slot_items, loaded):
    per, groups, block, _, cols = loaded.shape
    weights_here = loaded.reshape(per, groups * block, 3, cols)
    slot_items = block_order(slot_items, 3)
    gate_proj = jnp.einsum(
        "gjcd,jdf->gjcf", slot_items, weights_here[:, :, 0, :], preferred_element_type=jnp.float32
    )
    up_proj = jnp.einsum(
        "gjcd,jdf->gjcf", slot_items, weights_here[:, :, 1, :], preferred_element_type=jnp.float32
    )
    hidden = (jax.nn.silu(gate_proj) * up_proj).astype(jnp.bfloat16)
    terms = jnp.einsum(
        "gjcf,jdf->gjcd", hidden, weights_here[:, :, 2, :], preferred_element_type=jnp.float32
    )
    return block_order(terms.astype(jnp.bfloat16), 3)


def gather_slots(hidden):
    dp_groups = lax.axis_size("dp")
    me = lax.axis_index("dp")
    parity = me % 2
    half = me // 2
    chunks = [hidden]
    for shift in range(1, dp_groups // 2):
        chunks.append(lax.ppermute(hidden, "dp", [(i, i ^ (2 * shift)) for i in range(dp_groups)]))
    stacked = jnp.stack(chunks)
    by_half = jnp.take(stacked, half ^ jnp.arange(dp_groups // 2, dtype=jnp.int32), axis=0)
    other = lax.ppermute(by_half, "dp", [(i, i ^ 1) for i in range(dp_groups)])
    pair = jnp.where(
        parity == 0, jnp.stack([by_half, other], axis=1), jnp.stack([other, by_half], axis=1)
    )
    return pair.reshape((SLOTS,) + hidden.shape[1:])


def ffn_stationary(normed_rows, target, placement, chosen, col_width):
    dp_groups = lax.axis_size("dp")
    ex_groups = lax.axis_size("expert")
    me_dp = lax.axis_index("dp")
    model_width = normed_rows.shape[1]
    block = model_width // dp_groups
    ratio = dp_groups // ex_groups
    full = fill_buffer(normed_rows, target)
    blocks = full.reshape(SLOTS, CAP, dp_groups, block).transpose(2, 0, 1, 3)
    rows_here = lax.all_to_all(blocks, "dp", split_axis=0, concat_axis=0, tiled=True)
    partial = jnp.einsum(
        "gscd,sdkf->gsckf", rows_here, chosen[:, :, 0:2, :], preferred_element_type=jnp.float32
    ).astype(jnp.bfloat16)
    summed = lax.psum_scatter(partial, "dp", scatter_dimension=1, tiled=True).astype(jnp.float32)
    hidden = (jax.nn.silu(summed[..., 0, :]) * summed[..., 1, :]).astype(jnp.bfloat16)
    hidden_all = gather_slots(hidden.transpose(1, 0, 2, 3)).transpose(1, 0, 2, 3)
    terms = jnp.einsum(
        "gscf,sdf->gscd", hidden_all, chosen[:, :, 2, :], preferred_element_type=jnp.float32
    ).astype(jnp.bfloat16)
    reduced = lax.psum_scatter(terms, "expert", scatter_dimension=0, tiled=True)
    pieces = []
    for part in range(ratio):
        got = None
        for lead in range(ratio):
            pairs = []
            for src_dp in range(dp_groups):
                if src_dp % ratio != part:
                    continue
                for src_ex in range(ex_groups):
                    dst = (ratio * src_ex + lead) * ex_groups + src_dp // ratio
                    pairs.append((src_dp * ex_groups + src_ex, dst))
            moved = lax.ppermute(reduced[lead], ("dp", "expert"), pairs)
            moved = jnp.where(me_dp % ratio == lead, moved, jnp.zeros_like(moved))
            got = moved if got is None else got + moved
        pieces.append(got)
    cols = jnp.concatenate(pieces, axis=-1)
    return collect(cols.reshape(SLOTS * CAP, col_width), target)


def attend(
    hidden_cols,
    lens_here,
    routes,
    gain_vec,
    router,
    query_flat,
    key_value_flat,
    output_flat,
    cosine,
    sine_table,
    placement,
    stored,
):
    full_rows = hidden_cols
    req_count, seq_len, model_width = full_rows.shape
    token_count = req_count * seq_len
    expert_count = router.shape[1]
    head_width = cosine.shape[1] * 2
    normed = rms_norm(full_rows.reshape(token_count, model_width), gain_vec)
    logits = jnp.dot(normed, router, preferred_element_type=jnp.float32)
    gate_pair = pair_gates(logits, routes)
    every_query = jnp.einsum(
        "td,dehk->tehk", normed, query_flat, preferred_element_type=jnp.float32
    )
    route_hits = (
        routes[:, :, None] == jnp.arange(expert_count, dtype=jnp.int32)[None, None, :]
    ).astype(jnp.float32)
    queries = jnp.einsum(
        "tke,tehd->tkhd", route_hits, every_query, precision=lax.Precision.HIGHEST
    )
    queries = rope_apply(
        queries.reshape(req_count, seq_len, 2, -1, head_width), cosine, sine_table, 1
    ).astype(jnp.bfloat16)
    key_value = jnp.einsum(
        "td,dchk->tchk", normed, key_value_flat, preferred_element_type=jnp.float32
    ).reshape(req_count, seq_len, 2, -1, head_width)
    key_rows = rope_apply(key_value[:, :, 0], cosine, sine_table, 1).astype(jnp.bfloat16)
    values = key_value[:, :, 1].astype(jnp.bfloat16)
    scores = jnp.einsum(
        "rtkhd,ruhd->rkhtu", queries, key_rows, preferred_element_type=jnp.float32
    ) / math.sqrt(head_width)
    positions = jnp.arange(seq_len, dtype=jnp.int32)
    allowed = (positions[None, None, :] <= positions[None, :, None]) & (
        positions[None, None, :] < lens_here[:, None, None]
    )
    raised = jnp.where(allowed[:, None, None], jnp.exp(scores), 0.0)
    probability = (raised / jnp.sum(raised, axis=-1, keepdims=True)).astype(jnp.bfloat16)
    head_out = jnp.einsum(
        "rkhtu,ruhd->rtkhd", probability, values, preferred_element_type=jnp.float32
    )
    head_out = head_out.reshape(token_count, 2, -1, head_width)
    expert_hits = (
        routes[:, :, None] == jnp.arange(expert_count, dtype=jnp.int32)[None, None, :]
    ).astype(jnp.float32) * gate_pair[:, :, None]
    mixed_heads = jnp.einsum(
        "tke,tkhd->tehd", expert_hits, head_out, precision=lax.Precision.HIGHEST
    ).astype(jnp.bfloat16)
    partial_value = jnp.dot(
        mixed_heads.reshape(token_count, -1), output_flat, preferred_element_type=jnp.float32
    )
    partial_value, placement = lax.optimization_barrier(
        (partial_value.astype(jnp.bfloat16), placement)
    )
    attn_full = lax.psum(partial_value, "expert").astype(jnp.float32)
    chosen = stored.at[placement].get(mode="promise_in_bounds")
    residual = (full_rows.reshape(token_count, -1).astype(jnp.float32) + attn_full).astype(
        jnp.bfloat16
    )
    return residual, chosen


def per_device(
    hidden_in,
    request_order,
    request_lengths,
    attention_routes,
    expert_routes,
    replica_picks,
    old_slots,
    new_slots,
    norm_gain_att,
    norm_gain_ffn,
    att_router,
    query_weight,
    key_value_weight,
    output_weight,
    ffn_router,
    expert_weights,
):
    req_count = hidden_in.shape[1]
    seq_len = hidden_in.shape[2]
    col_width = hidden_in.shape[3]
    model_width = norm_gain_att.shape[0]
    token_count = req_count * seq_len
    dp_groups = lax.axis_size("dp")
    slots_here = SLOTS // dp_groups
    head_width = query_weight.shape[3]
    cosine, sine_table = rope_tables(seq_len, head_width)
    query_flat = query_weight
    key_value_flat = key_value_weight
    output_flat = output_weight.reshape(-1, model_width)
    column_start = lax.axis_index("expert") * col_width
    placements = jnp.stack([old_slots, new_slots])
    lens_all = jnp.take_along_axis(request_lengths, request_order, axis=1)
    lens_here = lax.dynamic_slice_in_dim(lens_all, lax.axis_index("dp") * req_count, req_count, 1)

    def one_batch(hidden_b, lens_b, att_b, ffn_b, picks_b, placement):
        live_rows = (jnp.arange(seq_len, dtype=jnp.int32)[None, :] < lens_b[:, None]).reshape(
            token_count
        )
        att_pairs = att_b.reshape(token_count, 2)
        full_rows = lax.all_gather(hidden_b, "expert", axis=2, tiled=True)
        residual_full, chosen = attend(
            full_rows,
            lens_b,
            att_pairs,
            norm_gain_att,
            att_router,
            query_flat,
            key_value_flat,
            output_flat,
            cosine,
            sine_table,
            placement,
            expert_weights,
        )
        ffn_pairs = ffn_b.reshape(token_count, 2)
        routes_flat = ffn_pairs.reshape(-1)
        picks_flat = picks_b.reshape(-1)
        live_assign = jnp.repeat(live_rows, 2)
        target = slot_targets(placement, routes_flat, picks_flat, live_assign)
        normed_rows = rms_norm(residual_full, norm_gain_ffn)
        logits = jnp.dot(normed_rows, ffn_router, preferred_element_type=jnp.float32)
        residual = lax.dynamic_slice_in_dim(residual_full, column_start, col_width, 1)
        gate_pair = pair_gates(logits, ffn_pairs)
        expert_out = ffn_stationary(normed_rows, target, placement, chosen, col_width).astype(
            jnp.float32
        )
        paired = expert_out.reshape(token_count, 2, col_width)
        combined = (
            residual.astype(jnp.float32)
            + gate_pair[:, 0:1] * paired[:, 0]
            + gate_pair[:, 1:2] * paired[:, 1]
        )
        combined = jnp.where(live_rows[:, None], combined, 0.0).astype(jnp.bfloat16)
        return combined.reshape(req_count, seq_len, col_width)

    return jax.vmap(one_batch)(
        hidden_in, lens_here, attention_routes, expert_routes, replica_picks, placements
    )


def solution(mesh):
    in_specs = (
        P(None, "dp", None, "expert"),
        P(),
        P(),
        P(None, "dp", None, None),
        P(None, "dp", None, None),
        P(None, "dp", None, None),
        P(),
        P(),
        P(),
        P(),
        P(),
        P(None, None, "expert", None),
        P(None, None, "expert", None),
        P(None, "expert", None, None),
        P(),
        P(None, "dp", None, "expert"),
    )
    out_specs = P(None, "dp", None, "expert")
    return jax.shard_map(
        per_device, mesh=mesh, in_specs=in_specs, out_specs=out_specs, check_vma=False
    )
```

```python
import math

import jax
import jax.numpy as jnp
from jax import lax
from jax.sharding import PartitionSpec as P

FEXP = 8
TOPK = 2
SLOTS = 16
CAP = 12


EPS = 1e-06
ROPE_BASE = 10000.0


def rope_tables(seq_len, head_width):
    half_width = head_width // 2
    frequency = ROPE_BASE ** (-(jnp.arange(half_width, dtype=jnp.float32) * 2.0 / head_width))
    angles = jnp.arange(seq_len, dtype=jnp.float32)[:, None] * frequency[None, :]
    return (jnp.cos(angles), jnp.sin(angles))


def rope_apply(values, cosine, sine_table, along_axis):
    half_width = values.shape[-1] // 2
    tile_shape = [1] * values.ndim
    tile_shape[along_axis] = cosine.shape[0]
    tile_shape[-1] = half_width
    cos_part = cosine.reshape(tile_shape)
    sin_part = sine_table.reshape(tile_shape)
    front_half = values[..., :half_width]
    back_half = values[..., half_width:]
    return jnp.concatenate(
        [
            front_half * cos_part - back_half * sin_part,
            back_half * cos_part + front_half * sin_part,
        ],
        axis=-1,
    )


def rms_norm(rows, gain_vec):
    widened = rows.astype(jnp.float32)
    inv_rms = lax.rsqrt(jnp.mean(widened * widened, axis=-1, keepdims=True) + EPS)
    return (widened * inv_rms * gain_vec).astype(jnp.bfloat16)


def pair_gates(logits, routes):
    picked = jnp.take_along_axis(logits, routes, axis=-1)
    leading = jax.nn.sigmoid(picked[..., 0] - picked[..., 1])
    return jnp.stack([leading, 1.0 - leading], axis=-1)


def slot_targets(placement, expert_ids, replica_ids, live_rows):
    slot_range = jnp.arange(SLOTS, dtype=jnp.int32)
    same_expert = placement[:, None] == placement[None, :]
    earlier = slot_range[:, None] > slot_range[None, :]
    occurrence = jnp.sum((same_expert & earlier).astype(jnp.int32), axis=1)
    hosting = (placement[None, :] == jnp.arange(FEXP, dtype=jnp.int32)[:, None]).astype(jnp.int32)
    copies_all = jnp.sum(hosting, axis=1)
    chosen = (expert_ids[:, None] == jnp.arange(FEXP, dtype=jnp.int32)[None, :]).astype(jnp.int32)
    copies = jnp.sum(chosen * copies_all[None, :], axis=1)
    replica = replica_ids % copies
    slot_hits = (
        (placement[None, :] == expert_ids[:, None])
        & (occurrence[None, :] == replica[:, None])
        & live_rows[:, None]
    )
    slot_hits = slot_hits.astype(jnp.int32)
    before = jnp.cumsum(slot_hits, axis=0) - slot_hits
    ranking = jnp.sum(before * slot_hits, axis=1)
    slot_ids = jnp.sum(slot_hits * slot_range[None, :], axis=1)
    within_cap = (jnp.sum(slot_hits, axis=1) > 0) & (ranking < CAP)
    return jnp.where(within_cap, slot_ids * CAP + ranking, SLOTS * CAP)


def fill_buffer(rows, target):
    positions = jnp.arange(SLOTS * CAP, dtype=jnp.int32)
    hits = (target[None, :] == positions[:, None]).reshape(SLOTS * CAP, -1, TOPK).any(axis=2)
    buffer = jnp.dot(hits.astype(rows.dtype), rows, preferred_element_type=jnp.float32)
    return buffer.astype(rows.dtype).reshape(SLOTS, CAP, rows.shape[1])


def collect(results, target):
    flat_rows = results.reshape(SLOTS * CAP, results.shape[-1])
    positions = jnp.arange(SLOTS * CAP, dtype=jnp.int32)
    hits = (target[:, None] == positions[None, :]).astype(flat_rows.dtype)
    return jnp.dot(hits, flat_rows, preferred_element_type=jnp.float32)


def load_weights(stored, placement):
    dp_groups = lax.axis_size("dp")
    per = SLOTS // dp_groups
    me = lax.axis_index("dp")
    pieces = []
    for shift in range(dp_groups):
        partner = me ^ shift
        ids = lax.dynamic_slice_in_dim(placement, partner * per, per)
        piece = jnp.take(stored, ids, axis=0)
        if shift:
            pairs = [(i, i ^ shift) for i in range(dp_groups)]
            piece = lax.ppermute(piece, "dp", pairs)
        pieces.append(piece)
    return jnp.stack(pieces, axis=1)


def block_order(rows, axis):
    dp_groups = lax.axis_size("dp")
    me = lax.axis_index("dp")
    shape = rows.shape
    split = shape[:axis] + (dp_groups, shape[axis] // dp_groups) + shape[axis + 1 :]
    order = me ^ jnp.arange(dp_groups, dtype=jnp.int32)
    return jnp.take(rows.reshape(split), order, axis=axis).reshape(shape)


def expert_terms(slot_items, loaded):
    per, groups, block, _, cols = loaded.shape
    weights_here = loaded.reshape(per, groups * block, 3, cols)
    slot_items = block_order(slot_items, 3)
    gate_proj = jnp.einsum(
        "gjcd,jdf->gjcf", slot_items, weights_here[:, :, 0, :], preferred_element_type=jnp.float32
    )
    up_proj = jnp.einsum(
        "gjcd,jdf->gjcf", slot_items, weights_here[:, :, 1, :], preferred_element_type=jnp.float32
    )
    hidden = (jax.nn.silu(gate_proj) * up_proj).astype(jnp.bfloat16)
    terms = jnp.einsum(
        "gjcf,jdf->gjcd", hidden, weights_here[:, :, 2, :], preferred_element_type=jnp.float32
    )
    return block_order(terms.astype(jnp.bfloat16), 3)


def gather_slots(hidden):
    dp_groups = lax.axis_size("dp")
    me = lax.axis_index("dp")
    parity = me % 2
    half = me // 2
    chunks = [hidden]
    for shift in range(1, dp_groups // 2):
        chunks.append(lax.ppermute(hidden, "dp", [(i, i ^ (2 * shift)) for i in range(dp_groups)]))
    stacked = jnp.stack(chunks)
    by_half = jnp.take(stacked, half ^ jnp.arange(dp_groups // 2, dtype=jnp.int32), axis=0)
    other = lax.ppermute(by_half, "dp", [(i, i ^ 1) for i in range(dp_groups)])
    pair = jnp.where(
        parity == 0, jnp.stack([by_half, other], axis=1), jnp.stack([other, by_half], axis=1)
    )
    return pair.reshape((SLOTS,) + hidden.shape[1:])


def ffn_stationary(normed_rows, target, placement, chosen, col_width):
    dp_groups = lax.axis_size("dp")
    ex_groups = lax.axis_size("expert")
    me_dp = lax.axis_index("dp")
    model_width = normed_rows.shape[1]
    block = model_width // dp_groups
    ratio = dp_groups // ex_groups
    full = fill_buffer(normed_rows, target)
    blocks = full.reshape(SLOTS, CAP, dp_groups, block).transpose(2, 0, 1, 3)
    rows_here = lax.all_to_all(blocks, "dp", split_axis=0, concat_axis=0, tiled=True)
    partial = jnp.einsum(
        "gscd,sdkf->gsckf", rows_here, chosen[:, :, 0:2, :], preferred_element_type=jnp.float32
    ).astype(jnp.bfloat16)
    summed = lax.psum_scatter(partial, "dp", scatter_dimension=1, tiled=True).astype(jnp.float32)
    hidden = (jax.nn.silu(summed[..., 0, :]) * summed[..., 1, :]).astype(jnp.bfloat16)
    hidden_all = gather_slots(hidden.transpose(1, 0, 2, 3)).transpose(1, 0, 2, 3)
    terms = jnp.einsum(
        "gscf,sdf->gscd", hidden_all, chosen[:, :, 2, :], preferred_element_type=jnp.float32
    ).astype(jnp.bfloat16)
    if ex_groups == 4:
        chunk_of = ((3, 2, 1, 0), (0, 2, 3, 1), (2, 0, 1, 3), (3, 1, 2, 0))
    else:
        chunk_of = tuple(tuple(range(ex_groups)) for _ in range(ex_groups))
    chunk_of = chunk_of[: dp_groups // ratio]
    order = jnp.asarray(
        [[ratio * row[k // ratio] + k % ratio for k in range(dp_groups)] for row in chunk_of],
        dtype=jnp.int32,
    )
    terms = jnp.take(terms, order[me_dp // ratio], axis=0)
    reduced = lax.psum_scatter(terms, "expert", scatter_dimension=0, tiled=True)
    pieces = []
    for part in range(ratio):
        got = None
        for lead in range(ratio):
            pairs = []
            for src_dp in range(dp_groups):
                if src_dp % ratio != part:
                    continue
                line = src_dp // ratio
                for src_ex in range(ex_groups):
                    dst = (ratio * chunk_of[line][src_ex] + lead) * ex_groups + line
                    pairs.append((src_dp * ex_groups + src_ex, dst))
            moved = lax.ppermute(reduced[lead], ("dp", "expert"), pairs)
            moved = jnp.where(me_dp % ratio == lead, moved, jnp.zeros_like(moved))
            got = moved if got is None else got + moved
        pieces.append(got)
    cols = jnp.concatenate(pieces, axis=-1)
    return collect(cols.reshape(SLOTS * CAP, col_width), target)


def attend(
    hidden_cols,
    lens_here,
    routes,
    gain_vec,
    router,
    query_flat,
    key_value_flat,
    output_flat,
    cosine,
    sine_table,
    placement,
    stored,
):
    full_rows = hidden_cols
    req_count, seq_len, model_width = full_rows.shape
    token_count = req_count * seq_len
    expert_count = router.shape[1]
    head_width = cosine.shape[1] * 2
    normed = rms_norm(full_rows.reshape(token_count, model_width), gain_vec)
    logits = jnp.dot(normed, router, preferred_element_type=jnp.float32)
    gate_pair = pair_gates(logits, routes)
    every_query = jnp.einsum(
        "td,dehk->tehk", normed, query_flat, preferred_element_type=jnp.float32
    )
    queries = jnp.take_along_axis(every_query, routes[:, :, None, None], axis=1)
    queries = rope_apply(
        queries.reshape(req_count, seq_len, 2, -1, head_width), cosine, sine_table, 1
    ).astype(jnp.bfloat16)
    key_value = jnp.einsum(
        "td,dchk->tchk", normed, key_value_flat, preferred_element_type=jnp.float32
    ).reshape(req_count, seq_len, 2, -1, head_width)
    key_rows = rope_apply(key_value[:, :, 0], cosine, sine_table, 1).astype(jnp.bfloat16)
    values = key_value[:, :, 1].astype(jnp.bfloat16)
    scores = jnp.einsum(
        "rtkhd,ruhd->rkhtu", queries, key_rows, preferred_element_type=jnp.float32
    ) / math.sqrt(head_width)
    positions = jnp.arange(seq_len, dtype=jnp.int32)
    allowed = (positions[None, None, :] <= positions[None, :, None]) & (
        positions[None, None, :] < lens_here[:, None, None]
    )
    raised = jnp.where(allowed[:, None, None], jnp.exp(scores), 0.0)
    probability = (raised / jnp.sum(raised, axis=-1, keepdims=True)).astype(jnp.bfloat16)
    head_out = jnp.einsum(
        "rkhtu,ruhd->rtkhd", probability, values, preferred_element_type=jnp.float32
    )
    head_out = head_out.reshape(token_count, 2, -1, head_width)
    expert_hits = (
        routes[:, :, None] == jnp.arange(expert_count, dtype=jnp.int32)[None, None, :]
    ).astype(jnp.float32) * gate_pair[:, :, None]
    mixed_heads = jnp.einsum(
        "tke,tkhd->tehd", expert_hits, head_out, precision=lax.Precision.HIGHEST
    ).astype(jnp.bfloat16)
    partial_value = jnp.dot(
        mixed_heads.reshape(token_count, -1), output_flat, preferred_element_type=jnp.float32
    )
    partial_value, placement = lax.optimization_barrier(
        (partial_value.astype(jnp.bfloat16), placement)
    )
    attn_full = lax.psum(partial_value, "expert").astype(jnp.float32)
    chosen = stored.at[placement].get(mode="promise_in_bounds")
    residual = (full_rows.reshape(token_count, -1).astype(jnp.float32) + attn_full).astype(
        jnp.bfloat16
    )
    return residual, chosen


def per_device(
    hidden_in,
    request_order,
    request_lengths,
    attention_routes,
    expert_routes,
    replica_picks,
    old_slots,
    new_slots,
    norm_gain_att,
    norm_gain_ffn,
    att_router,
    query_weight,
    key_value_weight,
    output_weight,
    ffn_router,
    expert_weights,
):
    req_count = hidden_in.shape[1]
    seq_len = hidden_in.shape[2]
    col_width = hidden_in.shape[3]
    model_width = norm_gain_att.shape[0]
    token_count = req_count * seq_len
    dp_groups = lax.axis_size("dp")
    slots_here = SLOTS // dp_groups
    head_width = query_weight.shape[3]
    cosine, sine_table = rope_tables(seq_len, head_width)
    query_flat = query_weight
    key_value_flat = key_value_weight
    output_flat = output_weight.reshape(-1, model_width)
    column_start = lax.axis_index("expert") * col_width
    placements = jnp.stack([old_slots, new_slots])
    lens_all = jnp.take_along_axis(request_lengths, request_order, axis=1)
    lens_here = lax.dynamic_slice_in_dim(lens_all, lax.axis_index("dp") * req_count, req_count, 1)

    def one_batch(hidden_b, lens_b, att_b, ffn_b, picks_b, placement):
        live_rows = (jnp.arange(seq_len, dtype=jnp.int32)[None, :] < lens_b[:, None]).reshape(
            token_count
        )
        att_pairs = att_b.reshape(token_count, 2)
        full_rows = lax.all_gather(hidden_b, "expert", axis=2, tiled=True)
        residual_full, chosen = attend(
            full_rows,
            lens_b,
            att_pairs,
            norm_gain_att,
            att_router,
            query_flat,
            key_value_flat,
            output_flat,
            cosine,
            sine_table,
            placement,
            expert_weights,
        )
        ffn_pairs = ffn_b.reshape(token_count, 2)
        routes_flat = ffn_pairs.reshape(-1)
        picks_flat = picks_b.reshape(-1)
        live_assign = jnp.repeat(live_rows, 2)
        target = slot_targets(placement, routes_flat, picks_flat, live_assign)
        normed_rows = rms_norm(residual_full, norm_gain_ffn)
        logits = jnp.dot(normed_rows, ffn_router, preferred_element_type=jnp.float32)
        residual = lax.dynamic_slice_in_dim(residual_full, column_start, col_width, 1)
        gate_pair = pair_gates(logits, ffn_pairs)
        expert_out = ffn_stationary(normed_rows, target, placement, chosen, col_width).astype(
            jnp.float32
        )
        paired = expert_out.reshape(token_count, 2, col_width)
        combined = (
            residual.astype(jnp.float32)
            + gate_pair[:, 0:1] * paired[:, 0]
            + gate_pair[:, 1:2] * paired[:, 1]
        )
        combined = jnp.where(live_rows[:, None], combined, 0.0).astype(jnp.bfloat16)
        return combined.reshape(req_count, seq_len, col_width)

    return jax.vmap(one_batch)(
        hidden_in, lens_here, attention_routes, expert_routes, replica_picks, placements
    )


def solution(mesh):
    in_specs = (
        P(None, "dp", None, "expert"),
        P(),
        P(),
        P(None, "dp", None, None),
        P(None, "dp", None, None),
        P(None, "dp", None, None),
        P(),
        P(),
        P(),
        P(),
        P(),
        P(None, None, "expert", None),
        P(None, None, "expert", None),
        P(None, "expert", None, None),
        P(),
        P(None, "dp", None, "expert"),
    )
    out_specs = P(None, "dp", None, "expert")
    return jax.shard_map(
        per_device, mesh=mesh, in_specs=in_specs, out_specs=out_specs, check_vma=False
    )
```

```python
import math

import jax
import jax.numpy as jnp
from jax import lax
from jax.sharding import PartitionSpec as P

FEXP = 8
TOPK = 2
SLOTS = 16
CAP = 12


EPS = 1e-06
ROPE_BASE = 10000.0


def rope_tables(seq_len, head_width):
    half_width = head_width // 2
    frequency = ROPE_BASE ** (-(jnp.arange(half_width, dtype=jnp.float32) * 2.0 / head_width))
    angles = jnp.arange(seq_len, dtype=jnp.float32)[:, None] * frequency[None, :]
    return (jnp.cos(angles), jnp.sin(angles))


def rope_apply(values, cosine, sine_table, along_axis):
    half_width = values.shape[-1] // 2
    tile_shape = [1] * values.ndim
    tile_shape[along_axis] = cosine.shape[0]
    tile_shape[-1] = half_width
    cos_part = cosine.reshape(tile_shape)
    sin_part = sine_table.reshape(tile_shape)
    front_half = values[..., :half_width]
    back_half = values[..., half_width:]
    return jnp.concatenate(
        [
            front_half * cos_part - back_half * sin_part,
            back_half * cos_part + front_half * sin_part,
        ],
        axis=-1,
    )


def rms_norm(rows, gain_vec):
    widened = rows.astype(jnp.float32)
    inv_rms = lax.rsqrt(jnp.mean(widened * widened, axis=-1, keepdims=True) + EPS)
    return (widened * inv_rms * gain_vec).astype(jnp.bfloat16)


def pair_gates(logits, routes):
    picked = jnp.take_along_axis(logits, routes, axis=-1)
    leading = jax.nn.sigmoid(picked[..., 0] - picked[..., 1])
    return jnp.stack([leading, 1.0 - leading], axis=-1)


def slot_targets(placement, expert_ids, replica_ids, live_rows):
    slot_range = jnp.arange(SLOTS, dtype=jnp.int32)
    same_expert = placement[:, None] == placement[None, :]
    earlier = slot_range[:, None] > slot_range[None, :]
    occurrence = jnp.sum((same_expert & earlier).astype(jnp.int32), axis=1)
    hosting = (placement[None, :] == jnp.arange(FEXP, dtype=jnp.int32)[:, None]).astype(jnp.int32)
    copies_all = jnp.sum(hosting, axis=1)
    chosen = (expert_ids[:, None] == jnp.arange(FEXP, dtype=jnp.int32)[None, :]).astype(jnp.int32)
    copies = jnp.sum(chosen * copies_all[None, :], axis=1)
    replica = replica_ids % copies
    slot_hits = (
        (placement[None, :] == expert_ids[:, None])
        & (occurrence[None, :] == replica[:, None])
        & live_rows[:, None]
    )
    slot_hits = slot_hits.astype(jnp.int32)
    before = jnp.cumsum(slot_hits, axis=0) - slot_hits
    ranking = jnp.sum(before * slot_hits, axis=1)
    slot_ids = jnp.sum(slot_hits * slot_range[None, :], axis=1)
    within_cap = (jnp.sum(slot_hits, axis=1) > 0) & (ranking < CAP)
    return jnp.where(within_cap, slot_ids * CAP + ranking, SLOTS * CAP)


def fill_buffer(rows, target):
    positions = jnp.arange(SLOTS * CAP, dtype=jnp.int32)
    hits = (target[None, :] == positions[:, None]).reshape(SLOTS * CAP, -1, TOPK).any(axis=2)
    buffer = jnp.dot(hits.astype(rows.dtype), rows, preferred_element_type=jnp.float32)
    return buffer.astype(rows.dtype).reshape(SLOTS, CAP, rows.shape[1])


def collect(results, target):
    flat_rows = results.reshape(SLOTS * CAP, results.shape[-1])
    positions = jnp.arange(SLOTS * CAP, dtype=jnp.int32)
    hits = (target[:, None] == positions[None, :]).astype(flat_rows.dtype)
    return jnp.dot(hits, flat_rows, preferred_element_type=jnp.float32)


def load_weights(stored, placement):
    dp_groups = lax.axis_size("dp")
    per = SLOTS // dp_groups
    me = lax.axis_index("dp")
    pieces = []
    for shift in range(dp_groups):
        partner = me ^ shift
        ids = lax.dynamic_slice_in_dim(placement, partner * per, per)
        piece = jnp.take(stored, ids, axis=0)
        if shift:
            pairs = [(i, i ^ shift) for i in range(dp_groups)]
            piece = lax.ppermute(piece, "dp", pairs)
        pieces.append(piece)
    return jnp.stack(pieces, axis=1)


def block_order(rows, axis):
    dp_groups = lax.axis_size("dp")
    me = lax.axis_index("dp")
    shape = rows.shape
    split = shape[:axis] + (dp_groups, shape[axis] // dp_groups) + shape[axis + 1 :]
    order = me ^ jnp.arange(dp_groups, dtype=jnp.int32)
    return jnp.take(rows.reshape(split), order, axis=axis).reshape(shape)


def expert_terms(slot_items, loaded):
    per, groups, block, _, cols = loaded.shape
    weights_here = loaded.reshape(per, groups * block, 3, cols)
    slot_items = block_order(slot_items, 3)
    gate_proj = jnp.einsum(
        "gjcd,jdf->gjcf", slot_items, weights_here[:, :, 0, :], preferred_element_type=jnp.float32
    )
    up_proj = jnp.einsum(
        "gjcd,jdf->gjcf", slot_items, weights_here[:, :, 1, :], preferred_element_type=jnp.float32
    )
    hidden = (jax.nn.silu(gate_proj) * up_proj).astype(jnp.bfloat16)
    terms = jnp.einsum(
        "gjcf,jdf->gjcd", hidden, weights_here[:, :, 2, :], preferred_element_type=jnp.float32
    )
    return block_order(terms.astype(jnp.bfloat16), 3)


def gather_slots(hidden):
    dp_groups = lax.axis_size("dp")
    me = lax.axis_index("dp")
    parity = me % 2
    half = me // 2
    chunks = [hidden]
    for shift in range(1, dp_groups // 2):
        chunks.append(lax.ppermute(hidden, "dp", [(i, i ^ (2 * shift)) for i in range(dp_groups)]))
    stacked = jnp.stack(chunks)
    by_half = jnp.take(stacked, half ^ jnp.arange(dp_groups // 2, dtype=jnp.int32), axis=0)
    other = lax.ppermute(by_half, "dp", [(i, i ^ 1) for i in range(dp_groups)])
    pair = jnp.where(
        parity == 0, jnp.stack([by_half, other], axis=1), jnp.stack([other, by_half], axis=1)
    )
    return pair.reshape((SLOTS,) + hidden.shape[1:])


def ffn_stationary(normed_rows, target, placement, chosen, col_width):
    dp_groups = lax.axis_size("dp")
    ex_groups = lax.axis_size("expert")
    me_dp = lax.axis_index("dp")
    model_width = normed_rows.shape[1]
    block = model_width // dp_groups
    ratio = dp_groups // ex_groups
    full = fill_buffer(normed_rows, target)
    blocks = full.reshape(SLOTS, CAP, dp_groups, block).transpose(2, 0, 1, 3)
    rows_here = lax.all_to_all(blocks, "dp", split_axis=0, concat_axis=0, tiled=True)
    partial = jnp.einsum(
        "gscd,sdkf->gsckf", rows_here, chosen[:, :, 0:2, :], preferred_element_type=jnp.float32
    ).astype(jnp.bfloat16)
    summed = lax.psum_scatter(partial, "dp", scatter_dimension=1, tiled=True).astype(jnp.float32)
    hidden = (jax.nn.silu(summed[..., 0, :]) * summed[..., 1, :]).astype(jnp.bfloat16)
    hidden_all = gather_slots(hidden.transpose(1, 0, 2, 3)).transpose(1, 0, 2, 3)
    terms = jnp.einsum(
        "gscf,sdf->gscd", hidden_all, chosen[:, :, 2, :], preferred_element_type=jnp.float32
    ).astype(jnp.bfloat16)
    spread = terms.reshape((ex_groups, ratio) + terms.shape[1:])
    arrived = lax.all_to_all(spread, "expert", split_axis=0, concat_axis=0, tiled=True)
    reduced = jnp.sum(arrived.astype(jnp.float32), axis=0).astype(jnp.bfloat16)
    pieces = []
    for part in range(ratio):
        got = None
        for lead in range(ratio):
            pairs = []
            for src_dp in range(dp_groups):
                if src_dp % ratio != part:
                    continue
                for src_ex in range(ex_groups):
                    dst = (ratio * src_ex + lead) * ex_groups + src_dp // ratio
                    pairs.append((src_dp * ex_groups + src_ex, dst))
            moved = lax.ppermute(reduced[lead], ("dp", "expert"), pairs)
            moved = jnp.where(me_dp % ratio == lead, moved, jnp.zeros_like(moved))
            got = moved if got is None else got + moved
        pieces.append(got)
    cols = jnp.concatenate(pieces, axis=-1)
    return collect(cols.reshape(SLOTS * CAP, col_width), target)


def attend(
    hidden_cols,
    lens_here,
    routes,
    gain_vec,
    router,
    query_flat,
    key_value_flat,
    output_flat,
    cosine,
    sine_table,
    placement,
    stored,
):
    full_rows = hidden_cols
    req_count, seq_len, model_width = full_rows.shape
    token_count = req_count * seq_len
    expert_count = router.shape[1]
    head_width = cosine.shape[1] * 2
    normed = rms_norm(full_rows.reshape(token_count, model_width), gain_vec)
    logits = jnp.dot(normed, router, preferred_element_type=jnp.float32)
    gate_pair = pair_gates(logits, routes)
    every_query = jnp.einsum(
        "td,dehk->tehk", normed, query_flat, preferred_element_type=jnp.float32
    )
    queries = jnp.take_along_axis(every_query, routes[:, :, None, None], axis=1)
    queries = rope_apply(
        queries.reshape(req_count, seq_len, 2, -1, head_width), cosine, sine_table, 1
    ).astype(jnp.bfloat16)
    key_value = jnp.einsum(
        "td,dchk->tchk", normed, key_value_flat, preferred_element_type=jnp.float32
    ).reshape(req_count, seq_len, 2, -1, head_width)
    key_rows = rope_apply(key_value[:, :, 0], cosine, sine_table, 1).astype(jnp.bfloat16)
    values = key_value[:, :, 1].astype(jnp.bfloat16)
    scores = jnp.einsum(
        "rtkhd,ruhd->rkhtu", queries, key_rows, preferred_element_type=jnp.float32
    ) / math.sqrt(head_width)
    positions = jnp.arange(seq_len, dtype=jnp.int32)
    allowed = (positions[None, None, :] <= positions[None, :, None]) & (
        positions[None, None, :] < lens_here[:, None, None]
    )
    raised = jnp.where(allowed[:, None, None], jnp.exp(scores), 0.0)
    probability = (raised / jnp.sum(raised, axis=-1, keepdims=True)).astype(jnp.bfloat16)
    head_out = jnp.einsum(
        "rkhtu,ruhd->rtkhd", probability, values, preferred_element_type=jnp.float32
    )
    head_out = head_out.reshape(token_count, 2, -1, head_width)
    expert_hits = (
        routes[:, :, None] == jnp.arange(expert_count, dtype=jnp.int32)[None, None, :]
    ).astype(jnp.float32) * gate_pair[:, :, None]
    mixed_heads = jnp.einsum(
        "tke,tkhd->tehd", expert_hits, head_out, precision=lax.Precision.HIGHEST
    ).astype(jnp.bfloat16)
    partial_value = jnp.dot(
        mixed_heads.reshape(token_count, -1), output_flat, preferred_element_type=jnp.float32
    )
    partial_value, placement = lax.optimization_barrier(
        (partial_value.astype(jnp.bfloat16), placement)
    )
    attn_full = lax.psum(partial_value, "expert").astype(jnp.float32)
    chosen = stored.at[placement].get(mode="promise_in_bounds")
    residual = (full_rows.reshape(token_count, -1).astype(jnp.float32) + attn_full).astype(
        jnp.bfloat16
    )
    return residual, chosen


def per_device(
    hidden_in,
    request_order,
    request_lengths,
    attention_routes,
    expert_routes,
    replica_picks,
    old_slots,
    new_slots,
    norm_gain_att,
    norm_gain_ffn,
    att_router,
    query_weight,
    key_value_weight,
    output_weight,
    ffn_router,
    expert_weights,
):
    req_count = hidden_in.shape[1]
    seq_len = hidden_in.shape[2]
    col_width = hidden_in.shape[3]
    model_width = norm_gain_att.shape[0]
    token_count = req_count * seq_len
    dp_groups = lax.axis_size("dp")
    slots_here = SLOTS // dp_groups
    head_width = query_weight.shape[3]
    cosine, sine_table = rope_tables(seq_len, head_width)
    query_flat = query_weight
    key_value_flat = key_value_weight
    output_flat = output_weight.reshape(-1, model_width)
    column_start = lax.axis_index("expert") * col_width
    placements = jnp.stack([old_slots, new_slots])
    lens_all = jnp.take_along_axis(request_lengths, request_order, axis=1)
    lens_here = lax.dynamic_slice_in_dim(lens_all, lax.axis_index("dp") * req_count, req_count, 1)

    def one_batch(hidden_b, lens_b, att_b, ffn_b, picks_b, placement):
        live_rows = (jnp.arange(seq_len, dtype=jnp.int32)[None, :] < lens_b[:, None]).reshape(
            token_count
        )
        att_pairs = att_b.reshape(token_count, 2)
        full_rows = lax.all_gather(hidden_b, "expert", axis=2, tiled=True)
        residual_full, chosen = attend(
            full_rows,
            lens_b,
            att_pairs,
            norm_gain_att,
            att_router,
            query_flat,
            key_value_flat,
            output_flat,
            cosine,
            sine_table,
            placement,
            expert_weights,
        )
        ffn_pairs = ffn_b.reshape(token_count, 2)
        routes_flat = ffn_pairs.reshape(-1)
        picks_flat = picks_b.reshape(-1)
        live_assign = jnp.repeat(live_rows, 2)
        target = slot_targets(placement, routes_flat, picks_flat, live_assign)
        normed_rows = rms_norm(residual_full, norm_gain_ffn)
        logits = jnp.dot(normed_rows, ffn_router, preferred_element_type=jnp.float32)
        residual = lax.dynamic_slice_in_dim(residual_full, column_start, col_width, 1)
        gate_pair = pair_gates(logits, ffn_pairs)
        expert_out = ffn_stationary(normed_rows, target, placement, chosen, col_width).astype(
            jnp.float32
        )
        paired = expert_out.reshape(token_count, 2, col_width)
        combined = (
            residual.astype(jnp.float32)
            + gate_pair[:, 0:1] * paired[:, 0]
            + gate_pair[:, 1:2] * paired[:, 1]
        )
        combined = jnp.where(live_rows[:, None], combined, 0.0).astype(jnp.bfloat16)
        return combined.reshape(req_count, seq_len, col_width)

    return jax.vmap(one_batch)(
        hidden_in, lens_here, attention_routes, expert_routes, replica_picks, placements
    )


def solution(mesh):
    in_specs = (
        P(None, "dp", None, "expert"),
        P(),
        P(),
        P(None, "dp", None, None),
        P(None, "dp", None, None),
        P(None, "dp", None, None),
        P(),
        P(),
        P(),
        P(),
        P(),
        P(None, None, "expert", None),
        P(None, None, "expert", None),
        P(None, "expert", None, None),
        P(),
        P(None, "dp", None, "expert"),
    )
    out_specs = P(None, "dp", None, "expert")
    return jax.shard_map(
        per_device, mesh=mesh, in_specs=in_specs, out_specs=out_specs, check_vma=False
    )
```

```python
import math

import jax
import jax.numpy as jnp
from jax import lax
from jax.sharding import PartitionSpec as P

FEXP = 8
TOPK = 2
SLOTS = 16
CAP = 12


EPS = 1e-06
ROPE_BASE = 10000.0


def rope_tables(seq_len, head_width):
    half_width = head_width // 2
    frequency = ROPE_BASE ** (-(jnp.arange(half_width, dtype=jnp.float32) * 2.0 / head_width))
    angles = jnp.arange(seq_len, dtype=jnp.float32)[:, None] * frequency[None, :]
    return (jnp.cos(angles), jnp.sin(angles))


def rope_apply(values, cosine, sine_table, along_axis):
    half_width = values.shape[-1] // 2
    tile_shape = [1] * values.ndim
    tile_shape[along_axis] = cosine.shape[0]
    tile_shape[-1] = half_width
    cos_part = cosine.reshape(tile_shape)
    sin_part = sine_table.reshape(tile_shape)
    front_half = values[..., :half_width]
    back_half = values[..., half_width:]
    return jnp.concatenate(
        [
            front_half * cos_part - back_half * sin_part,
            back_half * cos_part + front_half * sin_part,
        ],
        axis=-1,
    )


def rms_norm(rows, gain_vec):
    widened = rows.astype(jnp.float32)
    inv_rms = lax.rsqrt(jnp.mean(widened * widened, axis=-1, keepdims=True) + EPS)
    return (widened * inv_rms * gain_vec).astype(jnp.bfloat16)


def pair_gates(logits, routes):
    picked = jnp.take_along_axis(logits, routes, axis=-1)
    leading = jax.nn.sigmoid(picked[..., 0] - picked[..., 1])
    return jnp.stack([leading, 1.0 - leading], axis=-1)


def slot_targets(placement, expert_ids, replica_ids, live_rows):
    slot_range = jnp.arange(SLOTS, dtype=jnp.int32)
    same_expert = placement[:, None] == placement[None, :]
    earlier = slot_range[:, None] > slot_range[None, :]
    occurrence = jnp.sum((same_expert & earlier).astype(jnp.int32), axis=1)
    hosting = (placement[None, :] == jnp.arange(FEXP, dtype=jnp.int32)[:, None]).astype(jnp.int32)
    copies_all = jnp.sum(hosting, axis=1)
    chosen = (expert_ids[:, None] == jnp.arange(FEXP, dtype=jnp.int32)[None, :]).astype(jnp.int32)
    copies = jnp.sum(chosen * copies_all[None, :], axis=1)
    replica = replica_ids % copies
    slot_hits = (
        (placement[None, :] == expert_ids[:, None])
        & (occurrence[None, :] == replica[:, None])
        & live_rows[:, None]
    )
    slot_hits = slot_hits.astype(jnp.int32)
    before = jnp.cumsum(slot_hits, axis=0) - slot_hits
    ranking = jnp.sum(before * slot_hits, axis=1)
    slot_ids = jnp.sum(slot_hits * slot_range[None, :], axis=1)
    within_cap = (jnp.sum(slot_hits, axis=1) > 0) & (ranking < CAP)
    return jnp.where(within_cap, slot_ids * CAP + ranking, SLOTS * CAP)


def fill_buffer(rows, target):
    positions = jnp.arange(SLOTS * CAP, dtype=jnp.int32)
    hits = (target[None, :] == positions[:, None]).reshape(SLOTS * CAP, -1, TOPK).any(axis=2)
    buffer = jnp.dot(hits.astype(rows.dtype), rows, preferred_element_type=jnp.float32)
    return buffer.astype(rows.dtype).reshape(SLOTS, CAP, rows.shape[1])


def collect(results, target):
    flat_rows = results.reshape(SLOTS * CAP, results.shape[-1])
    positions = jnp.arange(SLOTS * CAP, dtype=jnp.int32)
    hits = (target[:, None] == positions[None, :]).astype(flat_rows.dtype)
    return jnp.dot(hits, flat_rows, preferred_element_type=jnp.float32)


def load_weights(stored, placement):
    dp_groups = lax.axis_size("dp")
    per = SLOTS // dp_groups
    me = lax.axis_index("dp")
    pieces = []
    for shift in range(dp_groups):
        partner = me ^ shift
        ids = lax.dynamic_slice_in_dim(placement, partner * per, per)
        piece = jnp.take(stored, ids, axis=0)
        if shift:
            pairs = [(i, i ^ shift) for i in range(dp_groups)]
            piece = lax.ppermute(piece, "dp", pairs)
        pieces.append(piece)
    return jnp.stack(pieces, axis=1)


def block_order(rows, axis):
    dp_groups = lax.axis_size("dp")
    me = lax.axis_index("dp")
    shape = rows.shape
    split = shape[:axis] + (dp_groups, shape[axis] // dp_groups) + shape[axis + 1 :]
    order = me ^ jnp.arange(dp_groups, dtype=jnp.int32)
    return jnp.take(rows.reshape(split), order, axis=axis).reshape(shape)


def expert_terms(slot_items, loaded):
    per, groups, block, _, cols = loaded.shape
    weights_here = loaded.reshape(per, groups * block, 3, cols)
    slot_items = block_order(slot_items, 3)
    gate_proj = jnp.einsum(
        "gjcd,jdf->gjcf", slot_items, weights_here[:, :, 0, :], preferred_element_type=jnp.float32
    )
    up_proj = jnp.einsum(
        "gjcd,jdf->gjcf", slot_items, weights_here[:, :, 1, :], preferred_element_type=jnp.float32
    )
    hidden = (jax.nn.silu(gate_proj) * up_proj).astype(jnp.bfloat16)
    terms = jnp.einsum(
        "gjcf,jdf->gjcd", hidden, weights_here[:, :, 2, :], preferred_element_type=jnp.float32
    )
    return block_order(terms.astype(jnp.bfloat16), 3)


def gather_slots(hidden):
    dp_groups = lax.axis_size("dp")
    me = lax.axis_index("dp")
    parity = me % 2
    half = me // 2
    chunks = [hidden]
    for shift in range(1, dp_groups // 2):
        chunks.append(lax.ppermute(hidden, "dp", [(i, i ^ (2 * shift)) for i in range(dp_groups)]))
    stacked = jnp.stack(chunks)
    by_half = jnp.take(stacked, half ^ jnp.arange(dp_groups // 2, dtype=jnp.int32), axis=0)
    other = lax.ppermute(by_half, "dp", [(i, i ^ 1) for i in range(dp_groups)])
    pair = jnp.where(
        parity == 0, jnp.stack([by_half, other], axis=1), jnp.stack([other, by_half], axis=1)
    )
    return pair.reshape((SLOTS,) + hidden.shape[1:])


def ffn_stationary(normed_rows, target, placement, chosen, col_width):
    dp_groups = lax.axis_size("dp")
    ex_groups = lax.axis_size("expert")
    me_dp = lax.axis_index("dp")
    model_width = normed_rows.shape[1]
    block = model_width // dp_groups
    ratio = dp_groups // ex_groups
    full = fill_buffer(normed_rows, target)
    blocks = full.reshape(SLOTS, CAP, dp_groups, block).transpose(2, 0, 1, 3)
    rows_here = lax.all_to_all(blocks, "dp", split_axis=0, concat_axis=0, tiled=True)
    partial = jnp.einsum(
        "gscd,sdkf->gsckf", rows_here, chosen[:, :, 0:2, :], preferred_element_type=jnp.float32
    ).astype(jnp.bfloat16)
    return partial


def ffn_tail(summed, target, chosen, col_width):
    dp_groups = lax.axis_size("dp")
    ex_groups = lax.axis_size("expert")
    me_dp = lax.axis_index("dp")
    ratio = dp_groups // ex_groups
    summed = summed.astype(jnp.float32)
    hidden = (jax.nn.silu(summed[..., 0, :]) * summed[..., 1, :]).astype(jnp.bfloat16)
    hidden_all = gather_slots(hidden.transpose(1, 0, 2, 3)).transpose(1, 0, 2, 3)
    terms = jnp.einsum(
        "gscf,sdf->gscd", hidden_all, chosen[:, :, 2, :], preferred_element_type=jnp.float32
    ).astype(jnp.bfloat16)
    reduced = lax.psum_scatter(terms, "expert", scatter_dimension=0, tiled=True)
    pieces = []
    for part in range(ratio):
        got = None
        for lead in range(ratio):
            pairs = []
            for src_dp in range(dp_groups):
                if src_dp % ratio != part:
                    continue
                for src_ex in range(ex_groups):
                    dst = (ratio * src_ex + lead) * ex_groups + src_dp // ratio
                    pairs.append((src_dp * ex_groups + src_ex, dst))
            moved = lax.ppermute(reduced[lead], ("dp", "expert"), pairs)
            moved = jnp.where(me_dp % ratio == lead, moved, jnp.zeros_like(moved))
            got = moved if got is None else got + moved
        pieces.append(got)
    cols = jnp.concatenate(pieces, axis=-1)
    return collect(cols.reshape(SLOTS * CAP, col_width), target)


def attend(
    hidden_cols,
    lens_here,
    routes,
    gain_vec,
    router,
    query_flat,
    key_value_flat,
    output_flat,
    cosine,
    sine_table,
    placement,
    stored,
):
    full_rows = hidden_cols
    req_count, seq_len, model_width = full_rows.shape
    token_count = req_count * seq_len
    expert_count = router.shape[1]
    head_width = cosine.shape[1] * 2
    normed = rms_norm(full_rows.reshape(token_count, model_width), gain_vec)
    logits = jnp.dot(normed, router, preferred_element_type=jnp.float32)
    gate_pair = pair_gates(logits, routes)
    every_query = jnp.einsum(
        "td,dehk->tehk", normed, query_flat, preferred_element_type=jnp.float32
    )
    queries = jnp.take_along_axis(every_query, routes[:, :, None, None], axis=1)
    queries = rope_apply(
        queries.reshape(req_count, seq_len, 2, -1, head_width), cosine, sine_table, 1
    ).astype(jnp.bfloat16)
    key_value = jnp.einsum(
        "td,dchk->tchk", normed, key_value_flat, preferred_element_type=jnp.float32
    ).reshape(req_count, seq_len, 2, -1, head_width)
    key_rows = rope_apply(key_value[:, :, 0], cosine, sine_table, 1).astype(jnp.bfloat16)
    values = key_value[:, :, 1].astype(jnp.bfloat16)
    scores = jnp.einsum(
        "rtkhd,ruhd->rkhtu", queries, key_rows, preferred_element_type=jnp.float32
    ) / math.sqrt(head_width)
    positions = jnp.arange(seq_len, dtype=jnp.int32)
    allowed = (positions[None, None, :] <= positions[None, :, None]) & (
        positions[None, None, :] < lens_here[:, None, None]
    )
    raised = jnp.where(allowed[:, None, None], jnp.exp(scores), 0.0)
    probability = (raised / jnp.sum(raised, axis=-1, keepdims=True)).astype(jnp.bfloat16)
    head_out = jnp.einsum(
        "rkhtu,ruhd->rtkhd", probability, values, preferred_element_type=jnp.float32
    )
    head_out = head_out.reshape(token_count, 2, -1, head_width)
    expert_hits = (
        routes[:, :, None] == jnp.arange(expert_count, dtype=jnp.int32)[None, None, :]
    ).astype(jnp.float32) * gate_pair[:, :, None]
    mixed_heads = jnp.einsum(
        "tke,tkhd->tehd", expert_hits, head_out, precision=lax.Precision.HIGHEST
    ).astype(jnp.bfloat16)
    partial_value = jnp.dot(
        mixed_heads.reshape(token_count, -1), output_flat, preferred_element_type=jnp.float32
    )
    partial_value, placement = lax.optimization_barrier(
        (partial_value.astype(jnp.bfloat16), placement)
    )
    attn_full = lax.psum(partial_value, "expert").astype(jnp.float32)
    chosen = stored.at[placement].get(mode="promise_in_bounds")
    residual = (full_rows.reshape(token_count, -1).astype(jnp.float32) + attn_full).astype(
        jnp.bfloat16
    )
    return residual, chosen


def per_device(
    hidden_in,
    request_order,
    request_lengths,
    attention_routes,
    expert_routes,
    replica_picks,
    old_slots,
    new_slots,
    norm_gain_att,
    norm_gain_ffn,
    att_router,
    query_weight,
    key_value_weight,
    output_weight,
    ffn_router,
    expert_weights,
):
    req_count = hidden_in.shape[1]
    seq_len = hidden_in.shape[2]
    col_width = hidden_in.shape[3]
    model_width = norm_gain_att.shape[0]
    token_count = req_count * seq_len
    dp_groups = lax.axis_size("dp")
    slots_here = SLOTS // dp_groups
    head_width = query_weight.shape[3]
    cosine, sine_table = rope_tables(seq_len, head_width)
    query_flat = query_weight
    key_value_flat = key_value_weight
    output_flat = output_weight.reshape(-1, model_width)
    column_start = lax.axis_index("expert") * col_width
    placements = jnp.stack([old_slots, new_slots])
    lens_all = jnp.take_along_axis(request_lengths, request_order, axis=1)
    lens_here = lax.dynamic_slice_in_dim(lens_all, lax.axis_index("dp") * req_count, req_count, 1)

    def one_batch(hidden_b, lens_b, att_b, ffn_b, picks_b, placement):
        live_rows = (jnp.arange(seq_len, dtype=jnp.int32)[None, :] < lens_b[:, None]).reshape(
            token_count
        )
        att_pairs = att_b.reshape(token_count, 2)
        full_rows = lax.all_gather(hidden_b, "expert", axis=2, tiled=True)
        residual_full, chosen = attend(
            full_rows,
            lens_b,
            att_pairs,
            norm_gain_att,
            att_router,
            query_flat,
            key_value_flat,
            output_flat,
            cosine,
            sine_table,
            placement,
            expert_weights,
        )
        ffn_pairs = ffn_b.reshape(token_count, 2)
        routes_flat = ffn_pairs.reshape(-1)
        picks_flat = picks_b.reshape(-1)
        live_assign = jnp.repeat(live_rows, 2)
        target = slot_targets(placement, routes_flat, picks_flat, live_assign)
        normed_rows = rms_norm(residual_full, norm_gain_ffn)
        logits = jnp.dot(normed_rows, ffn_router, preferred_element_type=jnp.float32)
        residual = lax.dynamic_slice_in_dim(residual_full, column_start, col_width, 1)
        gate_pair = pair_gates(logits, ffn_pairs)
        return residual, normed_rows, target, chosen, gate_pair, live_rows

    residual, normed_rows, target, chosen, gate_pair, live_rows = jax.vmap(one_batch)(
        hidden_in, lens_here, attention_routes, expert_routes, replica_picks, placements
    )
    partials = [
        ffn_stationary(normed_rows[b], target[b], placements[b], chosen[b], col_width)
        for b in range(hidden_in.shape[0])
    ]
    summed = lax.psum_scatter(jnp.stack(partials), "dp", scatter_dimension=2, tiled=True)

    def back(summed_b, target_b, chosen_b, residual_b, gates, live_b):
        expert_out = ffn_tail(summed_b, target_b, chosen_b, col_width).astype(jnp.float32)
        paired = expert_out.reshape(token_count, 2, col_width)
        combined = (
            residual_b.astype(jnp.float32)
            + gates[:, 0:1] * paired[:, 0]
            + gates[:, 1:2] * paired[:, 1]
        )
        combined = jnp.where(live_b[:, None], combined, 0.0).astype(jnp.bfloat16)
        return combined.reshape(req_count, seq_len, col_width)

    return jax.vmap(back)(summed, target, chosen, residual, gate_pair, live_rows)


def solution(mesh):
    in_specs = (
        P(None, "dp", None, "expert"),
        P(),
        P(),
        P(None, "dp", None, None),
        P(None, "dp", None, None),
        P(None, "dp", None, None),
        P(),
        P(),
        P(),
        P(),
        P(),
        P(None, None, "expert", None),
        P(None, None, "expert", None),
        P(None, "expert", None, None),
        P(),
        P(None, "dp", None, "expert"),
    )
    out_specs = P(None, "dp", None, "expert")
    return jax.shard_map(
        per_device, mesh=mesh, in_specs=in_specs, out_specs=out_specs, check_vma=False
    )
```
